32 devices in a mesh: req: 8 (over z, x), kv: 4 (over y, core).
Axes of the slice: x: 2, y: 2, z: 4, core: 2. Of those that a mesh axis runs over, the one named last changes fastest.
Arguments:
- activations: bfloat16 [4992, 2048], P('req', 'kv'), may hold values from -6 to 6
- span_length: int32 [104], P('req'), may hold values from 1 to 48, as said below
- offsets: int32 [104], P('req'), may hold values from 64 to 8191
- decode_slot: int32 [104], P('req'), may hold values from 0 to 103, as said below
- attention_gain: float32 [2048], replicated, may hold values from 0.1 to 1.9
- query_weight: bfloat16 [2048, 2048], P(None, 'kv'), may hold values from -0.125 to 0.125
- key_projection_matrix: bfloat16 [2048, 1024], P(None, 'kv'), may hold values from -0.125 to 0.125
- value_projection_matrix: bfloat16 [2048, 1024], P(None, 'kv'), may hold values from -0.125 to 0.125
- output_weight: bfloat16 [2048, 2048], P('kv'), may hold values from -0.125 to 0.125
- feedforward_gain: float32 [2048], replicated, may hold values from 0.1 to 1.9
- gate_weight: bfloat16 [2048, 4096], P(None, 'kv'), may hold values from -0.125 to 0.125
- up_weight: bfloat16 [2048, 4096], P(None, 'kv'), may hold values from -0.125 to 0.125
- down_weight: bfloat16 [4096, 2048], P('kv'), may hold values from -0.09375 to 0.09375
- earlier_rotated_keys: bfloat16 [104, 64, 1024], P('req', 'kv'), may hold values from -300 to 300
- earlier_values: bfloat16 [104, 64, 1024], P('req', 'kv'), may hold values from -6 to 6
Outputs:
- layer_out: bfloat16 [4992, 2048], P('req', 'kv')
- decode_keys: bfloat16 [104, 64, 1024], P('req', None, 'kv')
- decode_values: bfloat16 [104, 64, 1024], P('req', None, 'kv')
The draws below stay inside these ranges and needn't reach their ends.
Inputs may be any that keep to these rules, and one draw needn't show every extreme that they name: `span_length`: on some prefill device every request fills all 48 positions. `decode_slot`: each slot appears once; decode device d owns slots d * 13 to (d + 1) * 13 - 1; at most 2 requests of one prefill device go to one decode device; every prefill device p sends exactly 2 requests to decode device p + 1 (counted round); the differences of decode device minus prefill device, modulo the number of devices of req, form the same multiset on every prefill device.
All inputs are finite; a program needn't handle non-finite values.
Results may differ from the reference program's by a relative error of at most 0.012.
Values may be sent and summed in bfloat16 or wider, within the bound.
No kernel may reach another device: no remote copies, remote signals or barrier semaphores. Data moves between devices by JAX's collectives and lax.ppermute only.
A program may use at most 128 MiB of HBM per device.

```python
import math
import jax
import jax.numpy as jnp
from jax import lax

MODEL_WIDTH = 2048
QUERY_HEADS = 8
KEY_VALUE_HEADS = 4
HEAD_WIDTH = 256
FF_WIN = 4096
REQ_DEV = 13
NEW_SPAN_LENGTH = 48
EARLIER_LENGTH = 64
REQUEST_COUNT = 104
ROWS = 4992
CAP = 2
N_REQ = 8


def draw_span_length(key, part):
    base_key = jax.random.fold_in(key, 3)
    first_key, second_key = jax.random.split(base_key, 2)
    lengths = jax.random.randint(first_key, (REQUEST_COUNT,), 1, NEW_SPAN_LENGTH + 1)
    device_pick = jax.random.randint(second_key, (), 0, N_REQ)
    full_device = jnp.arange(REQUEST_COUNT, dtype=jnp.int32) // REQ_DEV == device_pick
    return jnp.where(full_device, NEW_SPAN_LENGTH, lengths).astype(jnp.int32)


def draw_decode_slot(key, part):
    base_key = jax.random.fold_in(key, 7)
    first_key, second_key, third_key = jax.random.split(base_key, 3)
    pool_size = N_REQ * CAP
    forced_value = 1 % N_REQ
    far_value = N_REQ // 2
    pool_ids = jnp.arange(pool_size, dtype=jnp.int32)
    order_score = jax.random.permutation(second_key, pool_size).astype(jnp.int32)
    order_score = order_score - jnp.where(pool_ids // CAP == forced_value, 2 * pool_size, 0)
    order_score = order_score - jnp.where(pool_ids == far_value * CAP + CAP - 1, pool_size, 0)
    chosen = jnp.argsort(order_score, stable=True)[:REQ_DEV].astype(jnp.int32)
    shift_values = chosen // CAP
    source_keys = jax.random.split(third_key, N_REQ)
    source_perms = jax.vmap(lambda one_key: jax.random.permutation(one_key, REQ_DEV))(source_keys).astype(jnp.int32)
    shifts = shift_values[source_perms]
    source_ids = jnp.arange(N_REQ, dtype=jnp.int32)
    destination = (source_ids[:, None] + shifts) % N_REQ
    value_counts = jnp.sum((shift_values[None, :] == source_ids[:, None]).astype(jnp.int32), axis=1)
    pair_counts = value_counts[(source_ids[None, :] - source_ids[:, None]) % N_REQ]
    before_counts = jnp.cumsum(pair_counts, axis=0) - pair_counts
    request_ids = jnp.arange(REQ_DEV, dtype=jnp.int32)
    same_shift = shifts[:, :, None] == shifts[:, None, :]
    earlier = request_ids[None, :] < request_ids[:, None]
    ranks = jnp.sum((same_shift & earlier[None, :, :]).astype(jnp.int32), axis=2)
    starts = jnp.take_along_axis(before_counts, destination, axis=1)
    rotation = jax.random.randint(first_key, (N_REQ,), 0, REQ_DEV).astype(jnp.int32)
    slots = destination * REQ_DEV + (starts + ranks + rotation[destination]) % REQ_DEV
    return slots.reshape(REQUEST_COUNT).astype(jnp.int32)


def draw_earlier_rotated_keys(key, part):
    base_key = jax.random.fold_in(key, 11)
    first_key = jax.random.fold_in(base_key, 0)
    complete_shape = (REQUEST_COUNT, EARLIER_LENGTH, KEY_VALUE_HEADS * HEAD_WIDTH)
    base_values = jnp.clip(jax.random.normal(first_key, complete_shape, jnp.float32), -6.0, 6.0)
    return base_values.astype(jnp.bfloat16)


def set_ends(drawn, own_key, smallest, high):
    spot = [jax.random.randint(jax.random.fold_in(own_key, axis), (), 0, length) for axis, length in enumerate(drawn.shape)]
    main_axis = drawn.shape.index(max(drawn.shape))
    next_to = spot[:main_axis] + [(spot[main_axis] + 1) % drawn.shape[main_axis]] + spot[main_axis + 1:]
    return drawn.at[tuple(spot)].set(smallest).at[tuple(next_to)].set(high)


def level_of(key, extent, pieces, smallest, top_value):
    factor_of, own = 1.0, jax.random.fold_in(key, 6)
    for dim, parts in pieces:
        heights = jnp.exp(jax.random.uniform(jax.random.fold_in(own, dim), (parts,), jnp.float32, smallest / len(pieces), top_value / len(pieces)))
        factor_of = factor_of * jnp.repeat(heights, extent[dim] // parts).reshape([-1 if axis == dim else 1 for axis in range(len(extent))])
    return factor_of


def bell_draw(key, dims, scale, reach, shards=(), held_as=jnp.bfloat16):
    result = jax.random.normal(key, dims, jnp.float32) * scale
    if len(shards) > 0:
        result = level_of(key, dims, shards, -0.22, 0.18) * result
    return jnp.clip(result, min=-reach, max=reach).astype(held_as)


def setup_inputs(seed: int = 0) -> dict:
    key_of = jax.random.split(jax.random.key(seed), 16)
    activations = bell_draw(key_of[0], (ROWS, MODEL_WIDTH), 1.0, 6.0, ((0, 8), (1, 4)))
    span_length = draw_span_length(jax.random.fold_in(key_of[15], 71), 0)
    offsets = set_ends(jax.random.randint(key_of[2], (REQUEST_COUNT,), EARLIER_LENGTH, 8192), jax.random.fold_in(key_of[2], 1), EARLIER_LENGTH, 8191).astype(jnp.int32)
    decode_slot = draw_decode_slot(jax.random.fold_in(key_of[15], 71), 0)
    attention_gain = jnp.clip(1.0 + 0.18 * jax.random.normal(key_of[4], (MODEL_WIDTH,), jnp.float32), 0.1, 1.9)
    query_weight = bell_draw(key_of[5], (MODEL_WIDTH, QUERY_HEADS * HEAD_WIDTH), MODEL_WIDTH ** -0.5, 0.125, ((1, 4),))
    key_projection_matrix = bell_draw(key_of[6], (MODEL_WIDTH, KEY_VALUE_HEADS * HEAD_WIDTH), MODEL_WIDTH ** -0.5, 0.125, ((1, 4),))
    value_projection_matrix = bell_draw(key_of[7], (MODEL_WIDTH, KEY_VALUE_HEADS * HEAD_WIDTH), MODEL_WIDTH ** -0.5, 0.125, ((1, 4),))
    output_weight = bell_draw(key_of[8], (QUERY_HEADS * HEAD_WIDTH, MODEL_WIDTH), (QUERY_HEADS * HEAD_WIDTH) ** -0.5, 0.125, ((0, 4),))
    feedforward_gain = jnp.clip(1.0 + 0.18 * jax.random.normal(key_of[9], (MODEL_WIDTH,), jnp.float32), 0.1, 1.9)
    gate_weight = bell_draw(key_of[10], (MODEL_WIDTH, FF_WIN), MODEL_WIDTH ** -0.5, 0.125, ((1, 4),))
    up_weight = bell_draw(key_of[11], (MODEL_WIDTH, FF_WIN), MODEL_WIDTH ** -0.5, 0.125, ((1, 4),))
    down_weight = bell_draw(key_of[12], (FF_WIN, MODEL_WIDTH), FF_WIN ** -0.5, 0.09375, ((0, 4),))
    earlier_rotated_keys = draw_earlier_rotated_keys(jax.random.fold_in(key_of[15], 71), 0)
    earlier_values = bell_draw(key_of[14], (REQUEST_COUNT, EARLIER_LENGTH, KEY_VALUE_HEADS * HEAD_WIDTH), 1.0, 6.0, ((0, 8), (1, 4)))
    return dict(activations=activations, span_length=span_length, offsets=offsets, decode_slot=decode_slot, attention_gain=attention_gain, query_weight=query_weight, key_projection_matrix=key_projection_matrix, value_projection_matrix=value_projection_matrix, output_weight=output_weight, feedforward_gain=feedforward_gain, gate_weight=gate_weight, up_weight=up_weight, down_weight=down_weight, earlier_rotated_keys=earlier_rotated_keys, earlier_values=earlier_values)


rope_base = 1000042.0
epsilon = 1e-05

def rms_scale(values, gain_row):
    square_sum = lax.optimization_barrier(jnp.sum(values * values, axis=-1, keepdims=True))
    return values * lax.rsqrt(square_sum / values.shape[-1] + epsilon) * gain_row

def rotate_pairs(tensor, position):
    half_size = tensor.shape[-1] // 2
    steps_float = jnp.arange(half_size, dtype=jnp.float32)
    inverse = jnp.exp(steps_float * (-2.0 * math.log(rope_base) / tensor.shape[-1]))
    angles = position[:, :, None] * inverse[None, None, :]
    cosine = jnp.cos(angles)[:, :, None, :]
    sine_part = jnp.sin(angles)[:, :, None, :]
    first_half = tensor[..., :half_size]
    second = tensor[..., half_size:]
    return jnp.concatenate([first_half * cosine - second * sine_part, second * cosine + first_half * sine_part], axis=-1)

def allowed_keys(span_length, span_size, past_size):
    key_pos = jnp.arange(past_size + span_size, dtype=jnp.int32) - past_size
    query_pos = jnp.arange(span_size, dtype=jnp.int32)
    causal = key_pos[None, :] <= query_pos[:, None]
    live_keys = key_pos[None, None, :] < span_length[:, None, None]
    return (key_pos[None, None, :] < 0) | causal[None, :, :] & live_keys

def reference(activations, span_length, offsets, decode_slot, attention_gain, query_weight, key_projection_matrix, value_projection_matrix, output_weight, feedforward_gain, gate_weight, up_weight, down_weight, earlier_rotated_keys, earlier_values):
    request_list = REQ_DEV * N_REQ
    total_rows = request_list * NEW_SPAN_LENGTH
    query_groups = QUERY_HEADS // KEY_VALUE_HEADS
    x_float = activations.astype(jnp.float32)
    normalized_input = rms_scale(x_float, attention_gain).astype(jnp.bfloat16)
    position = offsets[:, None].astype(jnp.float32) + jnp.arange(NEW_SPAN_LENGTH, dtype=jnp.float32)[None, :]
    query_rows = jnp.dot(normalized_input, query_weight, preferred_element_type=jnp.float32).reshape(request_list, NEW_SPAN_LENGTH, QUERY_HEADS, HEAD_WIDTH)
    query_rows = rotate_pairs(query_rows, position).astype(jnp.bfloat16)
    fresh_keys = jnp.dot(normalized_input, key_projection_matrix, preferred_element_type=jnp.float32).reshape(request_list, NEW_SPAN_LENGTH, KEY_VALUE_HEADS, HEAD_WIDTH)
    fresh_keys = rotate_pairs(fresh_keys, position).astype(jnp.bfloat16)
    fresh_values = jnp.dot(normalized_input, value_projection_matrix, preferred_element_type=jnp.float32).astype(jnp.bfloat16).reshape(request_list, NEW_SPAN_LENGTH, KEY_VALUE_HEADS, HEAD_WIDTH)
    combined_keys = jnp.concatenate([earlier_rotated_keys.reshape(request_list, EARLIER_LENGTH, KEY_VALUE_HEADS, HEAD_WIDTH), fresh_keys], axis=1)
    combined_values = jnp.concatenate([earlier_values.reshape(request_list, EARLIER_LENGTH, KEY_VALUE_HEADS, HEAD_WIDTH), fresh_values], axis=1)
    grouped_queries = query_rows.reshape(request_list, NEW_SPAN_LENGTH, KEY_VALUE_HEADS, query_groups, HEAD_WIDTH).astype(jnp.float32)
    scores = jnp.einsum('rckgd,rskd->rkgcs', grouped_queries, combined_keys.astype(jnp.float32)) / math.sqrt(HEAD_WIDTH)
    allowed = allowed_keys(span_length, NEW_SPAN_LENGTH, EARLIER_LENGTH)[:, None, None, :, :]
    scores = jnp.where(allowed, scores, -jnp.inf)
    weights = jax.nn.softmax(scores, axis=-1).astype(jnp.bfloat16)
    mixed_heads = jnp.einsum('rkgcs,rskd->rckgd', weights.astype(jnp.float32), combined_values.astype(jnp.float32))
    mixed_heads = mixed_heads.astype(jnp.bfloat16).reshape(total_rows, QUERY_HEADS * HEAD_WIDTH)
    residual = x_float + jnp.dot(mixed_heads, output_weight, preferred_element_type=jnp.float32)
    normed_two = rms_scale(residual, feedforward_gain).astype(jnp.bfloat16)
    gate_proj = jnp.dot(normed_two, gate_weight, preferred_element_type=jnp.float32)
    upward = jnp.dot(normed_two, up_weight, preferred_element_type=jnp.float32)
    hidden = (jax.nn.silu(gate_proj) * upward).astype(jnp.bfloat16)
    output_rows = residual + jnp.dot(hidden, down_weight, preferred_element_type=jnp.float32)
    live_rows = (jnp.arange(NEW_SPAN_LENGTH, dtype=jnp.int32)[None, :] < span_length[:, None]).reshape(total_rows)
    layer_out = jnp.where(live_rows[:, None], output_rows, 0.0).astype(jnp.bfloat16)
    decode_keys = jnp.zeros_like(earlier_rotated_keys).at[decode_slot].set(earlier_rotated_keys)
    decode_values = jnp.zeros_like(earlier_values).at[decode_slot].set(earlier_values)
    return (layer_out, decode_keys, decode_values)
```

```python
import math

import jax
import jax.numpy as jnp
from jax import lax
from jax.sharding import Mesh
from jax.sharding import PartitionSpec as P

HEAD_WIDTH = 256
CORES = 2


rope_base = 1000042.0
epsilon = 1e-05


def rotate_pairs(tensor, position):
    half_size = tensor.shape[-1] // 2
    steps_float = jnp.arange(half_size, dtype=jnp.float32)
    inverse = jnp.exp(steps_float * (-2.0 * math.log(rope_base) / tensor.shape[-1]))
    angles = position[:, :, None] * inverse[None, None, :]
    cosine = jnp.cos(angles)[:, :, None, :]
    sine_part = jnp.sin(angles)[:, :, None, :]
    first_half = tensor[..., :half_size]
    second = tensor[..., half_size:]
    return jnp.concatenate(
        [first_half * cosine - second * sine_part, second * cosine + first_half * sine_part],
        axis=-1,
    )


def allowed_keys(span_length, span_size, past_size):
    key_pos = jnp.arange(past_size + span_size, dtype=jnp.int32) - past_size
    query_pos = jnp.arange(span_size, dtype=jnp.int32)
    causal = key_pos[None, :] <= query_pos[:, None]
    live_keys = key_pos[None, None, :] < span_length[:, None, None]
    return (key_pos[None, None, :] < 0) | causal[None, :, :] & live_keys


def gather_features(share):
    chips = lax.axis_size("kvy")
    rows, width = share.shape
    pair = lax.all_gather(share, "kvy", axis=1, tiled=True)
    whole = lax.all_gather(pair, "core", axis=1, tiled=True)
    whole = whole.reshape(rows, CORES, chips, width).transpose(0, 2, 1, 3)
    return whole.reshape(rows, CORES * chips * width)


def swap_blocks(matrix):
    chips = lax.axis_size("kvy")
    rows, cols = matrix.shape
    width = cols // (CORES * chips)
    return matrix.reshape(rows, chips, CORES, width).transpose(0, 2, 1, 3).reshape(rows, cols)


def scatter_features(partial):
    on_chip = lax.psum_scatter(partial, "core", scatter_dimension=1, tiled=True)
    return lax.psum_scatter(on_chip, "kvy", scatter_dimension=1, tiled=True)


def row_scale(values, gain_share):
    square_sum = lax.psum(jnp.sum(values * values, axis=-1, keepdims=True), ("kvy", "core"))
    width = values.shape[-1] * lax.axis_size("kvy") * CORES
    return values * lax.rsqrt(square_sum / width + epsilon) * gain_share


def local(
    activations,
    span_length,
    offsets,
    decode_slot,
    attention_gain,
    query_weight,
    key_projection_matrix,
    value_projection_matrix,
    output_weight,
    feedforward_gain,
    gate_weight,
    up_weight,
    down_weight,
    earlier_rotated_keys,
    earlier_values,
):
    req_count = lax.axis_size("req")
    chips = lax.axis_size("kvy")
    kv_count = chips * CORES
    kv_index = lax.axis_index("kvy") * CORES + lax.axis_index("core")
    req_index = lax.axis_index("req")
    request_list = span_length.shape[0]
    total_rows, width_share = activations.shape
    span_size = total_rows // request_list
    local_kv = key_projection_matrix.shape[1] // HEAD_WIDTH
    local_q = query_weight.shape[1] // HEAD_WIDTH
    query_groups = local_q // local_kv

    past_share = earlier_rotated_keys.shape[1]
    stacked = jnp.stack([earlier_rotated_keys, earlier_values])
    stacked = stacked.reshape(2, request_list, past_share, kv_count, local_kv * HEAD_WIDTH)
    stacked = stacked.transpose(0, 3, 1, 2, 4)
    arrived = lax.all_to_all(stacked, ("kvy", "core"), split_axis=1, concat_axis=1, tiled=True)
    head_kv = arrived.transpose(0, 2, 1, 3, 4).reshape(
        2, request_list, kv_count * past_share, local_kv * HEAD_WIDTH
    )
    past_size = head_kv.shape[2]

    capacity = max(2, (request_list + req_count - 1) // req_count)
    order_ids = jnp.arange(request_list, dtype=jnp.int32)
    earlier = order_ids[None, :] < order_ids[:, None]
    own_dest = decode_slot // request_list
    same_dest = own_dest[:, None] == own_dest[None, :]
    own_rank = jnp.sum((same_dest & earlier).astype(jnp.int32), axis=1)
    buffer_place = own_dest * capacity + own_rank
    buffer_ids = jnp.arange(req_count * capacity, dtype=jnp.int32)
    matches = buffer_place[None, :] == buffer_ids[:, None]
    picked = jnp.sum(jnp.where(matches, order_ids[None, :], 0), axis=1)
    filled = jnp.any(matches, axis=1)
    packed = jnp.take(head_kv, picked, axis=1)
    packed = jnp.where(filled[None, :, None, None], packed, jnp.zeros((), packed.dtype))
    packed = packed.reshape((2, req_count, capacity) + packed.shape[2:])
    packed_slots = jnp.where(filled, jnp.take(decode_slot, picked), -1).reshape(req_count, capacity)
    landed = lax.all_to_all(packed, "req", split_axis=1, concat_axis=1, tiled=True)
    landed_slots = lax.all_to_all(packed_slots, "req", split_axis=0, concat_axis=0, tiled=True)
    wanted = req_index * request_list + order_ids
    slot_hits = landed_slots.reshape(1, -1) == wanted[:, None]
    entry_ids = jnp.arange(req_count * capacity, dtype=jnp.int32)
    slot_position = jnp.sum(jnp.where(slot_hits, entry_ids[None, :], 0), axis=1)
    landed = landed.reshape((2, req_count * capacity) + landed.shape[3:])
    decode_kv = jnp.take(landed, slot_position, axis=1)

    x_whole = gather_features(activations)
    x_float = x_whole.astype(jnp.float32)
    square_sum = jnp.sum(x_float * x_float, axis=-1, keepdims=True)
    normalized_input = (
        x_float * lax.rsqrt(square_sum / x_float.shape[-1] + epsilon) * attention_gain
    ).astype(jnp.bfloat16)
    position = (
        offsets[:, None].astype(jnp.float32) + jnp.arange(span_size, dtype=jnp.float32)[None, :]
    )
    query_rows = jnp.dot(
        normalized_input, query_weight, preferred_element_type=jnp.float32
    ).reshape(request_list, span_size, local_q, HEAD_WIDTH)
    query_rows = rotate_pairs(query_rows, position).astype(jnp.bfloat16)
    fresh_keys = jnp.dot(
        normalized_input, key_projection_matrix, preferred_element_type=jnp.float32
    ).reshape(request_list, span_size, local_kv, HEAD_WIDTH)
    fresh_keys = rotate_pairs(fresh_keys, position).astype(jnp.bfloat16)
    fresh_values = (
        jnp.dot(normalized_input, value_projection_matrix, preferred_element_type=jnp.float32)
        .astype(jnp.bfloat16)
        .reshape(request_list, span_size, local_kv, HEAD_WIDTH)
    )
    combined_keys = jnp.concatenate(
        [head_kv[0].reshape(request_list, past_size, local_kv, HEAD_WIDTH), fresh_keys], axis=1
    )
    combined_values = jnp.concatenate(
        [head_kv[1].reshape(request_list, past_size, local_kv, HEAD_WIDTH), fresh_values], axis=1
    )
    grouped_queries = query_rows.reshape(
        request_list, span_size, local_kv, query_groups, HEAD_WIDTH
    )
    scores = jnp.einsum(
        "rckgd,rskd->rkgcs", grouped_queries, combined_keys, preferred_element_type=jnp.float32
    ) / math.sqrt(HEAD_WIDTH)
    allowed = allowed_keys(span_length, span_size, past_size)[:, None, None, :, :]
    scores = jnp.where(allowed, scores, -jnp.inf)
    weights = jax.nn.softmax(scores, axis=-1).astype(jnp.bfloat16)
    mixed_heads = jnp.einsum(
        "rkgcs,rskd->rckgd", weights, combined_values, preferred_element_type=jnp.float32
    )
    mixed_heads = mixed_heads.astype(jnp.bfloat16).reshape(total_rows, local_q * HEAD_WIDTH)
    head_part = jnp.dot(mixed_heads, swap_blocks(output_weight), preferred_element_type=jnp.float32)
    head_share = scatter_features(head_part)
    residual_share = activations.astype(jnp.float32) + head_share

    gain_share = lax.dynamic_slice_in_dim(feedforward_gain, kv_index * width_share, width_share)
    normed_share = row_scale(residual_share, gain_share).astype(jnp.bfloat16)
    normed_two = gather_features(normed_share)
    gate_proj = jnp.dot(normed_two, gate_weight, preferred_element_type=jnp.float32)
    upward = jnp.dot(normed_two, up_weight, preferred_element_type=jnp.float32)
    hidden = (jax.nn.silu(gate_proj) * upward).astype(jnp.bfloat16)
    mlp_share = scatter_features(
        jnp.dot(hidden, swap_blocks(down_weight), preferred_element_type=jnp.float32)
    )
    live_rows = (jnp.arange(span_size, dtype=jnp.int32)[None, :] < span_length[:, None]).reshape(
        total_rows
    )
    layer_out = jnp.where(live_rows[:, None], residual_share + mlp_share, 0.0).astype(jnp.bfloat16)
    return (layer_out, decode_kv[0], decode_kv[1])


def solution(mesh):
    req_size, kv_size = mesh.devices.shape
    split_mesh = Mesh(
        mesh.devices.reshape(req_size, kv_size // CORES, CORES), ("req", "kvy", "core")
    )
    kv = ("kvy", "core")
    return jax.shard_map(
        local,
        mesh=split_mesh,
        in_specs=(
            P("req", kv),
            P("req"),
            P("req"),
            P("req"),
            P(),
            P(None, kv),
            P(None, kv),
            P(None, kv),
            P(kv, None),
            P(),
            P(None, kv),
            P(None, kv),
            P(kv, None),
            P("req", kv, None),
            P("req", kv, None),
        ),
        out_specs=(P("req", kv), P("req", None, kv), P("req", None, kv)),
        check_vma=False,
    )
```

```python
import math

import jax
import jax.numpy as jnp
from jax import lax
from jax.sharding import Mesh
from jax.sharding import PartitionSpec as P

HEAD_WIDTH = 256
CORES = 2


rope_base = 1000042.0
epsilon = 1e-05


def rotate_pairs(tensor, position):
    half_size = tensor.shape[-1] // 2
    steps_float = jnp.arange(half_size, dtype=jnp.float32)
    inverse = jnp.exp(steps_float * (-2.0 * math.log(rope_base) / tensor.shape[-1]))
    angles = position[:, :, None] * inverse[None, None, :]
    cosine = jnp.cos(angles)[:, :, None, :]
    sine_part = jnp.sin(angles)[:, :, None, :]
    first_half = tensor[..., :half_size]
    second = tensor[..., half_size:]
    return jnp.concatenate(
        [first_half * cosine - second * sine_part, second * cosine + first_half * sine_part],
        axis=-1,
    )


def allowed_keys(span_length, span_size, past_size):
    key_pos = jnp.arange(past_size + span_size, dtype=jnp.int32) - past_size
    query_pos = jnp.arange(span_size, dtype=jnp.int32)
    causal = key_pos[None, :] <= query_pos[:, None]
    live_keys = key_pos[None, None, :] < span_length[:, None, None]
    return (key_pos[None, None, :] < 0) | causal[None, :, :] & live_keys


def swap(values, axis_name):
    return lax.ppermute(values, axis_name, [(0, 1), (1, 0)])


def gather_features(share):
    chip = lax.axis_index("kvy")
    core = lax.axis_index("core")
    partner = swap(share, "kvy")
    pair = jnp.where(chip == 0, jnp.stack([share, partner]), jnp.stack([partner, share]))
    other = swap(pair, "core")
    blocks = []
    for chip_block in range(2):
        for core_block in range(2):
            blocks.append(jnp.where(core == core_block, pair[chip_block], other[chip_block]))
    return jnp.concatenate(blocks, axis=1)


def scatter_features(matrix_in, weight):
    chip = lax.axis_index("kvy")
    core = lax.axis_index("core")
    rows, cols = weight.shape
    width = cols // (2 * CORES)
    blocks = jnp.einsum(
        "rd,dkcf->ckrf",
        matrix_in,
        weight.reshape(rows, 2, CORES, width),
        preferred_element_type=jnp.float32,
    )
    keep = jnp.where(core == 0, blocks[0], blocks[1])
    give = jnp.where(core == 0, blocks[1], blocks[0])
    chip_sum = keep + swap(give, "core")
    mine = jnp.where(chip == 0, chip_sum[0], chip_sum[1])
    theirs = jnp.where(chip == 0, chip_sum[1], chip_sum[0])
    return mine + swap(theirs, "kvy")


def row_scale(values, gain_share):
    square_sum = jnp.sum(values * values, axis=-1, keepdims=True)
    square_sum = square_sum + swap(square_sum, "core")
    square_sum = square_sum + swap(square_sum, "kvy")
    width = values.shape[-1] * 2 * CORES
    return values * lax.rsqrt(square_sum / width + epsilon) * gain_share


def local(
    activations,
    span_length,
    offsets,
    decode_slot,
    attention_gain,
    query_weight,
    key_projection_matrix,
    value_projection_matrix,
    output_weight,
    feedforward_gain,
    gate_weight,
    up_weight,
    down_weight,
    earlier_rotated_keys,
    earlier_values,
):
    req_count = lax.axis_size("req")
    chips = lax.axis_size("kvy")
    kv_count = chips * CORES
    kv_index = lax.axis_index("kvy") * CORES + lax.axis_index("core")
    req_index = lax.axis_index("req")
    request_list = span_length.shape[0]
    total_rows, width_share = activations.shape
    span_size = total_rows // request_list
    local_kv = key_projection_matrix.shape[1] // HEAD_WIDTH
    local_q = query_weight.shape[1] // HEAD_WIDTH
    query_groups = local_q // local_kv

    past_share = earlier_rotated_keys.shape[1]
    stacked = jnp.stack([earlier_rotated_keys, earlier_values])
    stacked = stacked.reshape(2, request_list, past_share, kv_count, local_kv * HEAD_WIDTH)
    stacked = stacked.transpose(0, 3, 1, 2, 4)
    arrived = lax.all_to_all(stacked, ("kvy", "core"), split_axis=1, concat_axis=1, tiled=True)
    head_kv = arrived.transpose(0, 2, 1, 3, 4).reshape(
        2, request_list, kv_count * past_share, local_kv * HEAD_WIDTH
    )
    past_size = head_kv.shape[2]

    capacity = max(2, (request_list + req_count - 1) // req_count)
    order_ids = jnp.arange(request_list, dtype=jnp.int32)
    earlier = order_ids[None, :] < order_ids[:, None]
    own_dest = decode_slot // request_list
    same_dest = own_dest[:, None] == own_dest[None, :]
    own_rank = jnp.sum((same_dest & earlier).astype(jnp.int32), axis=1)
    buffer_place = own_dest * capacity + own_rank
    buffer_ids = jnp.arange(req_count * capacity, dtype=jnp.int32)
    matches = buffer_place[None, :] == buffer_ids[:, None]
    picked = jnp.sum(jnp.where(matches, order_ids[None, :], 0), axis=1)
    filled = jnp.any(matches, axis=1)
    packed = jnp.take(head_kv, picked, axis=1)
    packed = jnp.where(filled[None, :, None, None], packed, jnp.zeros((), packed.dtype))
    packed = packed.reshape((2, req_count, capacity) + packed.shape[2:])
    packed_slots = jnp.where(filled, jnp.take(decode_slot, picked), -1).reshape(req_count, capacity)
    landed = lax.all_to_all(packed, "req", split_axis=1, concat_axis=1, tiled=True)
    landed_slots = lax.all_to_all(packed_slots, "req", split_axis=0, concat_axis=0, tiled=True)
    wanted = req_index * request_list + order_ids
    slot_hits = landed_slots.reshape(1, -1) == wanted[:, None]
    entry_ids = jnp.arange(req_count * capacity, dtype=jnp.int32)
    slot_position = jnp.sum(jnp.where(slot_hits, entry_ids[None, :], 0), axis=1)
    landed = landed.reshape((2, req_count * capacity) + landed.shape[3:])
    decode_kv = jnp.take(landed, slot_position, axis=1)

    x_whole = gather_features(activations)
    x_float = x_whole.astype(jnp.float32)
    square_sum = jnp.sum(x_float * x_float, axis=-1, keepdims=True)
    normalized_input = (
        x_float * lax.rsqrt(square_sum / x_float.shape[-1] + epsilon) * attention_gain
    ).astype(jnp.bfloat16)
    position = (
        offsets[:, None].astype(jnp.float32) + jnp.arange(span_size, dtype=jnp.float32)[None, :]
    )
    query_rows = jnp.dot(
        normalized_input, query_weight, preferred_element_type=jnp.float32
    ).reshape(request_list, span_size, local_q, HEAD_WIDTH)
    query_rows = rotate_pairs(query_rows, position).astype(jnp.bfloat16)
    fresh_keys = jnp.dot(
        normalized_input, key_projection_matrix, preferred_element_type=jnp.float32
    ).reshape(request_list, span_size, local_kv, HEAD_WIDTH)
    fresh_keys = rotate_pairs(fresh_keys, position).astype(jnp.bfloat16)
    fresh_values = (
        jnp.dot(normalized_input, value_projection_matrix, preferred_element_type=jnp.float32)
        .astype(jnp.bfloat16)
        .reshape(request_list, span_size, local_kv, HEAD_WIDTH)
    )
    combined_keys = jnp.concatenate(
        [head_kv[0].reshape(request_list, past_size, local_kv, HEAD_WIDTH), fresh_keys], axis=1
    )
    combined_values = jnp.concatenate(
        [head_kv[1].reshape(request_list, past_size, local_kv, HEAD_WIDTH), fresh_values], axis=1
    )
    grouped_queries = query_rows.reshape(
        request_list, span_size, local_kv, query_groups, HEAD_WIDTH
    )
    scores = jnp.einsum(
        "rckgd,rskd->rkgcs", grouped_queries, combined_keys, preferred_element_type=jnp.float32
    ) / math.sqrt(HEAD_WIDTH)
    allowed = allowed_keys(span_length, span_size, past_size)[:, None, None, :, :]
    scores = jnp.where(allowed, scores, -jnp.inf)
    weights = jax.nn.softmax(scores, axis=-1).astype(jnp.bfloat16)
    mixed_heads = jnp.einsum(
        "rkgcs,rskd->rckgd", weights, combined_values, preferred_element_type=jnp.float32
    )
    mixed_heads = mixed_heads.astype(jnp.bfloat16).reshape(total_rows, local_q * HEAD_WIDTH)
    head_share = scatter_features(mixed_heads, output_weight)
    residual_share = activations.astype(jnp.float32) + head_share

    gain_share = lax.dynamic_slice_in_dim(feedforward_gain, kv_index * width_share, width_share)
    normed_share = row_scale(residual_share, gain_share).astype(jnp.bfloat16)
    normed_two = gather_features(normed_share)
    gate_proj = jnp.dot(normed_two, gate_weight, preferred_element_type=jnp.float32)
    upward = jnp.dot(normed_two, up_weight, preferred_element_type=jnp.float32)
    hidden = (jax.nn.silu(gate_proj) * upward).astype(jnp.bfloat16)
    mlp_share = scatter_features(hidden, down_weight)
    live_rows = (jnp.arange(span_size, dtype=jnp.int32)[None, :] < span_length[:, None]).reshape(
        total_rows
    )
    layer_out = jnp.where(live_rows[:, None], residual_share + mlp_share, 0.0).astype(jnp.bfloat16)
    return (layer_out, decode_kv[0], decode_kv[1])


def solution(mesh):
    req_size, kv_size = mesh.devices.shape
    split_mesh = Mesh(
        mesh.devices.reshape(req_size, kv_size // CORES, CORES), ("req", "kvy", "core")
    )
    kv = ("kvy", "core")
    return jax.shard_map(
        local,
        mesh=split_mesh,
        in_specs=(
            P("req", kv),
            P("req"),
            P("req"),
            P("req"),
            P(),
            P(None, kv),
            P(None, kv),
            P(None, kv),
            P(kv, None),
            P(),
            P(None, kv),
            P(None, kv),
            P(kv, None),
            P("req", kv, None),
            P("req", kv, None),
        ),
        out_specs=(P("req", kv), P("req", None, kv), P("req", None, kv)),
        check_vma=False,
    )
```

```python
import math

import jax
import jax.numpy as jnp
from jax import lax
from jax.sharding import Mesh
from jax.sharding import PartitionSpec as P

HEAD_WIDTH = 256
CORES = 2


rope_base = 1000042.0
epsilon = 1e-05


def rotate_pairs(tensor, position):
    half_size = tensor.shape[-1] // 2
    steps_float = jnp.arange(half_size, dtype=jnp.float32)
    inverse = jnp.exp(steps_float * (-2.0 * math.log(rope_base) / tensor.shape[-1]))
    angles = position[:, :, None] * inverse[None, None, :]
    cosine = jnp.cos(angles)[:, :, None, :]
    sine_part = jnp.sin(angles)[:, :, None, :]
    first_half = tensor[..., :half_size]
    second = tensor[..., half_size:]
    return jnp.concatenate(
        [first_half * cosine - second * sine_part, second * cosine + first_half * sine_part],
        axis=-1,
    )


def allowed_keys(span_length, span_size, past_size):
    key_pos = jnp.arange(past_size + span_size, dtype=jnp.int32) - past_size
    query_pos = jnp.arange(span_size, dtype=jnp.int32)
    causal = key_pos[None, :] <= query_pos[:, None]
    live_keys = key_pos[None, None, :] < span_length[:, None, None]
    return (key_pos[None, None, :] < 0) | causal[None, :, :] & live_keys


def swap(values, axis_name):
    return lax.ppermute(values, axis_name, [(0, 1), (1, 0)])


def gather_features(share):
    chip = lax.axis_index("kvy")
    core = lax.axis_index("core")
    partner = swap(share, "kvy")
    pair = jnp.where(chip == 0, jnp.stack([share, partner]), jnp.stack([partner, share]))
    other = swap(pair, "core")
    blocks = []
    for chip_block in range(2):
        for core_block in range(2):
            blocks.append(jnp.where(core == core_block, pair[chip_block], other[chip_block]))
    return jnp.concatenate(blocks, axis=1)


def scatter_features(matrix_in, weight):
    chip = lax.axis_index("kvy")
    core = lax.axis_index("core")
    product = jnp.dot(matrix_in, weight, preferred_element_type=jnp.float32)
    width = product.shape[1] // (2 * CORES)

    def block(chip_block, core_block):
        start = (chip_block * CORES + core_block) * width
        return product[:, start:start + width]

    keep = jnp.stack([jnp.where(core == 0, block(k, 0), block(k, 1)) for k in range(2)])
    give = jnp.stack([jnp.where(core == 0, block(k, 1), block(k, 0)) for k in range(2)])
    chip_sum = keep + swap(give, "core")
    mine = jnp.where(chip == 0, chip_sum[0], chip_sum[1])
    theirs = jnp.where(chip == 0, chip_sum[1], chip_sum[0])
    return mine + swap(theirs, "kvy")


def row_scale(values, gain_share):
    square_sum = jnp.sum(values * values, axis=-1, keepdims=True)
    square_sum = square_sum + swap(square_sum, "core")
    square_sum = square_sum + swap(square_sum, "kvy")
    width = values.shape[-1] * 2 * CORES
    return values * lax.rsqrt(square_sum / width + epsilon) * gain_share


def local(
    activations,
    span_length,
    offsets,
    decode_slot,
    attention_gain,
    query_weight,
    key_projection_matrix,
    value_projection_matrix,
    output_weight,
    feedforward_gain,
    gate_weight,
    up_weight,
    down_weight,
    earlier_rotated_keys,
    earlier_values,
):
    req_count = lax.axis_size("req")
    chips = lax.axis_size("kvy")
    kv_count = chips * CORES
    kv_index = lax.axis_index("kvy") * CORES + lax.axis_index("core")
    req_index = lax.axis_index("req")
    request_list = span_length.shape[0]
    total_rows, width_share = activations.shape
    span_size = total_rows // request_list
    local_kv = key_projection_matrix.shape[1] // HEAD_WIDTH
    local_q = query_weight.shape[1] // HEAD_WIDTH
    query_groups = local_q // local_kv

    past_share = earlier_rotated_keys.shape[1]
    stacked = jnp.stack([earlier_rotated_keys, earlier_values])
    stacked = stacked.reshape(2, request_list, past_share, kv_count, local_kv * HEAD_WIDTH)
    stacked = stacked.transpose(0, 3, 1, 2, 4)
    arrived = lax.all_to_all(stacked, ("kvy", "core"), split_axis=1, concat_axis=1, tiled=True)
    head_kv = arrived.transpose(0, 2, 1, 3, 4).reshape(
        2, request_list, kv_count * past_share, local_kv * HEAD_WIDTH
    )
    past_size = head_kv.shape[2]

    capacity = max(2, (request_list + req_count - 1) // req_count)
    order_ids = jnp.arange(request_list, dtype=jnp.int32)
    earlier = order_ids[None, :] < order_ids[:, None]
    own_dest = decode_slot // request_list
    same_dest = own_dest[:, None] == own_dest[None, :]
    own_rank = jnp.sum((same_dest & earlier).astype(jnp.int32), axis=1)
    buffer_place = own_dest * capacity + own_rank
    buffer_ids = jnp.arange(req_count * capacity, dtype=jnp.int32)
    matches = buffer_place[None, :] == buffer_ids[:, None]
    picked = jnp.sum(jnp.where(matches, order_ids[None, :], 0), axis=1)
    filled = jnp.any(matches, axis=1)
    lanes = local_kv * HEAD_WIDTH
    rows_kv = jnp.moveaxis(head_kv, 0, 1).reshape(request_list, 2 * past_size * lanes)
    slot_code = jnp.stack([decode_slot // 16, decode_slot % 16], axis=1).astype(jnp.bfloat16)
    trailer = jnp.pad(slot_code, ((0, 0), (0, lanes - 2)))
    payload = jnp.concatenate([rows_kv, trailer], axis=1)
    packed = jnp.take(payload, picked, axis=0)
    packed = jnp.where(filled[:, None], packed, -jnp.ones((), packed.dtype))
    packed = packed.reshape(req_count, capacity, payload.shape[1])
    landed = lax.all_to_all(packed, "req", split_axis=0, concat_axis=0, tiled=True)
    landed = landed.reshape(req_count * capacity, payload.shape[1])
    code = landed[:, 2 * past_size * lanes:2 * past_size * lanes + 2].astype(jnp.int32)
    landed_slots = code[:, 0] * 16 + code[:, 1]
    wanted = req_index * request_list + order_ids
    slot_hits = landed_slots[None, :] == wanted[:, None]
    entry_ids = jnp.arange(req_count * capacity, dtype=jnp.int32)
    slot_position = jnp.sum(jnp.where(slot_hits, entry_ids[None, :], 0), axis=1)
    decode_rows = jnp.take(landed[:, :2 * past_size * lanes], slot_position, axis=0)
    decode_kv = jnp.moveaxis(decode_rows.reshape(request_list, 2, past_size, lanes), 1, 0)

    x_whole = gather_features(activations)
    x_float = x_whole.astype(jnp.float32)
    square_sum = jnp.sum(x_float * x_float, axis=-1, keepdims=True)
    normalized_input = (
        x_float * lax.rsqrt(square_sum / x_float.shape[-1] + epsilon) * attention_gain
    ).astype(jnp.bfloat16)
    position = (
        offsets[:, None].astype(jnp.float32) + jnp.arange(span_size, dtype=jnp.float32)[None, :]
    )
    query_rows = jnp.dot(
        normalized_input, query_weight, preferred_element_type=jnp.float32
    ).reshape(request_list, span_size, local_q, HEAD_WIDTH)
    query_rows = rotate_pairs(query_rows, position).astype(jnp.bfloat16)
    fresh_keys = jnp.dot(
        normalized_input, key_projection_matrix, preferred_element_type=jnp.float32
    ).reshape(request_list, span_size, local_kv, HEAD_WIDTH)
    fresh_keys = rotate_pairs(fresh_keys, position).astype(jnp.bfloat16)
    fresh_values = (
        jnp.dot(normalized_input, value_projection_matrix, preferred_element_type=jnp.float32)
        .astype(jnp.bfloat16)
        .reshape(request_list, span_size, local_kv, HEAD_WIDTH)
    )
    combined_keys = jnp.concatenate(
        [head_kv[0].reshape(request_list, past_size, local_kv, HEAD_WIDTH), fresh_keys], axis=1
    )
    combined_values = jnp.concatenate(
        [head_kv[1].reshape(request_list, past_size, local_kv, HEAD_WIDTH), fresh_values], axis=1
    )
    grouped_queries = query_rows.reshape(
        request_list, span_size, local_kv, query_groups, HEAD_WIDTH
    )
    scores = jnp.einsum(
        "rckgd,rskd->rkgcs", grouped_queries, combined_keys, preferred_element_type=jnp.float32
    ) / math.sqrt(HEAD_WIDTH)
    allowed = allowed_keys(span_length, span_size, past_size)[:, None, None, :, :]
    scores = jnp.where(allowed, scores, -jnp.inf)
    weights = jax.nn.softmax(scores, axis=-1).astype(jnp.bfloat16)
    mixed_heads = jnp.einsum(
        "rkgcs,rskd->rckgd", weights, combined_values, preferred_element_type=jnp.float32
    )
    mixed_heads = mixed_heads.astype(jnp.bfloat16).reshape(total_rows, local_q * HEAD_WIDTH)
    head_share = scatter_features(mixed_heads, output_weight)
    residual_share = activations.astype(jnp.float32) + head_share

    gain_share = lax.dynamic_slice_in_dim(feedforward_gain, kv_index * width_share, width_share)
    normed_share = row_scale(residual_share, gain_share).astype(jnp.bfloat16)
    normed_two = gather_features(normed_share)
    gate_proj = jnp.dot(normed_two, gate_weight, preferred_element_type=jnp.float32)
    upward = jnp.dot(normed_two, up_weight, preferred_element_type=jnp.float32)
    hidden = (jax.nn.silu(gate_proj) * upward).astype(jnp.bfloat16)
    mlp_share = scatter_features(hidden, down_weight)
    live_rows = (jnp.arange(span_size, dtype=jnp.int32)[None, :] < span_length[:, None]).reshape(
        total_rows
    )
    layer_out = jnp.where(live_rows[:, None], residual_share + mlp_share, 0.0).astype(jnp.bfloat16)
    return (layer_out, decode_kv[0], decode_kv[1])


def solution(mesh):
    req_size, kv_size = mesh.devices.shape
    split_mesh = Mesh(
        mesh.devices.reshape(req_size, kv_size // CORES, CORES), ("req", "kvy", "core")
    )
    kv = ("kvy", "core")
    return jax.shard_map(
        local,
        mesh=split_mesh,
        in_specs=(
            P("req", kv),
            P("req"),
            P("req"),
            P("req"),
            P(),
            P(None, kv),
            P(None, kv),
            P(None, kv),
            P(kv, None),
            P(),
            P(None, kv),
            P(None, kv),
            P(kv, None),
            P("req", kv, None),
            P("req", kv, None),
        ),
        out_specs=(P("req", kv), P("req", None, kv), P("req", None, kv)),
        check_vma=False,
    )
```

```python
import math

import jax
import jax.numpy as jnp
from jax import lax
from jax.sharding import Mesh
from jax.sharding import PartitionSpec as P

HEAD_WIDTH = 256
CORES = 2


rope_base = 1000042.0
epsilon = 1e-05


def rotate_pairs(tensor, position):
    half_size = tensor.shape[-1] // 2
    steps_float = jnp.arange(half_size, dtype=jnp.float32)
    inverse = jnp.exp(steps_float * (-2.0 * math.log(rope_base) / tensor.shape[-1]))
    angles = position[:, :, None] * inverse[None, None, :]
    cosine = jnp.cos(angles)[:, :, None, :]
    sine_part = jnp.sin(angles)[:, :, None, :]
    first_half = tensor[..., :half_size]
    second = tensor[..., half_size:]
    return jnp.concatenate(
        [first_half * cosine - second * sine_part, second * cosine + first_half * sine_part],
        axis=-1,
    )


def allowed_keys(span_length, span_size, past_size):
    key_pos = jnp.arange(past_size + span_size, dtype=jnp.int32) - past_size
    query_pos = jnp.arange(span_size, dtype=jnp.int32)
    causal = key_pos[None, :] <= query_pos[:, None]
    live_keys = key_pos[None, None, :] < span_length[:, None, None]
    return (key_pos[None, None, :] < 0) | causal[None, :, :] & live_keys


def swap(values, axis_name):
    return lax.ppermute(values, axis_name, [(0, 1), (1, 0)])


def gather_features(share):
    chip = lax.axis_index("kvy")
    core = lax.axis_index("core")
    partner = swap(share, "kvy")
    pair = jnp.where(chip == 0, jnp.stack([share, partner]), jnp.stack([partner, share]))
    other = swap(pair, "core")
    blocks = []
    for chip_block in range(2):
        for core_block in range(2):
            blocks.append(jnp.where(core == core_block, pair[chip_block], other[chip_block]))
    return jnp.concatenate(blocks, axis=1)


def scatter_features(matrix_in, weight):
    chip = lax.axis_index("kvy")
    core = lax.axis_index("core")
    product = jnp.dot(matrix_in, weight, preferred_element_type=jnp.float32)
    width = product.shape[1] // (2 * CORES)

    def block(chip_block, core_block):
        start = (chip_block * CORES + core_block) * width
        return product[:, start:start + width]

    keep = jnp.stack([jnp.where(core == 0, block(k, 0), block(k, 1)) for k in range(2)])
    give = jnp.stack([jnp.where(core == 0, block(k, 1), block(k, 0)) for k in range(2)])
    chip_sum = keep + swap(give, "core")
    mine = jnp.where(chip == 0, chip_sum[0], chip_sum[1])
    theirs = jnp.where(chip == 0, chip_sum[1], chip_sum[0])
    return mine + swap(theirs, "kvy")


def row_scale(values, gain_share):
    square_sum = jnp.sum(values * values, axis=-1, keepdims=True)
    square_sum = square_sum + swap(square_sum, "core")
    square_sum = square_sum + swap(square_sum, "kvy")
    width = values.shape[-1] * 2 * CORES
    return values * lax.rsqrt(square_sum / width + epsilon) * gain_share


def local(
    activations,
    span_length,
    offsets,
    decode_slot,
    attention_gain,
    query_weight,
    key_projection_matrix,
    value_projection_matrix,
    output_weight,
    feedforward_gain,
    gate_weight,
    up_weight,
    down_weight,
    earlier_rotated_keys,
    earlier_values,
):
    req_count = lax.axis_size("req")
    chips = lax.axis_size("kvy")
    kv_count = chips * CORES
    kv_index = lax.axis_index("kvy") * CORES + lax.axis_index("core")
    req_index = lax.axis_index("req")
    request_list = span_length.shape[0]
    total_rows, width_share = activations.shape
    span_size = total_rows // request_list
    local_kv = key_projection_matrix.shape[1] // HEAD_WIDTH
    local_q = query_weight.shape[1] // HEAD_WIDTH
    query_groups = local_q // local_kv

    past_share = earlier_rotated_keys.shape[1]
    stacked = jnp.stack([earlier_rotated_keys, earlier_values])
    stacked = stacked.reshape(2, request_list, past_share, kv_count, local_kv * HEAD_WIDTH)
    stacked = stacked.transpose(0, 3, 1, 2, 4)
    arrived = lax.all_to_all(stacked, ("kvy", "core"), split_axis=1, concat_axis=1, tiled=True)
    head_kv = arrived.transpose(0, 2, 1, 3, 4).reshape(
        2, request_list, kv_count * past_share, local_kv * HEAD_WIDTH
    )
    past_size = head_kv.shape[2]

    capacity = max(2, (request_list + req_count - 1) // req_count)
    order_ids = jnp.arange(request_list, dtype=jnp.int32)
    earlier = order_ids[None, :] < order_ids[:, None]
    own_dest = decode_slot // request_list
    same_dest = own_dest[:, None] == own_dest[None, :]
    own_rank = jnp.sum((same_dest & earlier).astype(jnp.int32), axis=1)
    buffer_place = own_dest * capacity + own_rank
    buffer_ids = jnp.arange(req_count * capacity, dtype=jnp.int32)
    matches = buffer_place[None, :] == buffer_ids[:, None]
    picked = jnp.sum(jnp.where(matches, order_ids[None, :], 0), axis=1)
    filled = jnp.any(matches, axis=1)
    lanes = local_kv * HEAD_WIDTH
    rows_kv = jnp.moveaxis(head_kv, 0, 1).reshape(request_list, 2 * past_size * lanes)
    slot_code = jnp.stack([decode_slot // 16, decode_slot % 16], axis=1).astype(jnp.bfloat16)
    trailer = jnp.pad(slot_code, ((0, 0), (0, lanes - 2)))
    payload = jnp.concatenate([rows_kv, trailer], axis=1)
    packed = jnp.take(payload, picked, axis=0)
    packed = jnp.where(filled[:, None], packed, -jnp.ones((), packed.dtype))
    packed = packed.reshape(req_count, capacity, payload.shape[1])
    pieces = [lax.dynamic_index_in_dim(packed, req_index, 0, keepdims=False)]
    for shift in range(1, req_count):
        outgoing = lax.dynamic_index_in_dim(packed, (req_index + shift) % req_count, 0, keepdims=False)
        pairs = [(source, (source + shift) % req_count) for source in range(req_count)]
        pieces.append(lax.ppermute(outgoing, "req", pairs))
    landed = jnp.stack(pieces).reshape(req_count * capacity, payload.shape[1])
    code = landed[:, 2 * past_size * lanes:2 * past_size * lanes + 2].astype(jnp.int32)
    landed_slots = code[:, 0] * 16 + code[:, 1]
    wanted = req_index * request_list + order_ids
    slot_hits = landed_slots[None, :] == wanted[:, None]
    entry_ids = jnp.arange(req_count * capacity, dtype=jnp.int32)
    slot_position = jnp.sum(jnp.where(slot_hits, entry_ids[None, :], 0), axis=1)
    decode_rows = jnp.take(landed[:, :2 * past_size * lanes], slot_position, axis=0)
    decode_kv = jnp.moveaxis(decode_rows.reshape(request_list, 2, past_size, lanes), 1, 0)

    x_whole = gather_features(activations)
    x_float = x_whole.astype(jnp.float32)
    square_sum = jnp.sum(x_float * x_float, axis=-1, keepdims=True)
    normalized_input = (
        x_float * lax.rsqrt(square_sum / x_float.shape[-1] + epsilon) * attention_gain
    ).astype(jnp.bfloat16)
    position = (
        offsets[:, None].astype(jnp.float32) + jnp.arange(span_size, dtype=jnp.float32)[None, :]
    )
    query_rows = jnp.dot(
        normalized_input, query_weight, preferred_element_type=jnp.float32
    ).reshape(request_list, span_size, local_q, HEAD_WIDTH)
    query_rows = rotate_pairs(query_rows, position).astype(jnp.bfloat16)
    fresh_keys = jnp.dot(
        normalized_input, key_projection_matrix, preferred_element_type=jnp.float32
    ).reshape(request_list, span_size, local_kv, HEAD_WIDTH)
    fresh_keys = rotate_pairs(fresh_keys, position).astype(jnp.bfloat16)
    fresh_values = (
        jnp.dot(normalized_input, value_projection_matrix, preferred_element_type=jnp.float32)
        .astype(jnp.bfloat16)
        .reshape(request_list, span_size, local_kv, HEAD_WIDTH)
    )
    combined_keys = jnp.concatenate(
        [head_kv[0].reshape(request_list, past_size, local_kv, HEAD_WIDTH), fresh_keys], axis=1
    )
    combined_values = jnp.concatenate(
        [head_kv[1].reshape(request_list, past_size, local_kv, HEAD_WIDTH), fresh_values], axis=1
    )
    grouped_queries = query_rows.reshape(
        request_list, span_size, local_kv, query_groups, HEAD_WIDTH
    )
    scores = jnp.einsum(
        "rckgd,rskd->rkgcs", grouped_queries, combined_keys, preferred_element_type=jnp.float32
    ) / math.sqrt(HEAD_WIDTH)
    allowed = allowed_keys(span_length, span_size, past_size)[:, None, None, :, :]
    scores = jnp.where(allowed, scores, -jnp.inf)
    weights = jax.nn.softmax(scores, axis=-1).astype(jnp.bfloat16)
    mixed_heads = jnp.einsum(
        "rkgcs,rskd->rckgd", weights, combined_values, preferred_element_type=jnp.float32
    )
    mixed_heads = mixed_heads.astype(jnp.bfloat16).reshape(total_rows, local_q * HEAD_WIDTH)
    head_share = scatter_features(mixed_heads, output_weight)
    residual_share = activations.astype(jnp.float32) + head_share

    gain_share = lax.dynamic_slice_in_dim(feedforward_gain, kv_index * width_share, width_share)
    normed_share = row_scale(residual_share, gain_share).astype(jnp.bfloat16)
    normed_two = gather_features(normed_share)
    gate_proj = jnp.dot(normed_two, gate_weight, preferred_element_type=jnp.float32)
    upward = jnp.dot(normed_two, up_weight, preferred_element_type=jnp.float32)
    hidden = (jax.nn.silu(gate_proj) * upward).astype(jnp.bfloat16)
    mlp_share = scatter_features(hidden, down_weight)
    live_rows = (jnp.arange(span_size, dtype=jnp.int32)[None, :] < span_length[:, None]).reshape(
        total_rows
    )
    layer_out = jnp.where(live_rows[:, None], residual_share + mlp_share, 0.0).astype(jnp.bfloat16)
    return (layer_out, decode_kv[0], decode_kv[1])


def solution(mesh):
    req_size, kv_size = mesh.devices.shape
    split_mesh = Mesh(
        mesh.devices.reshape(req_size, kv_size // CORES, CORES), ("req", "kvy", "core")
    )
    kv = ("kvy", "core")
    return jax.shard_map(
        local,
        mesh=split_mesh,
        in_specs=(
            P("req", kv),
            P("req"),
            P("req"),
            P("req"),
            P(),
            P(None, kv),
            P(None, kv),
            P(None, kv),
            P(kv, None),
            P(),
            P(None, kv),
            P(None, kv),
            P(kv, None),
            P("req", kv, None),
            P("req", kv, None),
        ),
        out_specs=(P("req", kv), P("req", None, kv), P("req", None, kv)),
        check_vma=False,
    )
```

```python
import math

import jax
import jax.numpy as jnp
from jax import lax
from jax.sharding import Mesh
from jax.sharding import PartitionSpec as P

HEAD_WIDTH = 256
CORES = 2


rope_base = 1000042.0
epsilon = 1e-05


def rotate_pairs(tensor, position):
    half_size = tensor.shape[-1] // 2
    steps_float = jnp.arange(half_size, dtype=jnp.float32)
    inverse = jnp.exp(steps_float * (-2.0 * math.log(rope_base) / tensor.shape[-1]))
    angles = position[:, :, None] * inverse[None, None, :]
    cosine = jnp.cos(angles)[:, :, None, :]
    sine_part = jnp.sin(angles)[:, :, None, :]
    first_half = tensor[..., :half_size]
    second = tensor[..., half_size:]
    return jnp.concatenate(
        [first_half * cosine - second * sine_part, second * cosine + first_half * sine_part],
        axis=-1,
    )


def allowed_keys(span_length, span_size, past_size):
    key_pos = jnp.arange(past_size + span_size, dtype=jnp.int32) - past_size
    query_pos = jnp.arange(span_size, dtype=jnp.int32)
    causal = key_pos[None, :] <= query_pos[:, None]
    live_keys = key_pos[None, None, :] < span_length[:, None, None]
    return (key_pos[None, None, :] < 0) | causal[None, :, :] & live_keys


def swap(values, axis_name):
    return lax.ppermute(values, axis_name, [(0, 1), (1, 0)])


def gather_features(share):
    chip = lax.axis_index("kvy")
    core = lax.axis_index("core")
    partner = swap(share, "kvy")
    pair = jnp.where(chip == 0, jnp.stack([share, partner]), jnp.stack([partner, share]))
    other = swap(pair, "core")
    blocks = []
    for chip_block in range(2):
        for core_block in range(2):
            blocks.append(jnp.where(core == core_block, pair[chip_block], other[chip_block]))
    return jnp.concatenate(blocks, axis=1)


def scatter_features(matrix_in, weight, link_type=None):
    chip = lax.axis_index("kvy")
    core = lax.axis_index("core")
    product = jnp.dot(matrix_in, weight, preferred_element_type=jnp.float32)
    width = product.shape[1] // (2 * CORES)

    def block(chip_block, core_block):
        start = (chip_block * CORES + core_block) * width
        return product[:, start:start + width]

    keep = jnp.stack([jnp.where(core == 0, block(k, 0), block(k, 1)) for k in range(2)])
    give = jnp.stack([jnp.where(core == 0, block(k, 1), block(k, 0)) for k in range(2)])
    chip_sum = keep + swap(give, "core")
    mine = jnp.where(chip == 0, chip_sum[0], chip_sum[1])
    theirs = jnp.where(chip == 0, chip_sum[1], chip_sum[0])
    if link_type is not None:
        theirs = theirs.astype(link_type)
    return mine + swap(theirs, "kvy").astype(jnp.float32)


def row_scale(values, gain_share):
    square_sum = jnp.sum(values * values, axis=-1, keepdims=True)
    square_sum = square_sum + swap(square_sum, "core")
    square_sum = square_sum + swap(square_sum, "kvy")
    width = values.shape[-1] * 2 * CORES
    return values * lax.rsqrt(square_sum / width + epsilon) * gain_share


def local(
    activations,
    span_length,
    offsets,
    decode_slot,
    attention_gain,
    query_weight,
    key_projection_matrix,
    value_projection_matrix,
    output_weight,
    feedforward_gain,
    gate_weight,
    up_weight,
    down_weight,
    earlier_rotated_keys,
    earlier_values,
):
    req_count = lax.axis_size("req")
    chips = lax.axis_size("kvy")
    kv_count = chips * CORES
    kv_index = lax.axis_index("kvy") * CORES + lax.axis_index("core")
    req_index = lax.axis_index("req")
    request_list = span_length.shape[0]
    total_rows, width_share = activations.shape
    span_size = total_rows // request_list
    local_kv = key_projection_matrix.shape[1] // HEAD_WIDTH
    local_q = query_weight.shape[1] // HEAD_WIDTH
    query_groups = local_q // local_kv

    past_share = earlier_rotated_keys.shape[1]
    stacked = jnp.stack([earlier_rotated_keys, earlier_values])
    stacked = stacked.reshape(2, request_list, past_share, kv_count, local_kv * HEAD_WIDTH)
    stacked = stacked.transpose(0, 3, 1, 2, 4)
    arrived = lax.all_to_all(stacked, ("kvy", "core"), split_axis=1, concat_axis=1, tiled=True)
    head_kv = arrived.transpose(0, 2, 1, 3, 4).reshape(
        2, request_list, kv_count * past_share, local_kv * HEAD_WIDTH
    )
    past_size = head_kv.shape[2]

    capacity = max(2, (request_list + req_count - 1) // req_count)
    order_ids = jnp.arange(request_list, dtype=jnp.int32)
    earlier = order_ids[None, :] < order_ids[:, None]
    own_dest = decode_slot // request_list
    same_dest = own_dest[:, None] == own_dest[None, :]
    own_rank = jnp.sum((same_dest & earlier).astype(jnp.int32), axis=1)
    buffer_place = own_dest * capacity + own_rank
    buffer_ids = jnp.arange(req_count * capacity, dtype=jnp.int32)
    matches = buffer_place[None, :] == buffer_ids[:, None]
    picked = jnp.sum(jnp.where(matches, order_ids[None, :], 0), axis=1)
    filled = jnp.any(matches, axis=1)
    lanes = local_kv * HEAD_WIDTH
    slot_code = jnp.stack([decode_slot // 16, decode_slot % 16], axis=1).astype(jnp.bfloat16)
    trailer = jnp.pad(slot_code, ((0, 0), (0, lanes - 2)))[:, None, :]
    payload = jnp.concatenate([head_kv[0], head_kv[1], trailer], axis=1)
    packed = jnp.take(payload, picked, axis=0)
    packed = jnp.where(filled[:, None, None], packed, -jnp.ones((), packed.dtype))
    packed = packed.reshape((req_count, capacity) + payload.shape[1:])
    landed = lax.all_to_all(packed, "req", split_axis=0, concat_axis=0, tiled=True)
    landed = landed.reshape((req_count * capacity,) + payload.shape[1:])
    code = landed[:, 2 * past_size, :2].astype(jnp.int32)
    landed_slots = code[:, 0] * 16 + code[:, 1]
    wanted = req_index * request_list + order_ids
    slot_hits = landed_slots[None, :] == wanted[:, None]
    entry_ids = jnp.arange(req_count * capacity, dtype=jnp.int32)
    slot_position = jnp.sum(jnp.where(slot_hits, entry_ids[None, :], 0), axis=1)
    decode_rows = jnp.take(landed, slot_position, axis=0)
    decode_kv = (decode_rows[:, :past_size], decode_rows[:, past_size:2 * past_size])

    x_whole = gather_features(activations)
    x_float = x_whole.astype(jnp.float32)
    square_sum = jnp.sum(x_float * x_float, axis=-1, keepdims=True)
    normalized_input = (
        x_float * lax.rsqrt(square_sum / x_float.shape[-1] + epsilon) * attention_gain
    ).astype(jnp.bfloat16)
    position = (
        offsets[:, None].astype(jnp.float32) + jnp.arange(span_size, dtype=jnp.float32)[None, :]
    )
    query_rows = jnp.dot(
        normalized_input, query_weight, preferred_element_type=jnp.float32
    ).reshape(request_list, span_size, local_q, HEAD_WIDTH)
    query_rows = rotate_pairs(query_rows, position).astype(jnp.bfloat16)
    fresh_keys = jnp.dot(
        normalized_input, key_projection_matrix, preferred_element_type=jnp.float32
    ).reshape(request_list, span_size, local_kv, HEAD_WIDTH)
    fresh_keys = rotate_pairs(fresh_keys, position).astype(jnp.bfloat16)
    fresh_values = (
        jnp.dot(normalized_input, value_projection_matrix, preferred_element_type=jnp.float32)
        .astype(jnp.bfloat16)
        .reshape(request_list, span_size, local_kv, HEAD_WIDTH)
    )
    combined_keys = jnp.concatenate(
        [head_kv[0].reshape(request_list, past_size, local_kv, HEAD_WIDTH), fresh_keys], axis=1
    )
    combined_values = jnp.concatenate(
        [head_kv[1].reshape(request_list, past_size, local_kv, HEAD_WIDTH), fresh_values], axis=1
    )
    grouped_queries = query_rows.reshape(
        request_list, span_size, local_kv, query_groups, HEAD_WIDTH
    )
    scores = jnp.einsum(
        "rckgd,rskd->rkgcs", grouped_queries, combined_keys, preferred_element_type=jnp.float32
    ) / math.sqrt(HEAD_WIDTH)
    allowed = allowed_keys(span_length, span_size, past_size)[:, None, None, :, :]
    scores = jnp.where(allowed, scores, -jnp.inf)
    weights = jax.nn.softmax(scores, axis=-1).astype(jnp.bfloat16)
    mixed_heads = jnp.einsum(
        "rkgcs,rskd->rckgd", weights, combined_values, preferred_element_type=jnp.float32
    )
    mixed_heads = mixed_heads.astype(jnp.bfloat16).reshape(total_rows, local_q * HEAD_WIDTH)
    head_share = scatter_features(mixed_heads, output_weight)
    residual_share = activations.astype(jnp.float32) + head_share

    gain_share = lax.dynamic_slice_in_dim(feedforward_gain, kv_index * width_share, width_share)
    normed_share = row_scale(residual_share, gain_share).astype(jnp.bfloat16)
    normed_two = gather_features(normed_share)
    gate_proj = jnp.dot(normed_two, gate_weight, preferred_element_type=jnp.float32)
    upward = jnp.dot(normed_two, up_weight, preferred_element_type=jnp.float32)
    hidden = (jax.nn.silu(gate_proj) * upward).astype(jnp.bfloat16)
    mlp_share = scatter_features(hidden, down_weight, jnp.bfloat16)
    live_rows = (jnp.arange(span_size, dtype=jnp.int32)[None, :] < span_length[:, None]).reshape(
        total_rows
    )
    layer_out = jnp.where(live_rows[:, None], residual_share + mlp_share, 0.0).astype(jnp.bfloat16)
    return (layer_out, decode_kv[0], decode_kv[1])


def solution(mesh):
    req_size, kv_size = mesh.devices.shape
    split_mesh = Mesh(
        mesh.devices.reshape(req_size, kv_size // CORES, CORES), ("req", "kvy", "core")
    )
    kv = ("kvy", "core")
    return jax.shard_map(
        local,
        mesh=split_mesh,
        in_specs=(
            P("req", kv),
            P("req"),
            P("req"),
            P("req"),
            P(),
            P(None, kv),
            P(None, kv),
            P(None, kv),
            P(kv, None),
            P(),
            P(None, kv),
            P(None, kv),
            P(kv, None),
            P("req", kv, None),
            P("req", kv, None),
        ),
        out_specs=(P("req", kv), P("req", None, kv), P("req", None, kv)),
        check_vma=False,
    )
```

```python
import math

import jax
import jax.numpy as jnp
from jax import lax
from jax.sharding import Mesh
from jax.sharding import PartitionSpec as P

HEAD_WIDTH = 256
CORES = 2


rope_base = 1000042.0
epsilon = 1e-05


def rotate_pairs(tensor, position):
    half_size = tensor.shape[-1] // 2
    steps_float = jnp.arange(half_size, dtype=jnp.float32)
    inverse = jnp.exp(steps_float * (-2.0 * math.log(rope_base) / tensor.shape[-1]))
    angles = position[:, :, None] * inverse[None, None, :]
    cosine = jnp.cos(angles)[:, :, None, :]
    sine_part = jnp.sin(angles)[:, :, None, :]
    first_half = tensor[..., :half_size]
    second = tensor[..., half_size:]
    return jnp.concatenate(
        [first_half * cosine - second * sine_part, second * cosine + first_half * sine_part],
        axis=-1,
    )


def allowed_keys(span_length, span_size, past_size):
    key_pos = jnp.arange(past_size + span_size, dtype=jnp.int32) - past_size
    query_pos = jnp.arange(span_size, dtype=jnp.int32)
    causal = key_pos[None, :] <= query_pos[:, None]
    live_keys = key_pos[None, None, :] < span_length[:, None, None]
    return (key_pos[None, None, :] < 0) | causal[None, :, :] & live_keys


def swap(values, axis_name):
    return lax.ppermute(values, axis_name, [(0, 1), (1, 0)])


def gather_features(share):
    chip = lax.axis_index("kvy")
    core = lax.axis_index("core")
    partner = swap(share, "kvy")
    pair = jnp.where(chip == 0, jnp.stack([share, partner]), jnp.stack([partner, share]))
    other = swap(pair, "core")
    blocks = []
    for chip_block in range(2):
        for core_block in range(2):
            blocks.append(jnp.where(core == core_block, pair[chip_block], other[chip_block]))
    return jnp.concatenate(blocks, axis=1)


def scatter_features(matrix_in, weight, link_type=None):
    chip = lax.axis_index("kvy")
    core = lax.axis_index("core")
    product = jnp.dot(matrix_in, weight, preferred_element_type=jnp.float32)
    width = product.shape[1] // (2 * CORES)

    def block(chip_block, core_block):
        start = (chip_block * CORES + core_block) * width
        return product[:, start:start + width]

    keep = jnp.stack([jnp.where(core == 0, block(k, 0), block(k, 1)) for k in range(2)])
    give = jnp.stack([jnp.where(core == 0, block(k, 1), block(k, 0)) for k in range(2)])
    chip_sum = keep + swap(give, "core")
    mine = jnp.where(chip == 0, chip_sum[0], chip_sum[1])
    theirs = jnp.where(chip == 0, chip_sum[1], chip_sum[0])
    if link_type is not None:
        theirs = theirs.astype(link_type)
    return mine + swap(theirs, "kvy").astype(jnp.float32)


def row_scale(values, gain_share):
    square_sum = jnp.sum(values * values, axis=-1, keepdims=True)
    square_sum = square_sum + swap(square_sum, "core")
    square_sum = square_sum + swap(square_sum, "kvy")
    width = values.shape[-1] * 2 * CORES
    return values * lax.rsqrt(square_sum / width + epsilon) * gain_share


def local(
    activations,
    span_length,
    offsets,
    decode_slot,
    attention_gain,
    query_weight,
    key_projection_matrix,
    value_projection_matrix,
    output_weight,
    feedforward_gain,
    gate_weight,
    up_weight,
    down_weight,
    earlier_rotated_keys,
    earlier_values,
):
    req_count = lax.axis_size("req")
    chips = lax.axis_size("kvy")
    kv_count = chips * CORES
    kv_index = lax.axis_index("kvy") * CORES + lax.axis_index("core")
    req_index = lax.axis_index("req")
    request_list = span_length.shape[0]
    total_rows, width_share = activations.shape
    span_size = total_rows // request_list
    local_kv = key_projection_matrix.shape[1] // HEAD_WIDTH
    local_q = query_weight.shape[1] // HEAD_WIDTH
    query_groups = local_q // local_kv

    past_share = earlier_rotated_keys.shape[1]
    stacked = jnp.stack([earlier_rotated_keys, earlier_values])
    stacked = stacked.reshape(2, request_list, past_share, kv_count, local_kv * HEAD_WIDTH)
    stacked = stacked.transpose(0, 3, 1, 2, 4)
    arrived = lax.all_to_all(stacked, ("kvy", "core"), split_axis=1, concat_axis=1, tiled=True)
    head_kv = arrived.transpose(0, 2, 1, 3, 4).reshape(
        2, request_list, kv_count * past_share, local_kv * HEAD_WIDTH
    )
    past_size = head_kv.shape[2]

    capacity = max(2, (request_list + req_count - 1) // req_count)
    order_ids = jnp.arange(request_list, dtype=jnp.int32)
    earlier = order_ids[None, :] < order_ids[:, None]
    own_dest = decode_slot // request_list
    same_dest = own_dest[:, None] == own_dest[None, :]
    own_rank = jnp.sum((same_dest & earlier).astype(jnp.int32), axis=1)
    buffer_place = own_dest * capacity + own_rank
    buffer_ids = jnp.arange(req_count * capacity, dtype=jnp.int32)
    matches = buffer_place[None, :] == buffer_ids[:, None]
    picked = jnp.sum(jnp.where(matches, order_ids[None, :], 0), axis=1)
    filled = jnp.any(matches, axis=1)
    lanes = local_kv * HEAD_WIDTH
    slot_code = jnp.stack([decode_slot // 16, decode_slot % 16], axis=1).astype(jnp.bfloat16)
    trailer = jnp.pad(slot_code, ((0, 0), (0, lanes - 2)))[:, None, :]
    payload = jnp.concatenate([head_kv[0], head_kv[1], trailer], axis=1)
    packed = jnp.take(payload, picked, axis=0)
    packed = jnp.where(filled[:, None, None], packed, -jnp.ones((), packed.dtype))
    packed = packed.reshape((req_count, capacity) + payload.shape[1:])
    landed = lax.all_to_all(packed, "req", split_axis=0, concat_axis=0, tiled=True)
    landed = landed.reshape((req_count * capacity,) + payload.shape[1:])
    code = landed[:, 2 * past_size, :2].astype(jnp.int32)
    landed_slots = code[:, 0] * 16 + code[:, 1]
    wanted = req_index * request_list + order_ids
    slot_hits = landed_slots[None, :] == wanted[:, None]
    entry_ids = jnp.arange(req_count * capacity, dtype=jnp.int32)
    slot_position = jnp.sum(jnp.where(slot_hits, entry_ids[None, :], 0), axis=1)
    decode_rows = jnp.take(landed, slot_position, axis=0)
    decode_kv = (decode_rows[:, :past_size], decode_rows[:, past_size:2 * past_size])

    gain_share = lax.dynamic_slice_in_dim(feedforward_gain, kv_index * width_share, width_share)

    def layer_rows(activations, span_length, offsets, past_keys, past_values):
        request_list = span_length.shape[0]
        total_rows = activations.shape[0]
        x_whole = gather_features(activations)
        x_float = x_whole.astype(jnp.float32)
        square_sum = jnp.sum(x_float * x_float, axis=-1, keepdims=True)
        normalized_input = (
            x_float * lax.rsqrt(square_sum / x_float.shape[-1] + epsilon) * attention_gain
        ).astype(jnp.bfloat16)
        position = (
            offsets[:, None].astype(jnp.float32) + jnp.arange(span_size, dtype=jnp.float32)[None, :]
        )
        query_rows = jnp.dot(
            normalized_input, query_weight, preferred_element_type=jnp.float32
        ).reshape(request_list, span_size, local_q, HEAD_WIDTH)
        query_rows = rotate_pairs(query_rows, position).astype(jnp.bfloat16)
        fresh_keys = jnp.dot(
            normalized_input, key_projection_matrix, preferred_element_type=jnp.float32
        ).reshape(request_list, span_size, local_kv, HEAD_WIDTH)
        fresh_keys = rotate_pairs(fresh_keys, position).astype(jnp.bfloat16)
        fresh_values = (
            jnp.dot(normalized_input, value_projection_matrix, preferred_element_type=jnp.float32)
            .astype(jnp.bfloat16)
            .reshape(request_list, span_size, local_kv, HEAD_WIDTH)
        )
        combined_keys = jnp.concatenate(
            [past_keys.reshape(request_list, past_size, local_kv, HEAD_WIDTH), fresh_keys], axis=1
        )
        combined_values = jnp.concatenate(
            [past_values.reshape(request_list, past_size, local_kv, HEAD_WIDTH), fresh_values], axis=1
        )
        grouped_queries = query_rows.reshape(
            request_list, span_size, local_kv, query_groups, HEAD_WIDTH
        )
        scores = jnp.einsum(
            "rckgd,rskd->rkgcs", grouped_queries, combined_keys, preferred_element_type=jnp.float32
        ) / math.sqrt(HEAD_WIDTH)
        allowed = allowed_keys(span_length, span_size, past_size)[:, None, None, :, :]
        scores = jnp.where(allowed, scores, -jnp.inf)
        weights = jax.nn.softmax(scores, axis=-1).astype(jnp.bfloat16)
        mixed_heads = jnp.einsum(
            "rkgcs,rskd->rckgd", weights, combined_values, preferred_element_type=jnp.float32
        )
        mixed_heads = mixed_heads.astype(jnp.bfloat16).reshape(total_rows, local_q * HEAD_WIDTH)
        head_share = scatter_features(mixed_heads, output_weight)
        residual_share = activations.astype(jnp.float32) + head_share

        normed_share = row_scale(residual_share, gain_share).astype(jnp.bfloat16)
        normed_two = gather_features(normed_share)
        gate_proj = jnp.dot(normed_two, gate_weight, preferred_element_type=jnp.float32)
        upward = jnp.dot(normed_two, up_weight, preferred_element_type=jnp.float32)
        hidden = (jax.nn.silu(gate_proj) * upward).astype(jnp.bfloat16)
        mlp_share = scatter_features(hidden, down_weight, jnp.bfloat16)
        live_rows = (jnp.arange(span_size, dtype=jnp.int32)[None, :] < span_length[:, None]).reshape(
            total_rows
        )
        layer_out = jnp.where(live_rows[:, None], residual_share + mlp_share, 0.0).astype(jnp.bfloat16)
        return layer_out

    first = (request_list + 1) // 2
    outputs = []
    for low, high in ((0, first), (first, request_list)):
        outputs.append(
            layer_rows(
                activations[low * span_size:high * span_size],
                span_length[low:high],
                offsets[low:high],
                head_kv[0, low:high],
                head_kv[1, low:high],
            )
        )
    layer_out = jnp.concatenate(outputs, axis=0)
    return (layer_out, decode_kv[0], decode_kv[1])


def solution(mesh):
    req_size, kv_size = mesh.devices.shape
    split_mesh = Mesh(
        mesh.devices.reshape(req_size, kv_size // CORES, CORES), ("req", "kvy", "core")
    )
    kv = ("kvy", "core")
    return jax.shard_map(
        local,
        mesh=split_mesh,
        in_specs=(
            P("req", kv),
            P("req"),
            P("req"),
            P("req"),
            P(),
            P(None, kv),
            P(None, kv),
            P(None, kv),
            P(kv, None),
            P(),
            P(None, kv),
            P(None, kv),
            P(kv, None),
            P("req", kv, None),
            P("req", kv, None),
        ),
        out_specs=(P("req", kv), P("req", None, kv), P("req", None, kv)),
        check_vma=False,
    )
```

```python
import math

import jax
import jax.numpy as jnp
from jax import lax
from jax.sharding import Mesh
from jax.sharding import PartitionSpec as P

HEAD_WIDTH = 256
CORES = 2


rope_base = 1000042.0
epsilon = 1e-05


def rotate_pairs(tensor, position):
    half_size = tensor.shape[-1] // 2
    steps_float = jnp.arange(half_size, dtype=jnp.float32)
    inverse = jnp.exp(steps_float * (-2.0 * math.log(rope_base) / tensor.shape[-1]))
    angles = position[:, :, None] * inverse[None, None, :]
    cosine = jnp.cos(angles)[:, :, None, :]
    sine_part = jnp.sin(angles)[:, :, None, :]
    first_half = tensor[..., :half_size]
    second = tensor[..., half_size:]
    return jnp.concatenate(
        [first_half * cosine - second * sine_part, second * cosine + first_half * sine_part],
        axis=-1,
    )


def allowed_keys(span_length, span_size, past_size):
    key_pos = jnp.arange(past_size + span_size, dtype=jnp.int32) - past_size
    query_pos = jnp.arange(span_size, dtype=jnp.int32)
    causal = key_pos[None, :] <= query_pos[:, None]
    live_keys = key_pos[None, None, :] < span_length[:, None, None]
    return (key_pos[None, None, :] < 0) | causal[None, :, :] & live_keys


def swap(values, axis_name):
    return lax.ppermute(values, axis_name, [(0, 1), (1, 0)])


def gather_features(share):
    chip = lax.axis_index("kvy")
    core = lax.axis_index("core")
    partner = swap(share, "kvy")
    pair = jnp.where(chip == 0, jnp.stack([share, partner]), jnp.stack([partner, share]))
    other = swap(pair, "core")
    blocks = []
    for chip_block in range(2):
        for core_block in range(2):
            blocks.append(jnp.where(core == core_block, pair[chip_block], other[chip_block]))
    return jnp.concatenate(blocks, axis=1)


def scatter_features(matrix_in, weight, link_type=None, ride=None):
    chip = lax.axis_index("kvy")
    core = lax.axis_index("core")
    product = jnp.dot(matrix_in, weight, preferred_element_type=jnp.float32)
    width = product.shape[1] // (2 * CORES)

    def block(chip_block, core_block):
        start = (chip_block * CORES + core_block) * width
        return product[:, start:start + width]

    keep = jnp.stack([jnp.where(core == 0, block(k, 0), block(k, 1)) for k in range(2)])
    give = jnp.stack([jnp.where(core == 0, block(k, 1), block(k, 0)) for k in range(2)])
    chip_sum = keep + swap(give, "core")
    mine = jnp.where(chip == 0, chip_sum[0], chip_sum[1])
    theirs = jnp.where(chip == 0, chip_sum[1], chip_sum[0])
    if link_type is not None:
        theirs = theirs.astype(link_type)
    if ride is None:
        return mine + swap(theirs, "kvy").astype(jnp.float32)
    ride_input, work = ride
    ride_input, theirs = lax.optimization_barrier((ride_input, theirs))
    arrived = swap(theirs, "kvy")
    ride_output = work(ride_input)
    ride_output, arrived = lax.optimization_barrier((ride_output, arrived))
    return mine + arrived.astype(jnp.float32), ride_output


def row_scale(values, gain_share):
    square_sum = jnp.sum(values * values, axis=-1, keepdims=True)
    square_sum = square_sum + swap(square_sum, "core")
    square_sum = square_sum + swap(square_sum, "kvy")
    width = values.shape[-1] * 2 * CORES
    return values * lax.rsqrt(square_sum / width + epsilon) * gain_share


def local(
    activations,
    span_length,
    offsets,
    decode_slot,
    attention_gain,
    query_weight,
    key_projection_matrix,
    value_projection_matrix,
    output_weight,
    feedforward_gain,
    gate_weight,
    up_weight,
    down_weight,
    earlier_rotated_keys,
    earlier_values,
):
    req_count = lax.axis_size("req")
    chips = lax.axis_size("kvy")
    kv_count = chips * CORES
    kv_index = lax.axis_index("kvy") * CORES + lax.axis_index("core")
    req_index = lax.axis_index("req")
    request_list = span_length.shape[0]
    total_rows, width_share = activations.shape
    span_size = total_rows // request_list
    local_kv = key_projection_matrix.shape[1] // HEAD_WIDTH
    local_q = query_weight.shape[1] // HEAD_WIDTH
    query_groups = local_q // local_kv

    past_share = earlier_rotated_keys.shape[1]
    stacked = jnp.stack([earlier_rotated_keys, earlier_values])
    stacked = stacked.reshape(2, request_list, past_share, kv_count, local_kv * HEAD_WIDTH)
    stacked = stacked.transpose(0, 3, 1, 2, 4)
    arrived = lax.all_to_all(stacked, ("kvy", "core"), split_axis=1, concat_axis=1, tiled=True)
    head_kv = arrived.transpose(0, 2, 1, 3, 4).reshape(
        2, request_list, kv_count * past_share, local_kv * HEAD_WIDTH
    )
    past_size = head_kv.shape[2]

    capacity = max(2, (request_list + req_count - 1) // req_count)
    order_ids = jnp.arange(request_list, dtype=jnp.int32)
    earlier = order_ids[None, :] < order_ids[:, None]
    own_dest = decode_slot // request_list
    same_dest = own_dest[:, None] == own_dest[None, :]
    own_rank = jnp.sum((same_dest & earlier).astype(jnp.int32), axis=1)
    buffer_place = own_dest * capacity + own_rank
    buffer_ids = jnp.arange(req_count * capacity, dtype=jnp.int32)
    matches = buffer_place[None, :] == buffer_ids[:, None]
    picked = jnp.sum(jnp.where(matches, order_ids[None, :], 0), axis=1)
    filled = jnp.any(matches, axis=1)
    def hand_off(ride_input):
        head_kv, decode_slot, picked, filled = ride_input
        lanes = local_kv * HEAD_WIDTH
        slot_code = jnp.stack([decode_slot // 16, decode_slot % 16], axis=1).astype(jnp.bfloat16)
        trailer = jnp.pad(slot_code, ((0, 0), (0, lanes - 2)))[:, None, :]
        payload = jnp.concatenate([head_kv[0], head_kv[1], trailer], axis=1)
        packed = jnp.take(payload, picked, axis=0)
        packed = jnp.where(filled[:, None, None], packed, -jnp.ones((), packed.dtype))
        packed = packed.reshape((req_count, capacity) + payload.shape[1:])
        landed = lax.all_to_all(packed, "req", split_axis=0, concat_axis=0, tiled=True)
        landed = landed.reshape((req_count * capacity,) + payload.shape[1:])
        code = landed[:, 2 * past_size, :2].astype(jnp.int32)
        landed_slots = code[:, 0] * 16 + code[:, 1]
        wanted = req_index * request_list + order_ids
        slot_hits = landed_slots[None, :] == wanted[:, None]
        entry_ids = jnp.arange(req_count * capacity, dtype=jnp.int32)
        slot_position = jnp.sum(jnp.where(slot_hits, entry_ids[None, :], 0), axis=1)
        decode_rows = jnp.take(landed, slot_position, axis=0)
        return decode_rows[:, :past_size], decode_rows[:, past_size:2 * past_size]


    x_whole = gather_features(activations)
    x_float = x_whole.astype(jnp.float32)
    square_sum = jnp.sum(x_float * x_float, axis=-1, keepdims=True)
    normalized_input = (
        x_float * lax.rsqrt(square_sum / x_float.shape[-1] + epsilon) * attention_gain
    ).astype(jnp.bfloat16)
    position = (
        offsets[:, None].astype(jnp.float32) + jnp.arange(span_size, dtype=jnp.float32)[None, :]
    )
    query_rows = jnp.dot(
        normalized_input, query_weight, preferred_element_type=jnp.float32
    ).reshape(request_list, span_size, local_q, HEAD_WIDTH)
    query_rows = rotate_pairs(query_rows, position).astype(jnp.bfloat16)
    fresh_keys = jnp.dot(
        normalized_input, key_projection_matrix, preferred_element_type=jnp.float32
    ).reshape(request_list, span_size, local_kv, HEAD_WIDTH)
    fresh_keys = rotate_pairs(fresh_keys, position).astype(jnp.bfloat16)
    fresh_values = (
        jnp.dot(normalized_input, value_projection_matrix, preferred_element_type=jnp.float32)
        .astype(jnp.bfloat16)
        .reshape(request_list, span_size, local_kv, HEAD_WIDTH)
    )
    combined_keys = jnp.concatenate(
        [head_kv[0].reshape(request_list, past_size, local_kv, HEAD_WIDTH), fresh_keys], axis=1
    )
    combined_values = jnp.concatenate(
        [head_kv[1].reshape(request_list, past_size, local_kv, HEAD_WIDTH), fresh_values], axis=1
    )
    grouped_queries = query_rows.reshape(
        request_list, span_size, local_kv, query_groups, HEAD_WIDTH
    )
    scores = jnp.einsum(
        "rckgd,rskd->rkgcs", grouped_queries, combined_keys, preferred_element_type=jnp.float32
    ) / math.sqrt(HEAD_WIDTH)
    allowed = allowed_keys(span_length, span_size, past_size)[:, None, None, :, :]
    scores = jnp.where(allowed, scores, -jnp.inf)
    weights = jax.nn.softmax(scores, axis=-1).astype(jnp.bfloat16)
    mixed_heads = jnp.einsum(
        "rkgcs,rskd->rckgd", weights, combined_values, preferred_element_type=jnp.float32
    )
    mixed_heads = mixed_heads.astype(jnp.bfloat16).reshape(total_rows, local_q * HEAD_WIDTH)
    head_share, decode_kv = scatter_features(
        mixed_heads, output_weight, ride=((head_kv, decode_slot, picked, filled), hand_off)
    )
    residual_share = activations.astype(jnp.float32) + head_share

    gain_share = lax.dynamic_slice_in_dim(feedforward_gain, kv_index * width_share, width_share)
    normed_share = row_scale(residual_share, gain_share).astype(jnp.bfloat16)
    normed_two = gather_features(normed_share)
    gate_proj = jnp.dot(normed_two, gate_weight, preferred_element_type=jnp.float32)
    upward = jnp.dot(normed_two, up_weight, preferred_element_type=jnp.float32)
    hidden = (jax.nn.silu(gate_proj) * upward).astype(jnp.bfloat16)
    mlp_share = scatter_features(hidden, down_weight, jnp.bfloat16)
    live_rows = (jnp.arange(span_size, dtype=jnp.int32)[None, :] < span_length[:, None]).reshape(
        total_rows
    )
    layer_out = jnp.where(live_rows[:, None], residual_share + mlp_share, 0.0).astype(jnp.bfloat16)
    return (layer_out, decode_kv[0], decode_kv[1])


def solution(mesh):
    req_size, kv_size = mesh.devices.shape
    split_mesh = Mesh(
        mesh.devices.reshape(req_size, kv_size // CORES, CORES), ("req", "kvy", "core")
    )
    kv = ("kvy", "core")
    return jax.shard_map(
        local,
        mesh=split_mesh,
        in_specs=(
            P("req", kv),
            P("req"),
            P("req"),
            P("req"),
            P(),
            P(None, kv),
            P(None, kv),
            P(None, kv),
            P(kv, None),
            P(),
            P(None, kv),
            P(None, kv),
            P(kv, None),
            P("req", kv, None),
            P("req", kv, None),
        ),
        out_specs=(P("req", kv), P("req", None, kv), P("req", None, kv)),
        check_vma=False,
    )
```

```python
import math

import jax
import jax.numpy as jnp
from jax import lax
from jax.sharding import Mesh
from jax.sharding import PartitionSpec as P

HEAD_WIDTH = 256
CORES = 2


rope_base = 1000042.0
epsilon = 1e-05


def rotate_pairs(tensor, position):
    half_size = tensor.shape[-1] // 2
    steps_float = jnp.arange(half_size, dtype=jnp.float32)
    inverse = jnp.exp(steps_float * (-2.0 * math.log(rope_base) / tensor.shape[-1]))
    angles = position[:, :, None] * inverse[None, None, :]
    cosine = jnp.cos(angles)[:, :, None, :]
    sine_part = jnp.sin(angles)[:, :, None, :]
    first_half = tensor[..., :half_size]
    second = tensor[..., half_size:]
    return jnp.concatenate(
        [first_half * cosine - second * sine_part, second * cosine + first_half * sine_part],
        axis=-1,
    )


def allowed_keys(span_length, span_size, past_size):
    key_pos = jnp.arange(past_size + span_size, dtype=jnp.int32) - past_size
    query_pos = jnp.arange(span_size, dtype=jnp.int32)
    causal = key_pos[None, :] <= query_pos[:, None]
    live_keys = key_pos[None, None, :] < span_length[:, None, None]
    return (key_pos[None, None, :] < 0) | causal[None, :, :] & live_keys


def swap(values, axis_name):
    return lax.ppermute(values, axis_name, [(0, 1), (1, 0)])


def gather_features(share):
    chip = lax.axis_index("kvy")
    core = lax.axis_index("core")
    partner = swap(share, "kvy")
    pair = jnp.where(chip == 0, jnp.stack([share, partner]), jnp.stack([partner, share]))
    other = swap(pair, "core")
    blocks = []
    for chip_block in range(2):
        for core_block in range(2):
            blocks.append(jnp.where(core == core_block, pair[chip_block], other[chip_block]))
    return jnp.concatenate(blocks, axis=1)


def gather_project(share, weights):
    chip = lax.axis_index("kvy")
    core = lax.axis_index("core")
    from_core = swap(share, "core")
    from_chip = swap(share, "kvy")
    local_pair = jnp.where(
        core == 0,
        jnp.concatenate([share, from_core], axis=1),
        jnp.concatenate([from_core, share], axis=1),
    )
    half = local_pair.shape[1]
    local_parts = tuple(
        jnp.dot(
            local_pair,
            lax.dynamic_slice_in_dim(weight, chip * half, half, 0),
            preferred_element_type=jnp.float32,
        )
        for weight in weights
    )
    from_chip, local_parts = lax.optimization_barrier((from_chip, local_parts))
    from_diagonal = swap(from_chip, "core")
    remote_pair = jnp.where(
        core == 0,
        jnp.concatenate([from_chip, from_diagonal], axis=1),
        jnp.concatenate([from_diagonal, from_chip], axis=1),
    )
    return [
        part
        + jnp.dot(
            remote_pair,
            lax.dynamic_slice_in_dim(weight, (1 - chip) * half, half, 0),
            preferred_element_type=jnp.float32,
        )
        for part, weight in zip(local_parts, weights)
    ]


def scatter_features(matrix_in, weight, link_type=None):
    chip = lax.axis_index("kvy")
    core = lax.axis_index("core")
    product = jnp.dot(matrix_in, weight, preferred_element_type=jnp.float32)
    width = product.shape[1] // (2 * CORES)

    def block(chip_block, core_block):
        start = (chip_block * CORES + core_block) * width
        return product[:, start:start + width]

    keep = jnp.stack([jnp.where(core == 0, block(k, 0), block(k, 1)) for k in range(2)])
    give = jnp.stack([jnp.where(core == 0, block(k, 1), block(k, 0)) for k in range(2)])
    chip_sum = keep + swap(give, "core")
    mine = jnp.where(chip == 0, chip_sum[0], chip_sum[1])
    theirs = jnp.where(chip == 0, chip_sum[1], chip_sum[0])
    if link_type is not None:
        theirs = theirs.astype(link_type)
    return mine + swap(theirs, "kvy").astype(jnp.float32)


def row_scale(values, gain_share):
    square_sum = jnp.sum(values * values, axis=-1, keepdims=True)
    square_sum = square_sum + swap(square_sum, "core")
    square_sum = square_sum + swap(square_sum, "kvy")
    width = values.shape[-1] * 2 * CORES
    return values * lax.rsqrt(square_sum / width + epsilon) * gain_share


def local(
    activations,
    span_length,
    offsets,
    decode_slot,
    attention_gain,
    query_weight,
    key_projection_matrix,
    value_projection_matrix,
    output_weight,
    feedforward_gain,
    gate_weight,
    up_weight,
    down_weight,
    earlier_rotated_keys,
    earlier_values,
):
    req_count = lax.axis_size("req")
    chips = lax.axis_size("kvy")
    kv_count = chips * CORES
    kv_index = lax.axis_index("kvy") * CORES + lax.axis_index("core")
    req_index = lax.axis_index("req")
    request_list = span_length.shape[0]
    total_rows, width_share = activations.shape
    span_size = total_rows // request_list
    local_kv = key_projection_matrix.shape[1] // HEAD_WIDTH
    local_q = query_weight.shape[1] // HEAD_WIDTH
    query_groups = local_q // local_kv

    past_share = earlier_rotated_keys.shape[1]
    stacked = jnp.stack([earlier_rotated_keys, earlier_values])
    stacked = stacked.reshape(2, request_list, past_share, kv_count, local_kv * HEAD_WIDTH)
    stacked = stacked.transpose(0, 3, 1, 2, 4)
    arrived = lax.all_to_all(stacked, ("kvy", "core"), split_axis=1, concat_axis=1, tiled=True)
    head_kv = arrived.transpose(0, 2, 1, 3, 4).reshape(
        2, request_list, kv_count * past_share, local_kv * HEAD_WIDTH
    )
    past_size = head_kv.shape[2]

    capacity = max(2, (request_list + req_count - 1) // req_count)
    order_ids = jnp.arange(request_list, dtype=jnp.int32)
    earlier = order_ids[None, :] < order_ids[:, None]
    own_dest = decode_slot // request_list
    same_dest = own_dest[:, None] == own_dest[None, :]
    own_rank = jnp.sum((same_dest & earlier).astype(jnp.int32), axis=1)
    buffer_place = own_dest * capacity + own_rank
    buffer_ids = jnp.arange(req_count * capacity, dtype=jnp.int32)
    matches = buffer_place[None, :] == buffer_ids[:, None]
    picked = jnp.sum(jnp.where(matches, order_ids[None, :], 0), axis=1)
    filled = jnp.any(matches, axis=1)
    lanes = local_kv * HEAD_WIDTH
    slot_code = jnp.stack([decode_slot // 16, decode_slot % 16], axis=1).astype(jnp.bfloat16)
    trailer = jnp.pad(slot_code, ((0, 0), (0, lanes - 2)))[:, None, :]
    payload = jnp.concatenate([head_kv[0], head_kv[1], trailer], axis=1)
    packed = jnp.take(payload, picked, axis=0)
    packed = jnp.where(filled[:, None, None], packed, -jnp.ones((), packed.dtype))
    packed = packed.reshape((req_count, capacity) + payload.shape[1:])
    landed = lax.all_to_all(packed, "req", split_axis=0, concat_axis=0, tiled=True)
    landed = landed.reshape((req_count * capacity,) + payload.shape[1:])
    code = landed[:, 2 * past_size, :2].astype(jnp.int32)
    landed_slots = code[:, 0] * 16 + code[:, 1]
    wanted = req_index * request_list + order_ids
    slot_hits = landed_slots[None, :] == wanted[:, None]
    entry_ids = jnp.arange(req_count * capacity, dtype=jnp.int32)
    slot_position = jnp.sum(jnp.where(slot_hits, entry_ids[None, :], 0), axis=1)
    decode_rows = jnp.take(landed, slot_position, axis=0)
    decode_kv = (decode_rows[:, :past_size], decode_rows[:, past_size:2 * past_size])

    x_whole = gather_features(activations)
    x_float = x_whole.astype(jnp.float32)
    square_sum = jnp.sum(x_float * x_float, axis=-1, keepdims=True)
    normalized_input = (
        x_float * lax.rsqrt(square_sum / x_float.shape[-1] + epsilon) * attention_gain
    ).astype(jnp.bfloat16)
    position = (
        offsets[:, None].astype(jnp.float32) + jnp.arange(span_size, dtype=jnp.float32)[None, :]
    )
    query_rows = jnp.dot(
        normalized_input, query_weight, preferred_element_type=jnp.float32
    ).reshape(request_list, span_size, local_q, HEAD_WIDTH)
    query_rows = rotate_pairs(query_rows, position).astype(jnp.bfloat16)
    fresh_keys = jnp.dot(
        normalized_input, key_projection_matrix, preferred_element_type=jnp.float32
    ).reshape(request_list, span_size, local_kv, HEAD_WIDTH)
    fresh_keys = rotate_pairs(fresh_keys, position).astype(jnp.bfloat16)
    fresh_values = (
        jnp.dot(normalized_input, value_projection_matrix, preferred_element_type=jnp.float32)
        .astype(jnp.bfloat16)
        .reshape(request_list, span_size, local_kv, HEAD_WIDTH)
    )
    combined_keys = jnp.concatenate(
        [head_kv[0].reshape(request_list, past_size, local_kv, HEAD_WIDTH), fresh_keys], axis=1
    )
    combined_values = jnp.concatenate(
        [head_kv[1].reshape(request_list, past_size, local_kv, HEAD_WIDTH), fresh_values], axis=1
    )
    grouped_queries = query_rows.reshape(
        request_list, span_size, local_kv, query_groups, HEAD_WIDTH
    )
    scores = jnp.einsum(
        "rckgd,rskd->rkgcs", grouped_queries, combined_keys, preferred_element_type=jnp.float32
    ) / math.sqrt(HEAD_WIDTH)
    allowed = allowed_keys(span_length, span_size, past_size)[:, None, None, :, :]
    scores = jnp.where(allowed, scores, -jnp.inf)
    weights = jax.nn.softmax(scores, axis=-1).astype(jnp.bfloat16)
    mixed_heads = jnp.einsum(
        "rkgcs,rskd->rckgd", weights, combined_values, preferred_element_type=jnp.float32
    )
    mixed_heads = mixed_heads.astype(jnp.bfloat16).reshape(total_rows, local_q * HEAD_WIDTH)
    head_share = scatter_features(mixed_heads, output_weight)
    residual_share = activations.astype(jnp.float32) + head_share

    gain_share = lax.dynamic_slice_in_dim(feedforward_gain, kv_index * width_share, width_share)
    normed_share = row_scale(residual_share, gain_share).astype(jnp.bfloat16)
    gate_proj, upward = gather_project(normed_share, (gate_weight, up_weight))
    hidden = (jax.nn.silu(gate_proj) * upward).astype(jnp.bfloat16)
    mlp_share = scatter_features(hidden, down_weight, jnp.bfloat16)
    live_rows = (jnp.arange(span_size, dtype=jnp.int32)[None, :] < span_length[:, None]).reshape(
        total_rows
    )
    layer_out = jnp.where(live_rows[:, None], residual_share + mlp_share, 0.0).astype(jnp.bfloat16)
    return (layer_out, decode_kv[0], decode_kv[1])


def solution(mesh):
    req_size, kv_size = mesh.devices.shape
    split_mesh = Mesh(
        mesh.devices.reshape(req_size, kv_size // CORES, CORES), ("req", "kvy", "core")
    )
    kv = ("kvy", "core")
    return jax.shard_map(
        local,
        mesh=split_mesh,
        in_specs=(
            P("req", kv),
            P("req"),
            P("req"),
            P("req"),
            P(),
            P(None, kv),
            P(None, kv),
            P(None, kv),
            P(kv, None),
            P(),
            P(None, kv),
            P(None, kv),
            P(kv, None),
            P("req", kv, None),
            P("req", kv, None),
        ),
        out_specs=(P("req", kv), P("req", None, kv), P("req", None, kv)),
        check_vma=False,
    )
```

```python
import math

import jax
import jax.numpy as jnp
from jax import lax
from jax.sharding import Mesh
from jax.sharding import PartitionSpec as P

HEAD_WIDTH = 256
CORES = 2


rope_base = 1000042.0
epsilon = 1e-05


def rotate_pairs(tensor, position):
    half_size = tensor.shape[-1] // 2
    steps_float = jnp.arange(half_size, dtype=jnp.float32)
    inverse = jnp.exp(steps_float * (-2.0 * math.log(rope_base) / tensor.shape[-1]))
    angles = position[:, :, None] * inverse[None, None, :]
    cosine = jnp.cos(angles)[:, :, None, :]
    sine_part = jnp.sin(angles)[:, :, None, :]
    first_half = tensor[..., :half_size]
    second = tensor[..., half_size:]
    return jnp.concatenate(
        [first_half * cosine - second * sine_part, second * cosine + first_half * sine_part],
        axis=-1,
    )


def allowed_keys(span_length, span_size, past_size):
    key_pos = jnp.arange(past_size + span_size, dtype=jnp.int32) - past_size
    query_pos = jnp.arange(span_size, dtype=jnp.int32)
    causal = key_pos[None, :] <= query_pos[:, None]
    live_keys = key_pos[None, None, :] < span_length[:, None, None]
    return (key_pos[None, None, :] < 0) | causal[None, :, :] & live_keys


def swap(values, axis_name):
    return lax.ppermute(values, axis_name, [(0, 1), (1, 0)])


def gather_features(share):
    chip = lax.axis_index("kvy")
    core = lax.axis_index("core")
    partner = swap(share, "kvy")
    pair = jnp.where(chip == 0, jnp.stack([share, partner]), jnp.stack([partner, share]))
    other = swap(pair, "core")
    blocks = []
    for chip_block in range(2):
        for core_block in range(2):
            blocks.append(jnp.where(core == core_block, pair[chip_block], other[chip_block]))
    return jnp.concatenate(blocks, axis=1)


def gather_project(share, weights):
    chip = lax.axis_index("kvy")
    core = lax.axis_index("core")
    from_core = swap(share, "core")
    from_chip = swap(share, "kvy")
    local_pair = jnp.where(
        core == 0,
        jnp.concatenate([share, from_core], axis=1),
        jnp.concatenate([from_core, share], axis=1),
    )
    half = local_pair.shape[1]
    local_parts = tuple(
        jnp.dot(
            local_pair,
            lax.dynamic_slice_in_dim(weight, chip * half, half, 0),
            preferred_element_type=jnp.float32,
        )
        for weight in weights
    )
    from_chip, local_parts = lax.optimization_barrier((from_chip, local_parts))
    from_diagonal = swap(from_chip, "core")
    remote_pair = jnp.where(
        core == 0,
        jnp.concatenate([from_chip, from_diagonal], axis=1),
        jnp.concatenate([from_diagonal, from_chip], axis=1),
    )
    return [
        part
        + jnp.dot(
            remote_pair,
            lax.dynamic_slice_in_dim(weight, (1 - chip) * half, half, 0),
            preferred_element_type=jnp.float32,
        )
        for part, weight in zip(local_parts, weights)
    ]


def scatter_features(matrix_in, weight, link_type=None):
    chip = lax.axis_index("kvy")
    core = lax.axis_index("core")
    product = jnp.dot(matrix_in, weight, preferred_element_type=jnp.float32)
    width = product.shape[1] // (2 * CORES)

    def block(chip_block, core_block):
        start = (chip_block * CORES + core_block) * width
        return product[:, start:start + width]

    keep = jnp.stack([jnp.where(core == 0, block(k, 0), block(k, 1)) for k in range(2)])
    give = jnp.stack([jnp.where(core == 0, block(k, 1), block(k, 0)) for k in range(2)])
    chip_sum = keep + swap(give, "core")
    mine = jnp.where(chip == 0, chip_sum[0], chip_sum[1])
    theirs = jnp.where(chip == 0, chip_sum[1], chip_sum[0])
    if link_type is not None:
        theirs = theirs.astype(link_type)
    return mine + swap(theirs, "kvy").astype(jnp.float32)


def scatter_pipelined(matrix_in, weight, link_type):
    chip = lax.axis_index("kvy")
    core = lax.axis_index("core")
    width = weight.shape[1] // (2 * CORES)

    def product(chip_block, core_block, left):
        start = (chip_block * CORES + core_block) * width
        columns = lax.dynamic_slice_in_dim(weight, start, width, 1)
        return jnp.dot(left, columns, preferred_element_type=jnp.float32)

    for_partner = product(1 - chip, 1 - core, matrix_in)
    theirs = product(1 - chip, core, matrix_in) + swap(for_partner, "core")
    theirs = theirs.astype(link_type)
    theirs, later_in = lax.optimization_barrier((theirs, matrix_in))
    arrived = swap(theirs, "kvy")
    from_partner = swap(product(chip, 1 - core, later_in), "core")
    own = product(chip, core, later_in)
    own, from_partner = lax.optimization_barrier((own, from_partner))
    return own + from_partner + arrived.astype(jnp.float32)


def row_scale(values, gain_share):
    square_sum = jnp.sum(values * values, axis=-1, keepdims=True)
    square_sum = square_sum + swap(square_sum, "core")
    square_sum = square_sum + swap(square_sum, "kvy")
    width = values.shape[-1] * 2 * CORES
    return values * lax.rsqrt(square_sum / width + epsilon) * gain_share


def local(
    activations,
    span_length,
    offsets,
    decode_slot,
    attention_gain,
    query_weight,
    key_projection_matrix,
    value_projection_matrix,
    output_weight,
    feedforward_gain,
    gate_weight,
    up_weight,
    down_weight,
    earlier_rotated_keys,
    earlier_values,
):
    req_count = lax.axis_size("req")
    chips = lax.axis_size("kvy")
    kv_count = chips * CORES
    kv_index = lax.axis_index("kvy") * CORES + lax.axis_index("core")
    req_index = lax.axis_index("req")
    request_list = span_length.shape[0]
    total_rows, width_share = activations.shape
    span_size = total_rows // request_list
    local_kv = key_projection_matrix.shape[1] // HEAD_WIDTH
    local_q = query_weight.shape[1] // HEAD_WIDTH
    query_groups = local_q // local_kv

    past_share = earlier_rotated_keys.shape[1]
    stacked = jnp.stack([earlier_rotated_keys, earlier_values])
    stacked = stacked.reshape(2, request_list, past_share, kv_count, local_kv * HEAD_WIDTH)
    stacked = stacked.transpose(0, 3, 1, 2, 4)
    arrived = lax.all_to_all(stacked, ("kvy", "core"), split_axis=1, concat_axis=1, tiled=True)
    head_kv = arrived.transpose(0, 2, 1, 3, 4).reshape(
        2, request_list, kv_count * past_share, local_kv * HEAD_WIDTH
    )
    past_size = head_kv.shape[2]

    capacity = max(2, (request_list + req_count - 1) // req_count)
    order_ids = jnp.arange(request_list, dtype=jnp.int32)
    earlier = order_ids[None, :] < order_ids[:, None]
    own_dest = decode_slot // request_list
    same_dest = own_dest[:, None] == own_dest[None, :]
    own_rank = jnp.sum((same_dest & earlier).astype(jnp.int32), axis=1)
    buffer_place = own_dest * capacity + own_rank
    buffer_ids = jnp.arange(req_count * capacity, dtype=jnp.int32)
    matches = buffer_place[None, :] == buffer_ids[:, None]
    picked = jnp.sum(jnp.where(matches, order_ids[None, :], 0), axis=1)
    filled = jnp.any(matches, axis=1)
    lanes = local_kv * HEAD_WIDTH
    slot_code = jnp.stack([decode_slot // 16, decode_slot % 16], axis=1).astype(jnp.bfloat16)
    trailer = jnp.pad(slot_code, ((0, 0), (0, lanes - 2)))[:, None, :]
    payload = jnp.concatenate([head_kv[0], head_kv[1], trailer], axis=1)
    packed = jnp.take(payload, picked, axis=0)
    packed = jnp.where(filled[:, None, None], packed, -jnp.ones((), packed.dtype))
    packed = packed.reshape((req_count, capacity) + payload.shape[1:])
    landed = lax.all_to_all(packed, "req", split_axis=0, concat_axis=0, tiled=True)
    landed = landed.reshape((req_count * capacity,) + payload.shape[1:])
    code = landed[:, 2 * past_size, :2].astype(jnp.int32)
    landed_slots = code[:, 0] * 16 + code[:, 1]
    wanted = req_index * request_list + order_ids
    slot_hits = landed_slots[None, :] == wanted[:, None]
    entry_ids = jnp.arange(req_count * capacity, dtype=jnp.int32)
    slot_position = jnp.sum(jnp.where(slot_hits, entry_ids[None, :], 0), axis=1)
    decode_rows = jnp.take(landed, slot_position, axis=0)
    decode_kv = (decode_rows[:, :past_size], decode_rows[:, past_size:2 * past_size])

    x_whole = gather_features(activations)
    x_float = x_whole.astype(jnp.float32)
    square_sum = jnp.sum(x_float * x_float, axis=-1, keepdims=True)
    normalized_input = (
        x_float * lax.rsqrt(square_sum / x_float.shape[-1] + epsilon) * attention_gain
    ).astype(jnp.bfloat16)
    position = (
        offsets[:, None].astype(jnp.float32) + jnp.arange(span_size, dtype=jnp.float32)[None, :]
    )
    query_rows = jnp.dot(
        normalized_input, query_weight, preferred_element_type=jnp.float32
    ).reshape(request_list, span_size, local_q, HEAD_WIDTH)
    query_rows = rotate_pairs(query_rows, position).astype(jnp.bfloat16)
    fresh_keys = jnp.dot(
        normalized_input, key_projection_matrix, preferred_element_type=jnp.float32
    ).reshape(request_list, span_size, local_kv, HEAD_WIDTH)
    fresh_keys = rotate_pairs(fresh_keys, position).astype(jnp.bfloat16)
    fresh_values = (
        jnp.dot(normalized_input, value_projection_matrix, preferred_element_type=jnp.float32)
        .astype(jnp.bfloat16)
        .reshape(request_list, span_size, local_kv, HEAD_WIDTH)
    )
    combined_keys = jnp.concatenate(
        [head_kv[0].reshape(request_list, past_size, local_kv, HEAD_WIDTH), fresh_keys], axis=1
    )
    combined_values = jnp.concatenate(
        [head_kv[1].reshape(request_list, past_size, local_kv, HEAD_WIDTH), fresh_values], axis=1
    )
    grouped_queries = query_rows.reshape(
        request_list, span_size, local_kv, query_groups, HEAD_WIDTH
    )
    scores = jnp.einsum(
        "rckgd,rskd->rkgcs", grouped_queries, combined_keys, preferred_element_type=jnp.float32
    ) / math.sqrt(HEAD_WIDTH)
    allowed = allowed_keys(span_length, span_size, past_size)[:, None, None, :, :]
    scores = jnp.where(allowed, scores, -jnp.inf)
    weights = jax.nn.softmax(scores, axis=-1).astype(jnp.bfloat16)
    mixed_heads = jnp.einsum(
        "rkgcs,rskd->rckgd", weights, combined_values, preferred_element_type=jnp.float32
    )
    mixed_heads = mixed_heads.astype(jnp.bfloat16).reshape(total_rows, local_q * HEAD_WIDTH)
    head_share = scatter_features(mixed_heads, output_weight)
    residual_share = activations.astype(jnp.float32) + head_share

    gain_share = lax.dynamic_slice_in_dim(feedforward_gain, kv_index * width_share, width_share)
    normed_share = row_scale(residual_share, gain_share).astype(jnp.bfloat16)
    gate_proj, upward = gather_project(normed_share, (gate_weight, up_weight))
    hidden = (jax.nn.silu(gate_proj) * upward).astype(jnp.bfloat16)
    mlp_share = scatter_pipelined(hidden, down_weight, jnp.bfloat16)
    live_rows = (jnp.arange(span_size, dtype=jnp.int32)[None, :] < span_length[:, None]).reshape(
        total_rows
    )
    layer_out = jnp.where(live_rows[:, None], residual_share + mlp_share, 0.0).astype(jnp.bfloat16)
    return (layer_out, decode_kv[0], decode_kv[1])


def solution(mesh):
    req_size, kv_size = mesh.devices.shape
    split_mesh = Mesh(
        mesh.devices.reshape(req_size, kv_size // CORES, CORES), ("req", "kvy", "core")
    )
    kv = ("kvy", "core")
    return jax.shard_map(
        local,
        mesh=split_mesh,
        in_specs=(
            P("req", kv),
            P("req"),
            P("req"),
            P("req"),
            P(),
            P(None, kv),
            P(None, kv),
            P(None, kv),
            P(kv, None),
            P(),
            P(None, kv),
            P(None, kv),
            P(kv, None),
            P("req", kv, None),
            P("req", kv, None),
        ),
        out_specs=(P("req", kv), P("req", None, kv), P("req", None, kv)),
        check_vma=False,
    )
```

```python
import math

import jax
import jax.numpy as jnp
from jax import lax
from jax.sharding import Mesh
from jax.sharding import PartitionSpec as P

HEAD_WIDTH = 256
CORES = 2


rope_base = 1000042.0
epsilon = 1e-05


def rotate_pairs(tensor, position):
    half_size = tensor.shape[-1] // 2
    steps_float = jnp.arange(half_size, dtype=jnp.float32)
    inverse = jnp.exp(steps_float * (-2.0 * math.log(rope_base) / tensor.shape[-1]))
    angles = position[:, :, None] * inverse[None, None, :]
    cosine = jnp.cos(angles)[:, :, None, :]
    sine_part = jnp.sin(angles)[:, :, None, :]
    first_half = tensor[..., :half_size]
    second = tensor[..., half_size:]
    return jnp.concatenate(
        [first_half * cosine - second * sine_part, second * cosine + first_half * sine_part],
        axis=-1,
    )


def allowed_keys(span_length, span_size, past_size):
    key_pos = jnp.arange(past_size + span_size, dtype=jnp.int32) - past_size
    query_pos = jnp.arange(span_size, dtype=jnp.int32)
    causal = key_pos[None, :] <= query_pos[:, None]
    live_keys = key_pos[None, None, :] < span_length[:, None, None]
    return (key_pos[None, None, :] < 0) | causal[None, :, :] & live_keys


def swap(values, axis_name):
    return lax.ppermute(values, axis_name, [(0, 1), (1, 0)])


def gather_features(share):
    chip = lax.axis_index("kvy")
    core = lax.axis_index("core")
    partner = swap(share, "kvy")
    pair = jnp.where(chip == 0, jnp.stack([share, partner]), jnp.stack([partner, share]))
    other = swap(pair, "core")
    blocks = []
    for chip_block in range(2):
        for core_block in range(2):
            blocks.append(jnp.where(core == core_block, pair[chip_block], other[chip_block]))
    return jnp.concatenate(blocks, axis=1)


def gather_project(share, weights):
    chip = lax.axis_index("kvy")
    core = lax.axis_index("core")
    from_core = swap(share, "core")
    from_chip = swap(share, "kvy")
    local_pair = jnp.where(
        core == 0,
        jnp.concatenate([share, from_core], axis=1),
        jnp.concatenate([from_core, share], axis=1),
    )
    half = local_pair.shape[1]
    local_parts = tuple(
        jnp.dot(
            local_pair,
            lax.dynamic_slice_in_dim(weight, chip * half, half, 0),
            preferred_element_type=jnp.float32,
        )
        for weight in weights
    )
    from_chip, local_parts = lax.optimization_barrier((from_chip, local_parts))
    from_diagonal = swap(from_chip, "core")
    remote_pair = jnp.where(
        core == 0,
        jnp.concatenate([from_chip, from_diagonal], axis=1),
        jnp.concatenate([from_diagonal, from_chip], axis=1),
    )
    return [
        part
        + jnp.dot(
            remote_pair,
            lax.dynamic_slice_in_dim(weight, (1 - chip) * half, half, 0),
            preferred_element_type=jnp.float32,
        )
        for part, weight in zip(local_parts, weights)
    ]


def scatter_features(matrix_in, weight, link_type=None):
    chip = lax.axis_index("kvy")
    core = lax.axis_index("core")
    product = jnp.dot(matrix_in, weight, preferred_element_type=jnp.float32)
    width = product.shape[1] // (2 * CORES)

    def block(chip_block, core_block):
        start = (chip_block * CORES + core_block) * width
        return product[:, start:start + width]

    keep = jnp.stack([jnp.where(core == 0, block(k, 0), block(k, 1)) for k in range(2)])
    give = jnp.stack([jnp.where(core == 0, block(k, 1), block(k, 0)) for k in range(2)])
    chip_sum = keep + swap(give, "core")
    mine = jnp.where(chip == 0, chip_sum[0], chip_sum[1])
    theirs = jnp.where(chip == 0, chip_sum[1], chip_sum[0])
    if link_type is not None:
        theirs = theirs.astype(link_type)
    return mine + swap(theirs, "kvy").astype(jnp.float32)


def scatter_halves(matrix_in, weight, link_type):
    chip = lax.axis_index("kvy")
    core = lax.axis_index("core")
    width = weight.shape[1] // (2 * CORES)

    def columns(core_block):
        return jnp.concatenate(
            [
                lax.dynamic_slice_in_dim(weight, (chip_block * CORES + core_block) * width, width, 1)
                for chip_block in range(2)
            ],
            axis=1,
        )

    keep = jnp.dot(matrix_in, columns(core), preferred_element_type=jnp.float32)
    give = jnp.dot(matrix_in, columns(1 - core), preferred_element_type=jnp.float32)
    chip_sum = keep + swap(give, "core")
    mine = lax.dynamic_slice_in_dim(chip_sum, chip * width, width, 1)
    theirs = lax.dynamic_slice_in_dim(chip_sum, (1 - chip) * width, width, 1)
    return mine + swap(theirs.astype(link_type), "kvy").astype(jnp.float32)


def row_scale(values, gain_share):
    square_sum = jnp.sum(values * values, axis=-1, keepdims=True)
    square_sum = square_sum + swap(square_sum, "core")
    square_sum = square_sum + swap(square_sum, "kvy")
    width = values.shape[-1] * 2 * CORES
    return values * lax.rsqrt(square_sum / width + epsilon) * gain_share


def local(
    activations,
    span_length,
    offsets,
    decode_slot,
    attention_gain,
    query_weight,
    key_projection_matrix,
    value_projection_matrix,
    output_weight,
    feedforward_gain,
    gate_weight,
    up_weight,
    down_weight,
    earlier_rotated_keys,
    earlier_values,
):
    req_count = lax.axis_size("req")
    chips = lax.axis_size("kvy")
    kv_count = chips * CORES
    kv_index = lax.axis_index("kvy") * CORES + lax.axis_index("core")
    req_index = lax.axis_index("req")
    request_list = span_length.shape[0]
    total_rows, width_share = activations.shape
    span_size = total_rows // request_list
    local_kv = key_projection_matrix.shape[1] // HEAD_WIDTH
    local_q = query_weight.shape[1] // HEAD_WIDTH
    query_groups = local_q // local_kv

    past_share = earlier_rotated_keys.shape[1]
    stacked = jnp.stack([earlier_rotated_keys, earlier_values])
    stacked = stacked.reshape(2, request_list, past_share, kv_count, local_kv * HEAD_WIDTH)
    stacked = stacked.transpose(0, 3, 1, 2, 4)
    arrived = lax.all_to_all(stacked, ("kvy", "core"), split_axis=1, concat_axis=1, tiled=True)
    head_kv = arrived.transpose(0, 2, 1, 3, 4).reshape(
        2, request_list, kv_count * past_share, local_kv * HEAD_WIDTH
    )
    past_size = head_kv.shape[2]

    capacity = max(2, (request_list + req_count - 1) // req_count)
    order_ids = jnp.arange(request_list, dtype=jnp.int32)
    earlier = order_ids[None, :] < order_ids[:, None]
    own_dest = decode_slot // request_list
    same_dest = own_dest[:, None] == own_dest[None, :]
    own_rank = jnp.sum((same_dest & earlier).astype(jnp.int32), axis=1)
    buffer_place = own_dest * capacity + own_rank
    buffer_ids = jnp.arange(req_count * capacity, dtype=jnp.int32)
    matches = buffer_place[None, :] == buffer_ids[:, None]
    picked = jnp.sum(jnp.where(matches, order_ids[None, :], 0), axis=1)
    filled = jnp.any(matches, axis=1)
    lanes = local_kv * HEAD_WIDTH
    slot_code = jnp.stack([decode_slot // 16, decode_slot % 16], axis=1).astype(jnp.bfloat16)
    trailer = jnp.pad(slot_code, ((0, 0), (0, lanes - 2)))[:, None, :]
    payload = jnp.concatenate([head_kv[0], head_kv[1], trailer], axis=1)
    packed = jnp.take(payload, picked, axis=0)
    packed = jnp.where(filled[:, None, None], packed, -jnp.ones((), packed.dtype))
    packed = packed.reshape((req_count, capacity) + payload.shape[1:])
    landed = lax.all_to_all(packed, "req", split_axis=0, concat_axis=0, tiled=True)
    landed = landed.reshape((req_count * capacity,) + payload.shape[1:])
    code = landed[:, 2 * past_size, :2].astype(jnp.int32)
    landed_slots = code[:, 0] * 16 + code[:, 1]
    wanted = req_index * request_list + order_ids
    slot_hits = landed_slots[None, :] == wanted[:, None]
    entry_ids = jnp.arange(req_count * capacity, dtype=jnp.int32)
    slot_position = jnp.sum(jnp.where(slot_hits, entry_ids[None, :], 0), axis=1)
    decode_rows = jnp.take(landed, slot_position, axis=0)
    decode_kv = (decode_rows[:, :past_size], decode_rows[:, past_size:2 * past_size])

    x_whole = gather_features(activations)
    x_float = x_whole.astype(jnp.float32)
    square_sum = jnp.sum(x_float * x_float, axis=-1, keepdims=True)
    normalized_input = (
        x_float * lax.rsqrt(square_sum / x_float.shape[-1] + epsilon) * attention_gain
    ).astype(jnp.bfloat16)
    position = (
        offsets[:, None].astype(jnp.float32) + jnp.arange(span_size, dtype=jnp.float32)[None, :]
    )
    query_rows = jnp.dot(
        normalized_input, query_weight, preferred_element_type=jnp.float32
    ).reshape(request_list, span_size, local_q, HEAD_WIDTH)
    query_rows = rotate_pairs(query_rows, position).astype(jnp.bfloat16)
    fresh_keys = jnp.dot(
        normalized_input, key_projection_matrix, preferred_element_type=jnp.float32
    ).reshape(request_list, span_size, local_kv, HEAD_WIDTH)
    fresh_keys = rotate_pairs(fresh_keys, position).astype(jnp.bfloat16)
    fresh_values = (
        jnp.dot(normalized_input, value_projection_matrix, preferred_element_type=jnp.float32)
        .astype(jnp.bfloat16)
        .reshape(request_list, span_size, local_kv, HEAD_WIDTH)
    )
    combined_keys = jnp.concatenate(
        [head_kv[0].reshape(request_list, past_size, local_kv, HEAD_WIDTH), fresh_keys], axis=1
    )
    combined_values = jnp.concatenate(
        [head_kv[1].reshape(request_list, past_size, local_kv, HEAD_WIDTH), fresh_values], axis=1
    )
    grouped_queries = query_rows.reshape(
        request_list, span_size, local_kv, query_groups, HEAD_WIDTH
    )
    scores = jnp.einsum(
        "rckgd,rskd->rkgcs", grouped_queries, combined_keys, preferred_element_type=jnp.float32
    ) / math.sqrt(HEAD_WIDTH)
    allowed = allowed_keys(span_length, span_size, past_size)[:, None, None, :, :]
    scores = jnp.where(allowed, scores, -jnp.inf)
    weights = jax.nn.softmax(scores, axis=-1).astype(jnp.bfloat16)
    mixed_heads = jnp.einsum(
        "rkgcs,rskd->rckgd", weights, combined_values, preferred_element_type=jnp.float32
    )
    mixed_heads = mixed_heads.astype(jnp.bfloat16).reshape(total_rows, local_q * HEAD_WIDTH)
    head_share = scatter_features(mixed_heads, output_weight)
    residual_share = activations.astype(jnp.float32) + head_share

    gain_share = lax.dynamic_slice_in_dim(feedforward_gain, kv_index * width_share, width_share)
    normed_share = row_scale(residual_share, gain_share).astype(jnp.bfloat16)
    gate_proj, upward = gather_project(normed_share, (gate_weight, up_weight))
    hidden = (jax.nn.silu(gate_proj) * upward).astype(jnp.bfloat16)
    mlp_share = scatter_halves(hidden, down_weight, jnp.bfloat16)
    live_rows = (jnp.arange(span_size, dtype=jnp.int32)[None, :] < span_length[:, None]).reshape(
        total_rows
    )
    layer_out = jnp.where(live_rows[:, None], residual_share + mlp_share, 0.0).astype(jnp.bfloat16)
    return (layer_out, decode_kv[0], decode_kv[1])


def solution(mesh):
    req_size, kv_size = mesh.devices.shape
    split_mesh = Mesh(
        mesh.devices.reshape(req_size, kv_size // CORES, CORES), ("req", "kvy", "core")
    )
    kv = ("kvy", "core")
    return jax.shard_map(
        local,
        mesh=split_mesh,
        in_specs=(
            P("req", kv),
            P("req"),
            P("req"),
            P("req"),
            P(),
            P(None, kv),
            P(None, kv),
            P(None, kv),
            P(kv, None),
            P(),
            P(None, kv),
            P(None, kv),
            P(kv, None),
            P("req", kv, None),
            P("req", kv, None),
        ),
        out_specs=(P("req", kv), P("req", None, kv), P("req", None, kv)),
        check_vma=False,
    )
```

```python
import math

import jax
import jax.numpy as jnp
from jax import lax
from jax.sharding import Mesh
from jax.sharding import PartitionSpec as P

HEAD_WIDTH = 256
CORES = 2


rope_base = 1000042.0
epsilon = 1e-05


def rotate_pairs(tensor, position):
    half_size = tensor.shape[-1] // 2
    steps_float = jnp.arange(half_size, dtype=jnp.float32)
    inverse = jnp.exp(steps_float * (-2.0 * math.log(rope_base) / tensor.shape[-1]))
    angles = position[:, :, None] * inverse[None, None, :]
    cosine = jnp.cos(angles)[:, :, None, :]
    sine_part = jnp.sin(angles)[:, :, None, :]
    first_half = tensor[..., :half_size]
    second = tensor[..., half_size:]
    return jnp.concatenate(
        [first_half * cosine - second * sine_part, second * cosine + first_half * sine_part],
        axis=-1,
    )


def allowed_keys(span_length, span_size, past_size):
    key_pos = jnp.arange(past_size + span_size, dtype=jnp.int32) - past_size
    query_pos = jnp.arange(span_size, dtype=jnp.int32)
    causal = key_pos[None, :] <= query_pos[:, None]
    live_keys = key_pos[None, None, :] < span_length[:, None, None]
    return (key_pos[None, None, :] < 0) | causal[None, :, :] & live_keys


def swap(values, axis_name):
    return lax.ppermute(values, axis_name, [(0, 1), (1, 0)])


def gather_features(share):
    chip = lax.axis_index("kvy")
    core = lax.axis_index("core")
    partner = swap(share, "kvy")
    pair = jnp.where(chip == 0, jnp.stack([share, partner]), jnp.stack([partner, share]))
    other = swap(pair, "core")
    blocks = []
    for chip_block in range(2):
        for core_block in range(2):
            blocks.append(jnp.where(core == core_block, pair[chip_block], other[chip_block]))
    return jnp.concatenate(blocks, axis=1)


def gather_project(share, weights):
    chip = lax.axis_index("kvy")
    core = lax.axis_index("core")
    from_core = swap(share, "core")
    from_chip = swap(share, "kvy")
    local_pair = jnp.where(
        core == 0,
        jnp.concatenate([share, from_core], axis=1),
        jnp.concatenate([from_core, share], axis=1),
    )
    half = local_pair.shape[1]
    local_parts = tuple(
        jnp.dot(
            local_pair,
            lax.dynamic_slice_in_dim(weight, chip * half, half, 0),
            preferred_element_type=jnp.float32,
        )
        for weight in weights
    )
    from_chip, local_parts = lax.optimization_barrier((from_chip, local_parts))
    from_diagonal = swap(from_chip, "core")
    remote_pair = jnp.where(
        core == 0,
        jnp.concatenate([from_chip, from_diagonal], axis=1),
        jnp.concatenate([from_diagonal, from_chip], axis=1),
    )
    return [
        part
        + jnp.dot(
            remote_pair,
            lax.dynamic_slice_in_dim(weight, (1 - chip) * half, half, 0),
            preferred_element_type=jnp.float32,
        )
        for part, weight in zip(local_parts, weights)
    ]


def scatter_features(matrix_in, weight, link_type=None):
    chip = lax.axis_index("kvy")
    core = lax.axis_index("core")
    product = jnp.dot(matrix_in, weight, preferred_element_type=jnp.float32)
    width = product.shape[1] // (2 * CORES)

    def block(chip_block, core_block):
        start = (chip_block * CORES + core_block) * width
        return product[:, start:start + width]

    keep = jnp.stack([jnp.where(core == 0, block(k, 0), block(k, 1)) for k in range(2)])
    give = jnp.stack([jnp.where(core == 0, block(k, 1), block(k, 0)) for k in range(2)])
    chip_sum = keep + swap(give, "core")
    mine = jnp.where(chip == 0, chip_sum[0], chip_sum[1])
    theirs = jnp.where(chip == 0, chip_sum[1], chip_sum[0])
    if link_type is not None:
        theirs = theirs.astype(link_type)
    return mine + swap(theirs, "kvy").astype(jnp.float32)


def project_heads(mixed, weight, weight_far):
    chip = lax.axis_index("kvy")
    core = lax.axis_index("core")
    half = weight_far.shape[1]
    width = half // CORES
    mixed_far = swap(mixed, "kvy")
    weight_near = lax.dynamic_slice_in_dim(weight, chip * half, half, 1)
    chip_sum = jnp.dot(mixed, weight_near, preferred_element_type=jnp.float32) + jnp.dot(
        mixed_far, weight_far, preferred_element_type=jnp.float32
    )
    keep = lax.dynamic_slice_in_dim(chip_sum, core * width, width, 1)
    give = lax.dynamic_slice_in_dim(chip_sum, (1 - core) * width, width, 1)
    return keep + swap(give, "core")


def row_scale(values, gain_share):
    square_sum = jnp.sum(values * values, axis=-1, keepdims=True)
    square_sum = square_sum + swap(square_sum, "core")
    square_sum = square_sum + swap(square_sum, "kvy")
    width = values.shape[-1] * 2 * CORES
    return values * lax.rsqrt(square_sum / width + epsilon) * gain_share


def local(
    activations,
    span_length,
    offsets,
    decode_slot,
    attention_gain,
    query_weight,
    key_projection_matrix,
    value_projection_matrix,
    output_weight,
    feedforward_gain,
    gate_weight,
    up_weight,
    down_weight,
    earlier_rotated_keys,
    earlier_values,
):
    req_count = lax.axis_size("req")
    chips = lax.axis_size("kvy")
    kv_count = chips * CORES
    kv_index = lax.axis_index("kvy") * CORES + lax.axis_index("core")
    req_index = lax.axis_index("req")
    request_list = span_length.shape[0]
    total_rows, width_share = activations.shape
    span_size = total_rows // request_list
    local_kv = key_projection_matrix.shape[1] // HEAD_WIDTH
    local_q = query_weight.shape[1] // HEAD_WIDTH
    query_groups = local_q // local_kv

    past_share = earlier_rotated_keys.shape[1]
    stacked = jnp.stack([earlier_rotated_keys, earlier_values])
    stacked = stacked.reshape(2, request_list, past_share, kv_count, local_kv * HEAD_WIDTH)
    stacked = stacked.transpose(0, 3, 1, 2, 4)
    arrived = lax.all_to_all(stacked, ("kvy", "core"), split_axis=1, concat_axis=1, tiled=True)
    head_kv = arrived.transpose(0, 2, 1, 3, 4).reshape(
        2, request_list, kv_count * past_share, local_kv * HEAD_WIDTH
    )
    past_size = head_kv.shape[2]

    capacity = max(2, (request_list + req_count - 1) // req_count)
    order_ids = jnp.arange(request_list, dtype=jnp.int32)
    earlier = order_ids[None, :] < order_ids[:, None]
    own_dest = decode_slot // request_list
    same_dest = own_dest[:, None] == own_dest[None, :]
    own_rank = jnp.sum((same_dest & earlier).astype(jnp.int32), axis=1)
    buffer_place = own_dest * capacity + own_rank
    buffer_ids = jnp.arange(req_count * capacity, dtype=jnp.int32)
    matches = buffer_place[None, :] == buffer_ids[:, None]
    picked = jnp.sum(jnp.where(matches, order_ids[None, :], 0), axis=1)
    filled = jnp.any(matches, axis=1)
    lanes = local_kv * HEAD_WIDTH
    slot_code = jnp.stack([decode_slot // 16, decode_slot % 16], axis=1).astype(jnp.bfloat16)
    trailer = jnp.pad(slot_code, ((0, 0), (0, lanes - 2)))[:, None, :]
    payload = jnp.concatenate([head_kv[0], head_kv[1], trailer], axis=1)
    packed = jnp.take(payload, picked, axis=0)
    packed = jnp.where(filled[:, None, None], packed, -jnp.ones((), packed.dtype))
    packed = packed.reshape((req_count, capacity) + payload.shape[1:])
    landed = lax.all_to_all(packed, "req", split_axis=0, concat_axis=0, tiled=True)
    landed = landed.reshape((req_count * capacity,) + payload.shape[1:])
    code = landed[:, 2 * past_size, :2].astype(jnp.int32)
    landed_slots = code[:, 0] * 16 + code[:, 1]
    wanted = req_index * request_list + order_ids
    slot_hits = landed_slots[None, :] == wanted[:, None]
    entry_ids = jnp.arange(req_count * capacity, dtype=jnp.int32)
    slot_position = jnp.sum(jnp.where(slot_hits, entry_ids[None, :], 0), axis=1)
    decode_rows = jnp.take(landed, slot_position, axis=0)
    decode_kv = (decode_rows[:, :past_size], decode_rows[:, past_size:2 * past_size])

    x_whole = gather_features(activations)
    chip_cols = output_weight.shape[1] // chips
    far_cols = lax.dynamic_slice_in_dim(
        output_weight, (1 - lax.axis_index("kvy")) * chip_cols, chip_cols, 1
    )
    far_cols, x_whole = lax.optimization_barrier((far_cols, x_whole))
    weight_far = swap(far_cols, "kvy")
    x_float = x_whole.astype(jnp.float32)
    square_sum = jnp.sum(x_float * x_float, axis=-1, keepdims=True)
    normalized_input = (
        x_float * lax.rsqrt(square_sum / x_float.shape[-1] + epsilon) * attention_gain
    ).astype(jnp.bfloat16)
    position = (
        offsets[:, None].astype(jnp.float32) + jnp.arange(span_size, dtype=jnp.float32)[None, :]
    )
    query_rows = jnp.dot(
        normalized_input, query_weight, preferred_element_type=jnp.float32
    ).reshape(request_list, span_size, local_q, HEAD_WIDTH)
    query_rows = rotate_pairs(query_rows, position).astype(jnp.bfloat16)
    fresh_keys = jnp.dot(
        normalized_input, key_projection_matrix, preferred_element_type=jnp.float32
    ).reshape(request_list, span_size, local_kv, HEAD_WIDTH)
    fresh_keys = rotate_pairs(fresh_keys, position).astype(jnp.bfloat16)
    fresh_values = (
        jnp.dot(normalized_input, value_projection_matrix, preferred_element_type=jnp.float32)
        .astype(jnp.bfloat16)
        .reshape(request_list, span_size, local_kv, HEAD_WIDTH)
    )
    combined_keys = jnp.concatenate(
        [head_kv[0].reshape(request_list, past_size, local_kv, HEAD_WIDTH), fresh_keys], axis=1
    )
    combined_values = jnp.concatenate(
        [head_kv[1].reshape(request_list, past_size, local_kv, HEAD_WIDTH), fresh_values], axis=1
    )
    grouped_queries = query_rows.reshape(
        request_list, span_size, local_kv, query_groups, HEAD_WIDTH
    )
    scores = jnp.einsum(
        "rckgd,rskd->rkgcs", grouped_queries, combined_keys, preferred_element_type=jnp.float32
    ) / math.sqrt(HEAD_WIDTH)
    allowed = allowed_keys(span_length, span_size, past_size)[:, None, None, :, :]
    scores = jnp.where(allowed, scores, -jnp.inf)
    weights = jax.nn.softmax(scores, axis=-1).astype(jnp.bfloat16)
    mixed_heads = jnp.einsum(
        "rkgcs,rskd->rckgd", weights, combined_values, preferred_element_type=jnp.float32
    )
    mixed_heads = mixed_heads.astype(jnp.bfloat16).reshape(total_rows, local_q * HEAD_WIDTH)
    head_share = project_heads(mixed_heads, output_weight, weight_far)
    residual_share = activations.astype(jnp.float32) + head_share

    gain_share = lax.dynamic_slice_in_dim(feedforward_gain, kv_index * width_share, width_share)
    normed_share = row_scale(residual_share, gain_share).astype(jnp.bfloat16)
    gate_proj, upward = gather_project(normed_share, (gate_weight, up_weight))
    hidden = (jax.nn.silu(gate_proj) * upward).astype(jnp.bfloat16)
    mlp_share = scatter_features(hidden, down_weight, jnp.bfloat16)
    live_rows = (jnp.arange(span_size, dtype=jnp.int32)[None, :] < span_length[:, None]).reshape(
        total_rows
    )
    layer_out = jnp.where(live_rows[:, None], residual_share + mlp_share, 0.0).astype(jnp.bfloat16)
    return (layer_out, decode_kv[0], decode_kv[1])


def solution(mesh):
    req_size, kv_size = mesh.devices.shape
    split_mesh = Mesh(
        mesh.devices.reshape(req_size, kv_size // CORES, CORES), ("req", "kvy", "core")
    )
    kv = ("kvy", "core")
    return jax.shard_map(
        local,
        mesh=split_mesh,
        in_specs=(
            P("req", kv),
            P("req"),
            P("req"),
            P("req"),
            P(),
            P(None, kv),
            P(None, kv),
            P(None, kv),
            P(kv, None),
            P(),
            P(None, kv),
            P(None, kv),
            P(kv, None),
            P("req", kv, None),
            P("req", kv, None),
        ),
        out_specs=(P("req", kv), P("req", None, kv), P("req", None, kv)),
        check_vma=False,
    )
```

```python
import math

import jax
import jax.numpy as jnp
from jax import lax
from jax.sharding import Mesh
from jax.sharding import PartitionSpec as P

HEAD_WIDTH = 256
CORES = 2


rope_base = 1000042.0
epsilon = 1e-05


def rotate_pairs(tensor, position):
    half_size = tensor.shape[-1] // 2
    steps_float = jnp.arange(half_size, dtype=jnp.float32)
    inverse = jnp.exp(steps_float * (-2.0 * math.log(rope_base) / tensor.shape[-1]))
    angles = position[:, :, None] * inverse[None, None, :]
    cosine = jnp.cos(angles)[:, :, None, :]
    sine_part = jnp.sin(angles)[:, :, None, :]
    first_half = tensor[..., :half_size]
    second = tensor[..., half_size:]
    return jnp.concatenate(
        [first_half * cosine - second * sine_part, second * cosine + first_half * sine_part],
        axis=-1,
    )


def allowed_keys(span_length, span_size, past_size):
    key_pos = jnp.arange(past_size + span_size, dtype=jnp.int32) - past_size
    query_pos = jnp.arange(span_size, dtype=jnp.int32)
    causal = key_pos[None, :] <= query_pos[:, None]
    live_keys = key_pos[None, None, :] < span_length[:, None, None]
    return (key_pos[None, None, :] < 0) | causal[None, :, :] & live_keys


def swap(values, axis_name):
    return lax.ppermute(values, axis_name, [(0, 1), (1, 0)])


def gather_features(share):
    chip = lax.axis_index("kvy")
    core = lax.axis_index("core")
    partner = swap(share, "kvy")
    pair = jnp.where(chip == 0, jnp.stack([share, partner]), jnp.stack([partner, share]))
    other = swap(pair, "core")
    blocks = []
    for chip_block in range(2):
        for core_block in range(2):
            blocks.append(jnp.where(core == core_block, pair[chip_block], other[chip_block]))
    return jnp.concatenate(blocks, axis=1)


def gather_project(share, weights):
    chip = lax.axis_index("kvy")
    core = lax.axis_index("core")
    from_core = swap(share, "core")
    from_chip = swap(share, "kvy")
    local_pair = jnp.where(
        core == 0,
        jnp.concatenate([share, from_core], axis=1),
        jnp.concatenate([from_core, share], axis=1),
    )
    half = local_pair.shape[1]
    local_parts = tuple(
        jnp.dot(
            local_pair,
            lax.dynamic_slice_in_dim(weight, chip * half, half, 0),
            preferred_element_type=jnp.float32,
        )
        for weight in weights
    )
    from_chip, local_parts = lax.optimization_barrier((from_chip, local_parts))
    from_diagonal = swap(from_chip, "core")
    remote_pair = jnp.where(
        core == 0,
        jnp.concatenate([from_chip, from_diagonal], axis=1),
        jnp.concatenate([from_diagonal, from_chip], axis=1),
    )
    return [
        part
        + jnp.dot(
            remote_pair,
            lax.dynamic_slice_in_dim(weight, (1 - chip) * half, half, 0),
            preferred_element_type=jnp.float32,
        )
        for part, weight in zip(local_parts, weights)
    ]


def scatter_features(matrix_in, weight, link_type=None):
    chip = lax.axis_index("kvy")
    core = lax.axis_index("core")
    product = jnp.dot(matrix_in, weight, preferred_element_type=jnp.float32)
    width = product.shape[1] // (2 * CORES)

    def block(chip_block, core_block):
        start = (chip_block * CORES + core_block) * width
        return product[:, start:start + width]

    keep = jnp.stack([jnp.where(core == 0, block(k, 0), block(k, 1)) for k in range(2)])
    give = jnp.stack([jnp.where(core == 0, block(k, 1), block(k, 0)) for k in range(2)])
    chip_sum = keep + swap(give, "core")
    mine = jnp.where(chip == 0, chip_sum[0], chip_sum[1])
    theirs = jnp.where(chip == 0, chip_sum[1], chip_sum[0])
    if link_type is not None:
        theirs = theirs.astype(link_type)
    return mine + swap(theirs, "kvy").astype(jnp.float32)


def project_heads(mixed, weight, weight_far):
    chip = lax.axis_index("kvy")
    core = lax.axis_index("core")
    half = weight_far.shape[1]
    width = half // CORES
    mixed_far = swap(mixed, "kvy")
    weight_near = lax.dynamic_slice_in_dim(weight, chip * half, half, 1)
    chip_sum = jnp.dot(mixed, weight_near, preferred_element_type=jnp.float32) + jnp.dot(
        mixed_far, weight_far, preferred_element_type=jnp.float32
    )
    keep = lax.dynamic_slice_in_dim(chip_sum, core * width, width, 1)
    give = lax.dynamic_slice_in_dim(chip_sum, (1 - core) * width, width, 1)
    return keep + swap(give, "core")


def row_scale(values, gain_share):
    square_sum = jnp.sum(values * values, axis=-1, keepdims=True)
    square_sum = square_sum + swap(square_sum, "core")
    square_sum = square_sum + swap(square_sum, "kvy")
    width = values.shape[-1] * 2 * CORES
    return values * lax.rsqrt(square_sum / width + epsilon) * gain_share


def local(
    activations,
    span_length,
    offsets,
    decode_slot,
    attention_gain,
    query_weight,
    key_projection_matrix,
    value_projection_matrix,
    output_weight,
    feedforward_gain,
    gate_weight,
    up_weight,
    down_weight,
    earlier_rotated_keys,
    earlier_values,
):
    req_count = lax.axis_size("req")
    chips = lax.axis_size("kvy")
    kv_count = chips * CORES
    kv_index = lax.axis_index("kvy") * CORES + lax.axis_index("core")
    req_index = lax.axis_index("req")
    request_list = span_length.shape[0]
    total_rows, width_share = activations.shape
    span_size = total_rows // request_list
    local_kv = key_projection_matrix.shape[1] // HEAD_WIDTH
    local_q = query_weight.shape[1] // HEAD_WIDTH
    query_groups = local_q // local_kv

    past_share = earlier_rotated_keys.shape[1]
    stacked = jnp.stack([earlier_rotated_keys, earlier_values])
    stacked = stacked.reshape(2, request_list, past_share, kv_count, local_kv * HEAD_WIDTH)
    stacked = stacked.transpose(0, 3, 1, 2, 4)
    arrived = lax.all_to_all(stacked, ("kvy", "core"), split_axis=1, concat_axis=1, tiled=True)
    head_kv = arrived.transpose(0, 2, 1, 3, 4).reshape(
        2, request_list, kv_count * past_share, local_kv * HEAD_WIDTH
    )
    past_size = head_kv.shape[2]

    capacity = max(2, (request_list + req_count - 1) // req_count)
    order_ids = jnp.arange(request_list, dtype=jnp.int32)
    earlier = order_ids[None, :] < order_ids[:, None]
    own_dest = decode_slot // request_list
    same_dest = own_dest[:, None] == own_dest[None, :]
    own_rank = jnp.sum((same_dest & earlier).astype(jnp.int32), axis=1)
    buffer_place = own_dest * capacity + own_rank
    buffer_ids = jnp.arange(req_count * capacity, dtype=jnp.int32)
    matches = buffer_place[None, :] == buffer_ids[:, None]
    picked = jnp.sum(jnp.where(matches, order_ids[None, :], 0), axis=1)
    filled = jnp.any(matches, axis=1)
    lanes = local_kv * HEAD_WIDTH
    slot_code = jnp.stack([decode_slot // 16, decode_slot % 16], axis=1).astype(jnp.bfloat16)
    trailer = jnp.pad(slot_code, ((0, 0), (0, lanes - 2)))[:, None, :]
    payload = jnp.concatenate([head_kv[0], head_kv[1], trailer], axis=1)
    packed = jnp.take(payload, picked, axis=0)
    packed = jnp.where(filled[:, None, None], packed, -jnp.ones((), packed.dtype))
    packed = packed.reshape((req_count, capacity) + payload.shape[1:])
    landed = lax.all_to_all(packed, "req", split_axis=0, concat_axis=0, tiled=True)
    landed = landed.reshape((req_count * capacity,) + payload.shape[1:])
    code = landed[:, 2 * past_size, :2].astype(jnp.int32)
    landed_slots = code[:, 0] * 16 + code[:, 1]
    wanted = req_index * request_list + order_ids
    slot_hits = landed_slots[None, :] == wanted[:, None]
    entry_ids = jnp.arange(req_count * capacity, dtype=jnp.int32)
    slot_position = jnp.sum(jnp.where(slot_hits, entry_ids[None, :], 0), axis=1)
    decode_rows = jnp.take(landed, slot_position, axis=0)
    decode_kv = (decode_rows[:, :past_size], decode_rows[:, past_size:2 * past_size])

    x_whole = gather_features(activations)
    chip_cols = output_weight.shape[1] // chips
    far_cols = lax.dynamic_slice_in_dim(
        output_weight, (1 - lax.axis_index("kvy")) * chip_cols, chip_cols, 1
    )
    weight_far = swap(far_cols, "kvy")
    x_float = x_whole.astype(jnp.float32)
    square_sum = jnp.sum(x_float * x_float, axis=-1, keepdims=True)
    normalized_input = (
        x_float * lax.rsqrt(square_sum / x_float.shape[-1] + epsilon) * attention_gain
    ).astype(jnp.bfloat16)
    position = (
        offsets[:, None].astype(jnp.float32) + jnp.arange(span_size, dtype=jnp.float32)[None, :]
    )
    query_rows = jnp.dot(
        normalized_input, query_weight, preferred_element_type=jnp.float32
    ).reshape(request_list, span_size, local_q, HEAD_WIDTH)
    query_rows = rotate_pairs(query_rows, position).astype(jnp.bfloat16)
    fresh_keys = jnp.dot(
        normalized_input, key_projection_matrix, preferred_element_type=jnp.float32
    ).reshape(request_list, span_size, local_kv, HEAD_WIDTH)
    fresh_keys = rotate_pairs(fresh_keys, position).astype(jnp.bfloat16)
    fresh_values = (
        jnp.dot(normalized_input, value_projection_matrix, preferred_element_type=jnp.float32)
        .astype(jnp.bfloat16)
        .reshape(request_list, span_size, local_kv, HEAD_WIDTH)
    )
    combined_keys = jnp.concatenate(
        [head_kv[0].reshape(request_list, past_size, local_kv, HEAD_WIDTH), fresh_keys], axis=1
    )
    combined_values = jnp.concatenate(
        [head_kv[1].reshape(request_list, past_size, local_kv, HEAD_WIDTH), fresh_values], axis=1
    )
    grouped_queries = query_rows.reshape(
        request_list, span_size, local_kv, query_groups, HEAD_WIDTH
    )
    scores = jnp.einsum(
        "rckgd,rskd->rkgcs", grouped_queries, combined_keys, preferred_element_type=jnp.float32
    ) / math.sqrt(HEAD_WIDTH)
    allowed = allowed_keys(span_length, span_size, past_size)[:, None, None, :, :]
    scores = jnp.where(allowed, scores, -jnp.inf)
    weights = jax.nn.softmax(scores, axis=-1).astype(jnp.bfloat16)
    mixed_heads = jnp.einsum(
        "rkgcs,rskd->rckgd", weights, combined_values, preferred_element_type=jnp.float32
    )
    mixed_heads = mixed_heads.astype(jnp.bfloat16).reshape(total_rows, local_q * HEAD_WIDTH)
    head_share = project_heads(mixed_heads, output_weight, weight_far)
    residual_share = activations.astype(jnp.float32) + head_share

    gain_share = lax.dynamic_slice_in_dim(feedforward_gain, kv_index * width_share, width_share)
    normed_share = row_scale(residual_share, gain_share).astype(jnp.bfloat16)
    gate_proj, upward = gather_project(normed_share, (gate_weight, up_weight))
    hidden = (jax.nn.silu(gate_proj) * upward).astype(jnp.bfloat16)
    mlp_share = scatter_features(hidden, down_weight, jnp.bfloat16)
    live_rows = (jnp.arange(span_size, dtype=jnp.int32)[None, :] < span_length[:, None]).reshape(
        total_rows
    )
    layer_out = jnp.where(live_rows[:, None], residual_share + mlp_share, 0.0).astype(jnp.bfloat16)
    return (layer_out, decode_kv[0], decode_kv[1])


def solution(mesh):
    req_size, kv_size = mesh.devices.shape
    split_mesh = Mesh(
        mesh.devices.reshape(req_size, kv_size // CORES, CORES), ("req", "kvy", "core")
    )
    kv = ("kvy", "core")
    return jax.shard_map(
        local,
        mesh=split_mesh,
        in_specs=(
            P("req", kv),
            P("req"),
            P("req"),
            P("req"),
            P(),
            P(None, kv),
            P(None, kv),
            P(None, kv),
            P(kv, None),
            P(),
            P(None, kv),
            P(None, kv),
            P(kv, None),
            P("req", kv, None),
            P("req", kv, None),
        ),
        out_specs=(P("req", kv), P("req", None, kv), P("req", None, kv)),
        check_vma=False,
    )
```

```python
import math

import jax
import jax.numpy as jnp
from jax import lax
from jax.sharding import Mesh
from jax.sharding import PartitionSpec as P

HEAD_WIDTH = 256
CORES = 2


rope_base = 1000042.0
epsilon = 1e-05


def rotate_pairs(tensor, position):
    half_size = tensor.shape[-1] // 2
    steps_float = jnp.arange(half_size, dtype=jnp.float32)
    inverse = jnp.exp(steps_float * (-2.0 * math.log(rope_base) / tensor.shape[-1]))
    angles = position[:, :, None] * inverse[None, None, :]
    cosine = jnp.cos(angles)[:, :, None, :]
    sine_part = jnp.sin(angles)[:, :, None, :]
    first_half = tensor[..., :half_size]
    second = tensor[..., half_size:]
    return jnp.concatenate(
        [first_half * cosine - second * sine_part, second * cosine + first_half * sine_part],
        axis=-1,
    )


def allowed_keys(span_length, span_size, past_size):
    key_pos = jnp.arange(past_size + span_size, dtype=jnp.int32) - past_size
    query_pos = jnp.arange(span_size, dtype=jnp.int32)
    causal = key_pos[None, :] <= query_pos[:, None]
    live_keys = key_pos[None, None, :] < span_length[:, None, None]
    return (key_pos[None, None, :] < 0) | causal[None, :, :] & live_keys


def swap(values, axis_name):
    return lax.ppermute(values, axis_name, [(0, 1), (1, 0)])


def gather_features(share):
    chip = lax.axis_index("kvy")
    core = lax.axis_index("core")
    partner = swap(share, "kvy")
    pair = jnp.where(chip == 0, jnp.stack([share, partner]), jnp.stack([partner, share]))
    other = swap(pair, "core")
    blocks = []
    for chip_block in range(2):
        for core_block in range(2):
            blocks.append(jnp.where(core == core_block, pair[chip_block], other[chip_block]))
    return jnp.concatenate(blocks, axis=1)


def gather_project(share, weights):
    chip = lax.axis_index("kvy")
    core = lax.axis_index("core")
    from_core = swap(share, "core")
    from_chip = swap(share, "kvy")
    local_pair = jnp.where(
        core == 0,
        jnp.concatenate([share, from_core], axis=1),
        jnp.concatenate([from_core, share], axis=1),
    )
    half = local_pair.shape[1]
    local_parts = tuple(
        jnp.dot(
            local_pair,
            lax.dynamic_slice_in_dim(weight, chip * half, half, 0),
            preferred_element_type=jnp.float32,
        )
        for weight in weights
    )
    from_chip, local_parts = lax.optimization_barrier((from_chip, local_parts))
    from_diagonal = swap(from_chip, "core")
    remote_pair = jnp.where(
        core == 0,
        jnp.concatenate([from_chip, from_diagonal], axis=1),
        jnp.concatenate([from_diagonal, from_chip], axis=1),
    )
    return [
        part
        + jnp.dot(
            remote_pair,
            lax.dynamic_slice_in_dim(weight, (1 - chip) * half, half, 0),
            preferred_element_type=jnp.float32,
        )
        for part, weight in zip(local_parts, weights)
    ]


def scatter_features(matrix_in, weight, link_type=None):
    chip = lax.axis_index("kvy")
    core = lax.axis_index("core")
    product = jnp.dot(matrix_in, weight, preferred_element_type=jnp.float32)
    width = product.shape[1] // (2 * CORES)

    def block(chip_block, core_block):
        start = (chip_block * CORES + core_block) * width
        return product[:, start:start + width]

    keep = jnp.stack([jnp.where(core == 0, block(k, 0), block(k, 1)) for k in range(2)])
    give = jnp.stack([jnp.where(core == 0, block(k, 1), block(k, 0)) for k in range(2)])
    chip_sum = keep + swap(give, "core")
    mine = jnp.where(chip == 0, chip_sum[0], chip_sum[1])
    theirs = jnp.where(chip == 0, chip_sum[1], chip_sum[0])
    if link_type is not None:
        theirs = theirs.astype(link_type)
    return mine + swap(theirs, "kvy").astype(jnp.float32)


def project_heads(mixed, weight, weight_far):
    chip = lax.axis_index("kvy")
    core = lax.axis_index("core")
    half = weight_far.shape[1]
    width = half // CORES
    mixed_far = swap(mixed, "kvy")
    weight_near = lax.dynamic_slice_in_dim(weight, chip * half, half, 1)
    chip_sum = jnp.dot(mixed, weight_near, preferred_element_type=jnp.float32) + jnp.dot(
        mixed_far, weight_far, preferred_element_type=jnp.float32
    )
    keep = lax.dynamic_slice_in_dim(chip_sum, core * width, width, 1)
    give = lax.dynamic_slice_in_dim(chip_sum, (1 - core) * width, width, 1)
    return keep + swap(give, "core")


def row_scale(values, gain_share):
    square_sum = jnp.sum(values * values, axis=-1, keepdims=True)
    square_sum = square_sum + swap(square_sum, "core")
    square_sum = square_sum + swap(square_sum, "kvy")
    width = values.shape[-1] * 2 * CORES
    return values * lax.rsqrt(square_sum / width + epsilon) * gain_share


def local(
    activations,
    span_length,
    offsets,
    decode_slot,
    attention_gain,
    query_weight,
    key_projection_matrix,
    value_projection_matrix,
    output_weight,
    feedforward_gain,
    gate_weight,
    up_weight,
    down_weight,
    earlier_rotated_keys,
    earlier_values,
):
    req_count = lax.axis_size("req")
    chips = lax.axis_size("kvy")
    kv_count = chips * CORES
    kv_index = lax.axis_index("kvy") * CORES + lax.axis_index("core")
    req_index = lax.axis_index("req")
    request_list = span_length.shape[0]
    total_rows, width_share = activations.shape
    span_size = total_rows // request_list
    local_kv = key_projection_matrix.shape[1] // HEAD_WIDTH
    local_q = query_weight.shape[1] // HEAD_WIDTH
    query_groups = local_q // local_kv

    past_share = earlier_rotated_keys.shape[1]
    stacked = jnp.stack([earlier_rotated_keys, earlier_values])
    stacked = stacked.reshape(2, request_list, past_share, kv_count, local_kv * HEAD_WIDTH)

    def chunk_for(target):
        return lax.dynamic_index_in_dim(stacked, target, 3, keepdims=False)

    diagonal = [(source, kv_count - 1 - source) for source in range(kv_count)]
    pieces = {
        0: chunk_for(kv_index),
        1: swap(chunk_for(kv_index ^ 1), "core"),
        2: swap(chunk_for(kv_index ^ 2), "kvy"),
        3: lax.ppermute(chunk_for(kv_index ^ 3), ("kvy", "core"), diagonal),
    }
    blocks = []
    for source in range(kv_count):
        relation = source ^ kv_index
        block = pieces[3]
        for known in (2, 1, 0):
            block = jnp.where(relation == known, pieces[known], block)
        blocks.append(block)
    head_kv = jnp.concatenate(blocks, axis=2)
    past_size = head_kv.shape[2]

    capacity = max(2, (request_list + req_count - 1) // req_count)
    order_ids = jnp.arange(request_list, dtype=jnp.int32)
    earlier = order_ids[None, :] < order_ids[:, None]
    own_dest = decode_slot // request_list
    same_dest = own_dest[:, None] == own_dest[None, :]
    own_rank = jnp.sum((same_dest & earlier).astype(jnp.int32), axis=1)
    buffer_place = own_dest * capacity + own_rank
    buffer_ids = jnp.arange(req_count * capacity, dtype=jnp.int32)
    matches = buffer_place[None, :] == buffer_ids[:, None]
    picked = jnp.sum(jnp.where(matches, order_ids[None, :], 0), axis=1)
    filled = jnp.any(matches, axis=1)
    lanes = local_kv * HEAD_WIDTH
    slot_code = jnp.stack([decode_slot // 16, decode_slot % 16], axis=1).astype(jnp.bfloat16)
    trailer = jnp.pad(slot_code, ((0, 0), (0, lanes - 2)))[:, None, :]
    payload = jnp.concatenate([head_kv[0], head_kv[1], trailer], axis=1)
    packed = jnp.take(payload, picked, axis=0)
    packed = jnp.where(filled[:, None, None], packed, -jnp.ones((), packed.dtype))
    packed = packed.reshape((req_count, capacity) + payload.shape[1:])
    landed = lax.all_to_all(packed, "req", split_axis=0, concat_axis=0, tiled=True)
    landed = landed.reshape((req_count * capacity,) + payload.shape[1:])
    code = landed[:, 2 * past_size, :2].astype(jnp.int32)
    landed_slots = code[:, 0] * 16 + code[:, 1]
    wanted = req_index * request_list + order_ids
    slot_hits = landed_slots[None, :] == wanted[:, None]
    entry_ids = jnp.arange(req_count * capacity, dtype=jnp.int32)
    slot_position = jnp.sum(jnp.where(slot_hits, entry_ids[None, :], 0), axis=1)
    decode_rows = jnp.take(landed, slot_position, axis=0)
    decode_kv = (decode_rows[:, :past_size], decode_rows[:, past_size:2 * past_size])

    x_whole = gather_features(activations)
    chip_cols = output_weight.shape[1] // chips
    far_cols = lax.dynamic_slice_in_dim(
        output_weight, (1 - lax.axis_index("kvy")) * chip_cols, chip_cols, 1
    )
    weight_far = swap(far_cols, "kvy")
    x_float = x_whole.astype(jnp.float32)
    square_sum = jnp.sum(x_float * x_float, axis=-1, keepdims=True)
    normalized_input = (
        x_float * lax.rsqrt(square_sum / x_float.shape[-1] + epsilon) * attention_gain
    ).astype(jnp.bfloat16)
    position = (
        offsets[:, None].astype(jnp.float32) + jnp.arange(span_size, dtype=jnp.float32)[None, :]
    )
    query_rows = jnp.dot(
        normalized_input, query_weight, preferred_element_type=jnp.float32
    ).reshape(request_list, span_size, local_q, HEAD_WIDTH)
    query_rows = rotate_pairs(query_rows, position).astype(jnp.bfloat16)
    fresh_keys = jnp.dot(
        normalized_input, key_projection_matrix, preferred_element_type=jnp.float32
    ).reshape(request_list, span_size, local_kv, HEAD_WIDTH)
    fresh_keys = rotate_pairs(fresh_keys, position).astype(jnp.bfloat16)
    fresh_values = (
        jnp.dot(normalized_input, value_projection_matrix, preferred_element_type=jnp.float32)
        .astype(jnp.bfloat16)
        .reshape(request_list, span_size, local_kv, HEAD_WIDTH)
    )
    combined_keys = jnp.concatenate(
        [head_kv[0].reshape(request_list, past_size, local_kv, HEAD_WIDTH), fresh_keys], axis=1
    )
    combined_values = jnp.concatenate(
        [head_kv[1].reshape(request_list, past_size, local_kv, HEAD_WIDTH), fresh_values], axis=1
    )
    grouped_queries = query_rows.reshape(
        request_list, span_size, local_kv, query_groups, HEAD_WIDTH
    )
    scores = jnp.einsum(
        "rckgd,rskd->rkgcs", grouped_queries, combined_keys, preferred_element_type=jnp.float32
    ) / math.sqrt(HEAD_WIDTH)
    allowed = allowed_keys(span_length, span_size, past_size)[:, None, None, :, :]
    scores = jnp.where(allowed, scores, -jnp.inf)
    weights = jax.nn.softmax(scores, axis=-1).astype(jnp.bfloat16)
    mixed_heads = jnp.einsum(
        "rkgcs,rskd->rckgd", weights, combined_values, preferred_element_type=jnp.float32
    )
    mixed_heads = mixed_heads.astype(jnp.bfloat16).reshape(total_rows, local_q * HEAD_WIDTH)
    head_share = project_heads(mixed_heads, output_weight, weight_far)
    residual_share = activations.astype(jnp.float32) + head_share

    gain_share = lax.dynamic_slice_in_dim(feedforward_gain, kv_index * width_share, width_share)
    normed_share = row_scale(residual_share, gain_share).astype(jnp.bfloat16)
    gate_proj, upward = gather_project(normed_share, (gate_weight, up_weight))
    hidden = (jax.nn.silu(gate_proj) * upward).astype(jnp.bfloat16)
    mlp_share = scatter_features(hidden, down_weight, jnp.bfloat16)
    live_rows = (jnp.arange(span_size, dtype=jnp.int32)[None, :] < span_length[:, None]).reshape(
        total_rows
    )
    layer_out = jnp.where(live_rows[:, None], residual_share + mlp_share, 0.0).astype(jnp.bfloat16)
    return (layer_out, decode_kv[0], decode_kv[1])


def solution(mesh):
    req_size, kv_size = mesh.devices.shape
    split_mesh = Mesh(
        mesh.devices.reshape(req_size, kv_size // CORES, CORES), ("req", "kvy", "core")
    )
    kv = ("kvy", "core")
    return jax.shard_map(
        local,
        mesh=split_mesh,
        in_specs=(
            P("req", kv),
            P("req"),
            P("req"),
            P("req"),
            P(),
            P(None, kv),
            P(None, kv),
            P(None, kv),
            P(kv, None),
            P(),
            P(None, kv),
            P(None, kv),
            P(kv, None),
            P("req", kv, None),
            P("req", kv, None),
        ),
        out_specs=(P("req", kv), P("req", None, kv), P("req", None, kv)),
        check_vma=False,
    )
```

```python
import math

import jax
import jax.numpy as jnp
from jax import lax
from jax.sharding import Mesh
from jax.sharding import PartitionSpec as P

HEAD_WIDTH = 256
CORES = 2


rope_base = 1000042.0
epsilon = 1e-05


def rotate_pairs(tensor, position):
    half_size = tensor.shape[-1] // 2
    steps_float = jnp.arange(half_size, dtype=jnp.float32)
    inverse = jnp.exp(steps_float * (-2.0 * math.log(rope_base) / tensor.shape[-1]))
    angles = position[:, :, None] * inverse[None, None, :]
    cosine = jnp.cos(angles)[:, :, None, :]
    sine_part = jnp.sin(angles)[:, :, None, :]
    first_half = tensor[..., :half_size]
    second = tensor[..., half_size:]
    return jnp.concatenate(
        [first_half * cosine - second * sine_part, second * cosine + first_half * sine_part],
        axis=-1,
    )


def allowed_keys(span_length, span_size, past_size):
    key_pos = jnp.arange(past_size + span_size, dtype=jnp.int32) - past_size
    query_pos = jnp.arange(span_size, dtype=jnp.int32)
    causal = key_pos[None, :] <= query_pos[:, None]
    live_keys = key_pos[None, None, :] < span_length[:, None, None]
    return (key_pos[None, None, :] < 0) | causal[None, :, :] & live_keys


def swap(values, axis_name):
    return lax.ppermute(values, axis_name, [(0, 1), (1, 0)])


def gather_features(share):
    chip = lax.axis_index("kvy")
    core = lax.axis_index("core")
    partner = swap(share, "kvy")
    pair = jnp.where(chip == 0, jnp.stack([share, partner]), jnp.stack([partner, share]))
    other = swap(pair, "core")
    blocks = []
    for chip_block in range(2):
        for core_block in range(2):
            blocks.append(jnp.where(core == core_block, pair[chip_block], other[chip_block]))
    return jnp.concatenate(blocks, axis=1)


def gather_project(share, weights):
    chip = lax.axis_index("kvy")
    core = lax.axis_index("core")
    from_core = swap(share, "core")
    from_chip = swap(share, "kvy")
    local_pair = jnp.where(
        core == 0,
        jnp.concatenate([share, from_core], axis=1),
        jnp.concatenate([from_core, share], axis=1),
    )
    half = local_pair.shape[1]
    local_parts = tuple(
        jnp.dot(
            local_pair,
            lax.dynamic_slice_in_dim(weight, chip * half, half, 0),
            preferred_element_type=jnp.float32,
        )
        for weight in weights
    )
    from_chip, local_parts = lax.optimization_barrier((from_chip, local_parts))
    from_diagonal = swap(from_chip, "core")
    remote_pair = jnp.where(
        core == 0,
        jnp.concatenate([from_chip, from_diagonal], axis=1),
        jnp.concatenate([from_diagonal, from_chip], axis=1),
    )
    return [
        part
        + jnp.dot(
            remote_pair,
            lax.dynamic_slice_in_dim(weight, (1 - chip) * half, half, 0),
            preferred_element_type=jnp.float32,
        )
        for part, weight in zip(local_parts, weights)
    ]


def scatter_features(matrix_in, weight, link_type=None):
    chip = lax.axis_index("kvy")
    core = lax.axis_index("core")
    product = jnp.dot(matrix_in, weight, preferred_element_type=jnp.float32)
    width = product.shape[1] // (2 * CORES)

    def block(chip_block, core_block):
        start = (chip_block * CORES + core_block) * width
        return product[:, start:start + width]

    keep = jnp.stack([jnp.where(core == 0, block(k, 0), block(k, 1)) for k in range(2)])
    give = jnp.stack([jnp.where(core == 0, block(k, 1), block(k, 0)) for k in range(2)])
    chip_sum = keep + swap(give, "core")
    mine = jnp.where(chip == 0, chip_sum[0], chip_sum[1])
    theirs = jnp.where(chip == 0, chip_sum[1], chip_sum[0])
    if link_type is not None:
        theirs = theirs.astype(link_type)
    return mine + swap(theirs, "kvy").astype(jnp.float32)


def project_heads(mixed, weight, weight_far):
    chip = lax.axis_index("kvy")
    core = lax.axis_index("core")
    half = weight_far.shape[1]
    width = half // CORES
    mixed_far = swap(mixed, "kvy")
    weight_near = lax.dynamic_slice_in_dim(weight, chip * half, half, 1)
    chip_sum = jnp.dot(mixed, weight_near, preferred_element_type=jnp.float32) + jnp.dot(
        mixed_far, weight_far, preferred_element_type=jnp.float32
    )
    keep = lax.dynamic_slice_in_dim(chip_sum, core * width, width, 1)
    give = lax.dynamic_slice_in_dim(chip_sum, (1 - core) * width, width, 1)
    return keep + swap(give, "core")


def row_scale(values, gain_share):
    square_sum = jnp.sum(values * values, axis=-1, keepdims=True)
    square_sum = square_sum + swap(square_sum, "core")
    square_sum = square_sum + swap(square_sum, "kvy")
    width = values.shape[-1] * 2 * CORES
    return values * lax.rsqrt(square_sum / width + epsilon) * gain_share


def local(
    activations,
    span_length,
    offsets,
    decode_slot,
    attention_gain,
    query_weight,
    key_projection_matrix,
    value_projection_matrix,
    output_weight,
    feedforward_gain,
    gate_weight,
    up_weight,
    down_weight,
    earlier_rotated_keys,
    earlier_values,
):
    req_count = lax.axis_size("req")
    chips = lax.axis_size("kvy")
    kv_count = chips * CORES
    kv_index = lax.axis_index("kvy") * CORES + lax.axis_index("core")
    req_index = lax.axis_index("req")
    request_list = span_length.shape[0]
    total_rows, width_share = activations.shape
    span_size = total_rows // request_list
    local_kv = key_projection_matrix.shape[1] // HEAD_WIDTH
    local_q = query_weight.shape[1] // HEAD_WIDTH
    query_groups = local_q // local_kv

    past_share = earlier_rotated_keys.shape[1]
    stacked = jnp.stack([earlier_rotated_keys, earlier_values])
    stacked = stacked.reshape(2, request_list, past_share, kv_count, local_kv * HEAD_WIDTH)
    stacked = stacked.transpose(0, 3, 1, 2, 4)
    arrived = lax.all_to_all(stacked, ("kvy", "core"), split_axis=1, concat_axis=1, tiled=True)
    head_kv = arrived.transpose(0, 2, 1, 3, 4).reshape(
        2, request_list, kv_count * past_share, local_kv * HEAD_WIDTH
    )
    past_size = head_kv.shape[2]

    capacity = max(2, (request_list + req_count - 1) // req_count)
    order_ids = jnp.arange(request_list, dtype=jnp.int32)
    earlier = order_ids[None, :] < order_ids[:, None]
    own_dest = decode_slot // request_list
    same_dest = own_dest[:, None] == own_dest[None, :]
    own_rank = jnp.sum((same_dest & earlier).astype(jnp.int32), axis=1)
    buffer_place = own_dest * capacity + own_rank
    buffer_ids = jnp.arange(req_count * capacity, dtype=jnp.int32)
    matches = buffer_place[None, :] == buffer_ids[:, None]
    picked = jnp.sum(jnp.where(matches, order_ids[None, :], 0), axis=1)
    filled = jnp.any(matches, axis=1)
    lanes = local_kv * HEAD_WIDTH
    slot_code = jnp.stack([decode_slot // 16, decode_slot % 16], axis=1).astype(jnp.bfloat16)
    trailer = jnp.pad(slot_code[:, None, :], ((0, 0), (0, 7), (0, lanes - 2)))
    payload = jnp.concatenate([head_kv[0], head_kv[1], trailer], axis=1)
    packed = jnp.take(payload, picked, axis=0)
    packed = jnp.where(filled[:, None, None], packed, -jnp.ones((), packed.dtype))
    packed = packed.reshape((req_count, capacity) + payload.shape[1:])
    landed = lax.all_to_all(packed, "req", split_axis=0, concat_axis=0, tiled=True)
    landed = landed.reshape((req_count * capacity,) + payload.shape[1:])
    code = landed[:, 2 * past_size, :2].astype(jnp.int32)
    landed_slots = code[:, 0] * 16 + code[:, 1]
    wanted = req_index * request_list + order_ids
    slot_hits = landed_slots[None, :] == wanted[:, None]
    entry_ids = jnp.arange(req_count * capacity, dtype=jnp.int32)
    slot_position = jnp.sum(jnp.where(slot_hits, entry_ids[None, :], 0), axis=1)
    decode_rows = jnp.take(landed, slot_position, axis=0)
    decode_kv = (decode_rows[:, :past_size], decode_rows[:, past_size:2 * past_size])

    x_whole = gather_features(activations)
    chip_cols = output_weight.shape[1] // chips
    far_cols = lax.dynamic_slice_in_dim(
        output_weight, (1 - lax.axis_index("kvy")) * chip_cols, chip_cols, 1
    )
    weight_far = swap(far_cols, "kvy")
    x_float = x_whole.astype(jnp.float32)
    square_sum = jnp.sum(x_float * x_float, axis=-1, keepdims=True)
    normalized_input = (
        x_float * lax.rsqrt(square_sum / x_float.shape[-1] + epsilon) * attention_gain
    ).astype(jnp.bfloat16)
    position = (
        offsets[:, None].astype(jnp.float32) + jnp.arange(span_size, dtype=jnp.float32)[None, :]
    )
    query_rows = jnp.dot(
        normalized_input, query_weight, preferred_element_type=jnp.float32
    ).reshape(request_list, span_size, local_q, HEAD_WIDTH)
    query_rows = rotate_pairs(query_rows, position).astype(jnp.bfloat16)
    fresh_keys = jnp.dot(
        normalized_input, key_projection_matrix, preferred_element_type=jnp.float32
    ).reshape(request_list, span_size, local_kv, HEAD_WIDTH)
    fresh_keys = rotate_pairs(fresh_keys, position).astype(jnp.bfloat16)
    fresh_values = (
        jnp.dot(normalized_input, value_projection_matrix, preferred_element_type=jnp.float32)
        .astype(jnp.bfloat16)
        .reshape(request_list, span_size, local_kv, HEAD_WIDTH)
    )
    combined_keys = jnp.concatenate(
        [head_kv[0].reshape(request_list, past_size, local_kv, HEAD_WIDTH), fresh_keys], axis=1
    )
    combined_values = jnp.concatenate(
        [head_kv[1].reshape(request_list, past_size, local_kv, HEAD_WIDTH), fresh_values], axis=1
    )
    grouped_queries = query_rows.reshape(
        request_list, span_size, local_kv, query_groups, HEAD_WIDTH
    )
    scores = jnp.einsum(
        "rckgd,rskd->rkgcs", grouped_queries, combined_keys, preferred_element_type=jnp.float32
    ) / math.sqrt(HEAD_WIDTH)
    allowed = allowed_keys(span_length, span_size, past_size)[:, None, None, :, :]
    scores = jnp.where(allowed, scores, -jnp.inf)
    weights = jax.nn.softmax(scores, axis=-1).astype(jnp.bfloat16)
    mixed_heads = jnp.einsum(
        "rkgcs,rskd->rckgd", weights, combined_values, preferred_element_type=jnp.float32
    )
    mixed_heads = mixed_heads.astype(jnp.bfloat16).reshape(total_rows, local_q * HEAD_WIDTH)
    head_share = project_heads(mixed_heads, output_weight, weight_far)
    residual_share = activations.astype(jnp.float32) + head_share

    gain_share = lax.dynamic_slice_in_dim(feedforward_gain, kv_index * width_share, width_share)
    normed_share = row_scale(residual_share, gain_share).astype(jnp.bfloat16)
    gate_proj, upward = gather_project(normed_share, (gate_weight, up_weight))
    hidden = (jax.nn.silu(gate_proj) * upward).astype(jnp.bfloat16)
    mlp_share = scatter_features(hidden, down_weight, jnp.bfloat16)
    live_rows = (jnp.arange(span_size, dtype=jnp.int32)[None, :] < span_length[:, None]).reshape(
        total_rows
    )
    layer_out = jnp.where(live_rows[:, None], residual_share + mlp_share, 0.0).astype(jnp.bfloat16)
    return (layer_out, decode_kv[0], decode_kv[1])


def solution(mesh):
    req_size, kv_size = mesh.devices.shape
    split_mesh = Mesh(
        mesh.devices.reshape(req_size, kv_size // CORES, CORES), ("req", "kvy", "core")
    )
    kv = ("kvy", "core")
    return jax.shard_map(
        local,
        mesh=split_mesh,
        in_specs=(
            P("req", kv),
            P("req"),
            P("req"),
            P("req"),
            P(),
            P(None, kv),
            P(None, kv),
            P(None, kv),
            P(kv, None),
            P(),
            P(None, kv),
            P(None, kv),
            P(kv, None),
            P("req", kv, None),
            P("req", kv, None),
        ),
        out_specs=(P("req", kv), P("req", None, kv), P("req", None, kv)),
        check_vma=False,
    )
```

```python
import math

import jax
import jax.numpy as jnp
from jax import lax
from jax.sharding import Mesh
from jax.sharding import PartitionSpec as P

HEAD_WIDTH = 256
CORES = 2


rope_base = 1000042.0
epsilon = 1e-05


def rotate_pairs(tensor, position):
    half_size = tensor.shape[-1] // 2
    steps_float = jnp.arange(half_size, dtype=jnp.float32)
    inverse = jnp.exp(steps_float * (-2.0 * math.log(rope_base) / tensor.shape[-1]))
    angles = position[:, :, None] * inverse[None, None, :]
    cosine = jnp.cos(angles)[:, :, None, :]
    sine_part = jnp.sin(angles)[:, :, None, :]
    first_half = tensor[..., :half_size]
    second = tensor[..., half_size:]
    return jnp.concatenate(
        [first_half * cosine - second * sine_part, second * cosine + first_half * sine_part],
        axis=-1,
    )


def allowed_keys(span_length, span_size, past_size):
    key_pos = jnp.arange(past_size + span_size, dtype=jnp.int32) - past_size
    query_pos = jnp.arange(span_size, dtype=jnp.int32)
    causal = key_pos[None, :] <= query_pos[:, None]
    live_keys = key_pos[None, None, :] < span_length[:, None, None]
    return (key_pos[None, None, :] < 0) | causal[None, :, :] & live_keys


def swap(values, axis_name):
    return lax.ppermute(values, axis_name, [(0, 1), (1, 0)])


def gather_features(share):
    chip = lax.axis_index("kvy")
    core = lax.axis_index("core")
    partner = swap(share, "kvy")
    pair = jnp.where(chip == 0, jnp.stack([share, partner]), jnp.stack([partner, share]))
    other = swap(pair, "core")
    blocks = []
    for chip_block in range(2):
        for core_block in range(2):
            blocks.append(jnp.where(core == core_block, pair[chip_block], other[chip_block]))
    return jnp.concatenate(blocks, axis=1)


def gather_project(share, weights):
    chip = lax.axis_index("kvy")
    core = lax.axis_index("core")
    from_core = swap(share, "core")
    from_chip = swap(share, "kvy")
    local_pair = jnp.where(
        core == 0,
        jnp.concatenate([share, from_core], axis=1),
        jnp.concatenate([from_core, share], axis=1),
    )
    half = local_pair.shape[1]
    local_parts = tuple(
        jnp.dot(
            local_pair,
            lax.dynamic_slice_in_dim(weight, chip * half, half, 0),
            preferred_element_type=jnp.float32,
        )
        for weight in weights
    )
    from_chip, local_parts = lax.optimization_barrier((from_chip, local_parts))
    from_diagonal = swap(from_chip, "core")
    remote_pair = jnp.where(
        core == 0,
        jnp.concatenate([from_chip, from_diagonal], axis=1),
        jnp.concatenate([from_diagonal, from_chip], axis=1),
    )
    return [
        part
        + jnp.dot(
            remote_pair,
            lax.dynamic_slice_in_dim(weight, (1 - chip) * half, half, 0),
            preferred_element_type=jnp.float32,
        )
        for part, weight in zip(local_parts, weights)
    ]


def scatter_features(matrix_in, weight, link_type=None):
    chip = lax.axis_index("kvy")
    core = lax.axis_index("core")
    product = jnp.dot(matrix_in, weight, preferred_element_type=jnp.float32)
    width = product.shape[1] // (2 * CORES)

    def block(chip_block, core_block):
        start = (chip_block * CORES + core_block) * width
        return product[:, start:start + width]

    keep = jnp.stack([jnp.where(core == 0, block(k, 0), block(k, 1)) for k in range(2)])
    give = jnp.stack([jnp.where(core == 0, block(k, 1), block(k, 0)) for k in range(2)])
    chip_sum = keep + swap(give, "core")
    mine = jnp.where(chip == 0, chip_sum[0], chip_sum[1])
    theirs = jnp.where(chip == 0, chip_sum[1], chip_sum[0])
    if link_type is not None:
        theirs = theirs.astype(link_type)
    return mine + swap(theirs, "kvy").astype(jnp.float32)


def project_heads(mixed, weight, weight_far):
    chip = lax.axis_index("kvy")
    core = lax.axis_index("core")
    half = weight_far.shape[1]
    width = half // CORES
    mixed_far = swap(mixed, "kvy")
    weight_near = lax.dynamic_slice_in_dim(weight, chip * half, half, 1)
    chip_sum = jnp.dot(mixed, weight_near, preferred_element_type=jnp.float32) + jnp.dot(
        mixed_far, weight_far, preferred_element_type=jnp.float32
    )
    keep = lax.dynamic_slice_in_dim(chip_sum, core * width, width, 1)
    give = lax.dynamic_slice_in_dim(chip_sum, (1 - core) * width, width, 1)
    return keep + swap(give, "core")


def row_scale(values, gain_share):
    square_sum = jnp.sum(values * values, axis=-1, keepdims=True)
    square_sum = square_sum + swap(square_sum, "core")
    square_sum = square_sum + swap(square_sum, "kvy")
    width = values.shape[-1] * 2 * CORES
    return values * lax.rsqrt(square_sum / width + epsilon) * gain_share


def local(
    activations,
    span_length,
    offsets,
    decode_slot,
    attention_gain,
    query_weight,
    key_projection_matrix,
    value_projection_matrix,
    output_weight,
    feedforward_gain,
    gate_weight,
    up_weight,
    down_weight,
    earlier_rotated_keys,
    earlier_values,
):
    req_count = lax.axis_size("req")
    chips = lax.axis_size("kvy")
    kv_count = chips * CORES
    kv_index = lax.axis_index("kvy") * CORES + lax.axis_index("core")
    req_index = lax.axis_index("req")
    request_list = span_length.shape[0]
    total_rows, width_share = activations.shape
    span_size = total_rows // request_list
    local_kv = key_projection_matrix.shape[1] // HEAD_WIDTH
    local_q = query_weight.shape[1] // HEAD_WIDTH
    query_groups = local_q // local_kv

    past_share = earlier_rotated_keys.shape[1]
    lanes_share = local_kv * HEAD_WIDTH
    stacked = jnp.stack(
        [
            jnp.stack([past[..., j * lanes_share:(j + 1) * lanes_share] for past in (earlier_rotated_keys, earlier_values)])
            for j in range(kv_count)
        ]
    )
    arrived = lax.all_to_all(stacked, ("kvy", "core"), split_axis=0, concat_axis=0, tiled=True)
    head_kv = arrived.transpose(1, 2, 0, 3, 4).reshape(
        2, request_list, kv_count * past_share, lanes_share
    )
    past_size = head_kv.shape[2]

    capacity = max(2, (request_list + req_count - 1) // req_count)
    order_ids = jnp.arange(request_list, dtype=jnp.int32)
    earlier = order_ids[None, :] < order_ids[:, None]
    own_dest = decode_slot // request_list
    same_dest = own_dest[:, None] == own_dest[None, :]
    own_rank = jnp.sum((same_dest & earlier).astype(jnp.int32), axis=1)
    buffer_place = own_dest * capacity + own_rank
    buffer_ids = jnp.arange(req_count * capacity, dtype=jnp.int32)
    matches = buffer_place[None, :] == buffer_ids[:, None]
    picked = jnp.sum(jnp.where(matches, order_ids[None, :], 0), axis=1)
    filled = jnp.any(matches, axis=1)
    lanes = local_kv * HEAD_WIDTH
    slot_code = jnp.stack([decode_slot // 16, decode_slot % 16], axis=1).astype(jnp.bfloat16)
    trailer = jnp.pad(slot_code[:, None, :], ((0, 0), (0, 7), (0, lanes - 2)))
    payload = jnp.concatenate([head_kv[0], head_kv[1], trailer], axis=1)
    packed = jnp.take(payload, picked, axis=0)
    packed = jnp.where(filled[:, None, None], packed, -jnp.ones((), packed.dtype))
    packed = packed.reshape((req_count, capacity) + payload.shape[1:])
    landed = lax.all_to_all(packed, "req", split_axis=0, concat_axis=0, tiled=True)
    landed = landed.reshape((req_count * capacity,) + payload.shape[1:])
    code = landed[:, 2 * past_size, :2].astype(jnp.int32)
    landed_slots = code[:, 0] * 16 + code[:, 1]
    wanted = req_index * request_list + order_ids
    slot_hits = landed_slots[None, :] == wanted[:, None]
    entry_ids = jnp.arange(req_count * capacity, dtype=jnp.int32)
    slot_position = jnp.sum(jnp.where(slot_hits, entry_ids[None, :], 0), axis=1)
    decode_rows = jnp.take(landed, slot_position, axis=0)
    decode_kv = (decode_rows[:, :past_size], decode_rows[:, past_size:2 * past_size])

    x_whole = gather_features(activations)
    chip_cols = output_weight.shape[1] // chips
    far_cols = lax.dynamic_slice_in_dim(
        output_weight, (1 - lax.axis_index("kvy")) * chip_cols, chip_cols, 1
    )
    weight_far = swap(far_cols, "kvy")
    x_float = x_whole.astype(jnp.float32)
    square_sum = jnp.sum(x_float * x_float, axis=-1, keepdims=True)
    normalized_input = (
        x_float * lax.rsqrt(square_sum / x_float.shape[-1] + epsilon) * attention_gain
    ).astype(jnp.bfloat16)
    position = (
        offsets[:, None].astype(jnp.float32) + jnp.arange(span_size, dtype=jnp.float32)[None, :]
    )
    query_rows = jnp.dot(
        normalized_input, query_weight, preferred_element_type=jnp.float32
    ).reshape(request_list, span_size, local_q, HEAD_WIDTH)
    query_rows = rotate_pairs(query_rows, position).astype(jnp.bfloat16)
    fresh_keys = jnp.dot(
        normalized_input, key_projection_matrix, preferred_element_type=jnp.float32
    ).reshape(request_list, span_size, local_kv, HEAD_WIDTH)
    fresh_keys = rotate_pairs(fresh_keys, position).astype(jnp.bfloat16)
    fresh_values = (
        jnp.dot(normalized_input, value_projection_matrix, preferred_element_type=jnp.float32)
        .astype(jnp.bfloat16)
        .reshape(request_list, span_size, local_kv, HEAD_WIDTH)
    )
    combined_keys = jnp.concatenate(
        [head_kv[0].reshape(request_list, past_size, local_kv, HEAD_WIDTH), fresh_keys], axis=1
    )
    combined_values = jnp.concatenate(
        [head_kv[1].reshape(request_list, past_size, local_kv, HEAD_WIDTH), fresh_values], axis=1
    )
    grouped_queries = query_rows.reshape(
        request_list, span_size, local_kv, query_groups, HEAD_WIDTH
    )
    scores = jnp.einsum(
        "rckgd,rskd->rkgcs", grouped_queries, combined_keys, preferred_element_type=jnp.float32
    ) / math.sqrt(HEAD_WIDTH)
    allowed = allowed_keys(span_length, span_size, past_size)[:, None, None, :, :]
    scores = jnp.where(allowed, scores, -jnp.inf)
    weights = jax.nn.softmax(scores, axis=-1).astype(jnp.bfloat16)
    mixed_heads = jnp.einsum(
        "rkgcs,rskd->rckgd", weights, combined_values, preferred_element_type=jnp.float32
    )
    mixed_heads = mixed_heads.astype(jnp.bfloat16).reshape(total_rows, local_q * HEAD_WIDTH)
    head_share = project_heads(mixed_heads, output_weight, weight_far)
    residual_share = activations.astype(jnp.float32) + head_share

    gain_share = lax.dynamic_slice_in_dim(feedforward_gain, kv_index * width_share, width_share)
    normed_share = row_scale(residual_share, gain_share).astype(jnp.bfloat16)
    gate_proj, upward = gather_project(normed_share, (gate_weight, up_weight))
    hidden = (jax.nn.silu(gate_proj) * upward).astype(jnp.bfloat16)
    mlp_share = scatter_features(hidden, down_weight, jnp.bfloat16)
    live_rows = (jnp.arange(span_size, dtype=jnp.int32)[None, :] < span_length[:, None]).reshape(
        total_rows
    )
    layer_out = jnp.where(live_rows[:, None], residual_share + mlp_share, 0.0).astype(jnp.bfloat16)
    return (layer_out, decode_kv[0], decode_kv[1])


def solution(mesh):
    req_size, kv_size = mesh.devices.shape
    split_mesh = Mesh(
        mesh.devices.reshape(req_size, kv_size // CORES, CORES), ("req", "kvy", "core")
    )
    kv = ("kvy", "core")
    return jax.shard_map(
        local,
        mesh=split_mesh,
        in_specs=(
            P("req", kv),
            P("req"),
            P("req"),
            P("req"),
            P(),
            P(None, kv),
            P(None, kv),
            P(None, kv),
            P(kv, None),
            P(),
            P(None, kv),
            P(None, kv),
            P(kv, None),
            P("req", kv, None),
            P("req", kv, None),
        ),
        out_specs=(P("req", kv), P("req", None, kv), P("req", None, kv)),
        check_vma=False,
    )
```

```python
import math

import jax
import jax.numpy as jnp
from jax import lax
from jax.sharding import Mesh
from jax.sharding import PartitionSpec as P

HEAD_WIDTH = 256
CORES = 2


rope_base = 1000042.0
epsilon = 1e-05


def rotate_pairs(tensor, position):
    half_size = tensor.shape[-1] // 2
    steps_float = jnp.arange(half_size, dtype=jnp.float32)
    inverse = jnp.exp(steps_float * (-2.0 * math.log(rope_base) / tensor.shape[-1]))
    angles = position[:, :, None] * inverse[None, None, :]
    cosine = jnp.cos(angles)[:, :, None, :]
    sine_part = jnp.sin(angles)[:, :, None, :]
    first_half = tensor[..., :half_size]
    second = tensor[..., half_size:]
    return jnp.concatenate(
        [first_half * cosine - second * sine_part, second * cosine + first_half * sine_part],
        axis=-1,
    )


def allowed_keys(span_length, span_size, past_size):
    key_pos = jnp.arange(past_size + span_size, dtype=jnp.int32) - past_size
    query_pos = jnp.arange(span_size, dtype=jnp.int32)
    causal = key_pos[None, :] <= query_pos[:, None]
    live_keys = key_pos[None, None, :] < span_length[:, None, None]
    return (key_pos[None, None, :] < 0) | causal[None, :, :] & live_keys


def swap(values, axis_name):
    return lax.ppermute(values, axis_name, [(0, 1), (1, 0)])


def gather_features(share):
    chip = lax.axis_index("kvy")
    core = lax.axis_index("core")
    partner = swap(share, "kvy")
    pair = jnp.where(chip == 0, jnp.stack([share, partner]), jnp.stack([partner, share]))
    other = swap(pair, "core")
    blocks = []
    for chip_block in range(2):
        for core_block in range(2):
            blocks.append(jnp.where(core == core_block, pair[chip_block], other[chip_block]))
    return jnp.concatenate(blocks, axis=1)


def gather_project(share, weights):
    chip = lax.axis_index("kvy")
    core = lax.axis_index("core")
    from_core = swap(share, "core")
    from_chip = swap(share, "kvy")
    local_pair = jnp.where(
        core == 0,
        jnp.concatenate([share, from_core], axis=1),
        jnp.concatenate([from_core, share], axis=1),
    )
    half = local_pair.shape[1]
    local_parts = tuple(
        jnp.dot(
            local_pair,
            lax.dynamic_slice_in_dim(weight, chip * half, half, 0),
            preferred_element_type=jnp.float32,
        )
        for weight in weights
    )
    from_chip, local_parts = lax.optimization_barrier((from_chip, local_parts))
    from_diagonal = swap(from_chip, "core")
    remote_pair = jnp.where(
        core == 0,
        jnp.concatenate([from_chip, from_diagonal], axis=1),
        jnp.concatenate([from_diagonal, from_chip], axis=1),
    )
    return [
        part
        + jnp.dot(
            remote_pair,
            lax.dynamic_slice_in_dim(weight, (1 - chip) * half, half, 0),
            preferred_element_type=jnp.float32,
        )
        for part, weight in zip(local_parts, weights)
    ]


def scatter_features(matrix_in, weight, link_type=None):
    chip = lax.axis_index("kvy")
    core = lax.axis_index("core")
    product = jnp.dot(matrix_in, weight, preferred_element_type=jnp.float32)
    width = product.shape[1] // (2 * CORES)

    def block(chip_block, core_block):
        start = (chip_block * CORES + core_block) * width
        return product[:, start:start + width]

    keep = jnp.stack([jnp.where(core == 0, block(k, 0), block(k, 1)) for k in range(2)])
    give = jnp.stack([jnp.where(core == 0, block(k, 1), block(k, 0)) for k in range(2)])
    chip_sum = keep + swap(give, "core")
    mine = jnp.where(chip == 0, chip_sum[0], chip_sum[1])
    theirs = jnp.where(chip == 0, chip_sum[1], chip_sum[0])
    if link_type is not None:
        theirs = theirs.astype(link_type)
    return mine + swap(theirs, "kvy").astype(jnp.float32)


def project_heads(mixed, weight, weight_far):
    chip = lax.axis_index("kvy")
    core = lax.axis_index("core")
    half = weight_far.shape[1]
    width = half // CORES
    mixed_far = swap(mixed, "kvy")
    weight_near = lax.dynamic_slice_in_dim(weight, chip * half, half, 1)
    chip_sum = jnp.dot(mixed, weight_near, preferred_element_type=jnp.float32) + jnp.dot(
        mixed_far, weight_far, preferred_element_type=jnp.float32
    )
    keep = lax.dynamic_slice_in_dim(chip_sum, core * width, width, 1)
    give = lax.dynamic_slice_in_dim(chip_sum, (1 - core) * width, width, 1)
    return keep + swap(give, "core")


def row_scale(values, gain_share):
    square_sum = jnp.sum(values * values, axis=-1, keepdims=True)
    square_sum = square_sum + swap(square_sum, "core")
    square_sum = square_sum + swap(square_sum, "kvy")
    width = values.shape[-1] * 2 * CORES
    return values * lax.rsqrt(square_sum / width + epsilon) * gain_share


def local(
    activations,
    span_length,
    offsets,
    decode_slot,
    attention_gain,
    query_weight,
    key_projection_matrix,
    value_projection_matrix,
    output_weight,
    feedforward_gain,
    gate_weight,
    up_weight,
    down_weight,
    earlier_rotated_keys,
    earlier_values,
):
    req_count = lax.axis_size("req")
    chips = lax.axis_size("kvy")
    kv_count = chips * CORES
    kv_index = lax.axis_index("kvy") * CORES + lax.axis_index("core")
    req_index = lax.axis_index("req")
    request_list = span_length.shape[0]
    total_rows, width_share = activations.shape
    span_size = total_rows // request_list
    local_kv = key_projection_matrix.shape[1] // HEAD_WIDTH
    local_q = query_weight.shape[1] // HEAD_WIDTH
    query_groups = local_q // local_kv

    past_share = earlier_rotated_keys.shape[1]
    stacked = jnp.stack([earlier_rotated_keys, earlier_values])
    stacked = stacked.reshape(2, request_list, past_share, kv_count, local_kv * HEAD_WIDTH)
    stacked = stacked.transpose(0, 3, 1, 2, 4)
    arrived = lax.all_to_all(stacked, ("kvy", "core"), split_axis=1, concat_axis=1, tiled=True)
    head_kv = arrived.transpose(0, 2, 1, 3, 4).reshape(
        2, request_list, kv_count * past_share, local_kv * HEAD_WIDTH
    )
    past_size = head_kv.shape[2]

    capacity = max(2, (request_list + req_count - 1) // req_count)
    order_ids = jnp.arange(request_list, dtype=jnp.int32)
    earlier = order_ids[None, :] < order_ids[:, None]
    own_dest = decode_slot // request_list
    same_dest = own_dest[:, None] == own_dest[None, :]
    own_rank = jnp.sum((same_dest & earlier).astype(jnp.int32), axis=1)
    buffer_place = own_dest * capacity + own_rank
    buffer_ids = jnp.arange(req_count * capacity, dtype=jnp.int32)
    matches = buffer_place[None, :] == buffer_ids[:, None]
    picked = jnp.sum(jnp.where(matches, order_ids[None, :], 0), axis=1)
    filled = jnp.any(matches, axis=1)
    lanes = local_kv * HEAD_WIDTH
    slot_code = jnp.stack([decode_slot // 16, decode_slot % 16], axis=1).astype(jnp.bfloat16)
    trailer = jnp.pad(slot_code[:, None, :], ((0, 0), (0, 7), (0, lanes - 2)))
    payload = jnp.concatenate([head_kv[0], head_kv[1], trailer], axis=1)
    packed = jnp.take(payload, picked, axis=0)
    packed = jnp.where(filled[:, None, None], packed, -jnp.ones((), packed.dtype))
    packed = packed.reshape((req_count, capacity) + payload.shape[1:])
    landed = lax.all_to_all(packed, "req", split_axis=0, concat_axis=0, tiled=True)
    landed = landed.reshape((req_count * capacity,) + payload.shape[1:])
    code = landed[:, 2 * past_size, :2].astype(jnp.int32)
    landed_slots = code[:, 0] * 16 + code[:, 1]
    wanted = req_index * request_list + order_ids
    slot_hits = landed_slots[None, :] == wanted[:, None]
    entry_ids = jnp.arange(req_count * capacity, dtype=jnp.int32)
    slot_position = jnp.sum(jnp.where(slot_hits, entry_ids[None, :], 0), axis=1)
    decode_rows = jnp.take(landed, slot_position, axis=0)
    decode_kv = (decode_rows[:, :past_size], decode_rows[:, past_size:2 * past_size])

    x_whole = gather_features(activations)
    chip_cols = output_weight.shape[1] // chips
    far_cols = lax.dynamic_slice_in_dim(
        output_weight, (1 - lax.axis_index("kvy")) * chip_cols, chip_cols, 1
    )
    weight_far = swap(far_cols, "kvy")
    x_float = x_whole.astype(jnp.float32)
    square_sum = jnp.sum(x_float * x_float, axis=-1, keepdims=True)
    normalized_input = (
        x_float * lax.rsqrt(square_sum / x_float.shape[-1] + epsilon) * attention_gain
    ).astype(jnp.bfloat16)
    position = (
        offsets[:, None].astype(jnp.float32) + jnp.arange(span_size, dtype=jnp.float32)[None, :]
    )
    query_rows = jnp.dot(
        normalized_input, query_weight, preferred_element_type=jnp.float32
    ).reshape(request_list, span_size, local_q, HEAD_WIDTH)
    query_rows = rotate_pairs(query_rows, position).astype(jnp.bfloat16)
    fresh_keys = jnp.dot(
        normalized_input, key_projection_matrix, preferred_element_type=jnp.float32
    ).reshape(request_list, span_size, local_kv, HEAD_WIDTH)
    fresh_keys = rotate_pairs(fresh_keys, position).astype(jnp.bfloat16)
    fresh_values = (
        jnp.dot(normalized_input, value_projection_matrix, preferred_element_type=jnp.float32)
        .astype(jnp.bfloat16)
        .reshape(request_list, span_size, local_kv, HEAD_WIDTH)
    )
    combined_keys = jnp.concatenate(
        [head_kv[0].reshape(request_list, past_size, local_kv, HEAD_WIDTH), fresh_keys], axis=1
    )
    combined_values = jnp.concatenate(
        [head_kv[1].reshape(request_list, past_size, local_kv, HEAD_WIDTH), fresh_values], axis=1
    )
    grouped_queries = query_rows.reshape(
        request_list, span_size, local_kv, query_groups, HEAD_WIDTH
    )
    scores = jnp.einsum(
        "rckgd,rskd->rkgcs", grouped_queries, combined_keys, preferred_element_type=jnp.float32
    ) / math.sqrt(HEAD_WIDTH)
    allowed = allowed_keys(span_length, span_size, past_size)[:, None, None, :, :]
    scores = jnp.where(allowed, scores, -jnp.inf)
    weights = jax.nn.softmax(scores, axis=-1).astype(jnp.bfloat16)
    mixed_heads = jnp.einsum(
        "rkgcs,rskd->rckgd", weights, combined_values, preferred_element_type=jnp.float32
    )
    mixed_heads = mixed_heads.astype(jnp.bfloat16).reshape(total_rows, local_q * HEAD_WIDTH)
    head_share = project_heads(mixed_heads, output_weight, weight_far)
    residual_share = activations.astype(jnp.float32) + head_share

    gain_share = lax.dynamic_slice_in_dim(feedforward_gain, kv_index * width_share, width_share)
    normed_share = row_scale(residual_share, gain_share).astype(jnp.bfloat16)
    gate_proj, upward = gather_project(normed_share, (gate_weight, up_weight))
    hidden = (jax.nn.silu(gate_proj) * upward).astype(jnp.bfloat16)
    hidden = lax.optimization_barrier(hidden)
    mlp_share = scatter_features(hidden, down_weight, jnp.bfloat16)
    live_rows = (jnp.arange(span_size, dtype=jnp.int32)[None, :] < span_length[:, None]).reshape(
        total_rows
    )
    layer_out = jnp.where(live_rows[:, None], residual_share + mlp_share, 0.0).astype(jnp.bfloat16)
    return (layer_out, decode_kv[0], decode_kv[1])


def solution(mesh):
    req_size, kv_size = mesh.devices.shape
    split_mesh = Mesh(
        mesh.devices.reshape(req_size, kv_size // CORES, CORES), ("req", "kvy", "core")
    )
    kv = ("kvy", "core")
    return jax.shard_map(
        local,
        mesh=split_mesh,
        in_specs=(
            P("req", kv),
            P("req"),
            P("req"),
            P("req"),
            P(),
            P(None, kv),
            P(None, kv),
            P(None, kv),
            P(kv, None),
            P(),
            P(None, kv),
            P(None, kv),
            P(kv, None),
            P("req", kv, None),
            P("req", kv, None),
        ),
        out_specs=(P("req", kv), P("req", None, kv), P("req", None, kv)),
        check_vma=False,
    )
```

```python
import math

import jax
import jax.numpy as jnp
from jax import lax
from jax.sharding import Mesh
from jax.sharding import PartitionSpec as P

HEAD_WIDTH = 256
CORES = 2


rope_base = 1000042.0
epsilon = 1e-05


def rotate_pairs(tensor, position):
    half_size = tensor.shape[-1] // 2
    steps_float = jnp.arange(half_size, dtype=jnp.float32)
    inverse = jnp.exp(steps_float * (-2.0 * math.log(rope_base) / tensor.shape[-1]))
    angles = position[:, :, None] * inverse[None, None, :]
    cosine = jnp.cos(angles)[:, :, None, :]
    sine_part = jnp.sin(angles)[:, :, None, :]
    first_half = tensor[..., :half_size]
    second = tensor[..., half_size:]
    return jnp.concatenate(
        [first_half * cosine - second * sine_part, second * cosine + first_half * sine_part],
        axis=-1,
    )


def allowed_keys(span_length, span_size, past_size):
    key_pos = jnp.arange(past_size + span_size, dtype=jnp.int32) - past_size
    query_pos = jnp.arange(span_size, dtype=jnp.int32)
    causal = key_pos[None, :] <= query_pos[:, None]
    live_keys = key_pos[None, None, :] < span_length[:, None, None]
    return (key_pos[None, None, :] < 0) | causal[None, :, :] & live_keys


def swap(values, axis_name):
    return lax.ppermute(values, axis_name, [(0, 1), (1, 0)])


def gather_features(share):
    chip = lax.axis_index("kvy")
    core = lax.axis_index("core")
    partner = swap(share, "kvy")
    pair = jnp.where(chip == 0, jnp.stack([share, partner]), jnp.stack([partner, share]))
    other = swap(pair, "core")
    blocks = []
    for chip_block in range(2):
        for core_block in range(2):
            blocks.append(jnp.where(core == core_block, pair[chip_block], other[chip_block]))
    return jnp.concatenate(blocks, axis=1)


def gather_project(share, weights):
    chip = lax.axis_index("kvy")
    core = lax.axis_index("core")
    from_core = swap(share, "core")
    from_chip = swap(share, "kvy")
    local_pair = jnp.where(
        core == 0,
        jnp.concatenate([share, from_core], axis=1),
        jnp.concatenate([from_core, share], axis=1),
    )
    half = local_pair.shape[1]
    local_parts = tuple(
        jnp.dot(
            local_pair,
            lax.dynamic_slice_in_dim(weight, chip * half, half, 0),
            preferred_element_type=jnp.float32,
        )
        for weight in weights
    )
    from_chip, local_parts = lax.optimization_barrier((from_chip, local_parts))
    from_diagonal = swap(from_chip, "core")
    remote_pair = jnp.where(
        core == 0,
        jnp.concatenate([from_chip, from_diagonal], axis=1),
        jnp.concatenate([from_diagonal, from_chip], axis=1),
    )
    return [
        part
        + jnp.dot(
            remote_pair,
            lax.dynamic_slice_in_dim(weight, (1 - chip) * half, half, 0),
            preferred_element_type=jnp.float32,
        )
        for part, weight in zip(local_parts, weights)
    ]


def scatter_features(matrix_in, weight, link_type=None):
    chip = lax.axis_index("kvy")
    core = lax.axis_index("core")
    product = jnp.dot(matrix_in, weight, preferred_element_type=jnp.float32)
    width = product.shape[1] // (2 * CORES)

    def block(chip_block, core_block):
        start = (chip_block * CORES + core_block) * width
        return product[:, start:start + width]

    keep = jnp.stack([jnp.where(core == 0, block(k, 0), block(k, 1)) for k in range(2)])
    give = jnp.stack([jnp.where(core == 0, block(k, 1), block(k, 0)) for k in range(2)])
    chip_sum = keep + swap(give, "core")
    mine = jnp.where(chip == 0, chip_sum[0], chip_sum[1])
    theirs = jnp.where(chip == 0, chip_sum[1], chip_sum[0])
    if link_type is not None:
        theirs = theirs.astype(link_type)
    return mine + swap(theirs, "kvy").astype(jnp.float32)


def project_heads(mixed, weight, weight_far):
    chip = lax.axis_index("kvy")
    core = lax.axis_index("core")
    half = weight_far.shape[1]
    width = half // CORES
    mixed_far = swap(mixed, "kvy")
    weight_near = lax.dynamic_slice_in_dim(weight, chip * half, half, 1)
    chip_sum = jnp.dot(mixed, weight_near, preferred_element_type=jnp.float32) + jnp.dot(
        mixed_far, weight_far, preferred_element_type=jnp.float32
    )
    keep = lax.dynamic_slice_in_dim(chip_sum, core * width, width, 1)
    give = lax.dynamic_slice_in_dim(chip_sum, (1 - core) * width, width, 1)
    return keep + swap(give, "core")


def row_scale(values, gain_share):
    square_sum = jnp.sum(values * values, axis=-1, keepdims=True)
    square_sum = square_sum + swap(square_sum, "core")
    square_sum = square_sum + swap(square_sum, "kvy")
    width = values.shape[-1] * 2 * CORES
    return values * lax.rsqrt(square_sum / width + epsilon) * gain_share


def local(
    activations,
    span_length,
    offsets,
    decode_slot,
    attention_gain,
    query_weight,
    key_projection_matrix,
    value_projection_matrix,
    output_weight,
    feedforward_gain,
    gate_weight,
    up_weight,
    down_weight,
    earlier_rotated_keys,
    earlier_values,
):
    req_count = lax.axis_size("req")
    chips = lax.axis_size("kvy")
    kv_count = chips * CORES
    kv_index = lax.axis_index("kvy") * CORES + lax.axis_index("core")
    req_index = lax.axis_index("req")
    request_list = span_length.shape[0]
    total_rows, width_share = activations.shape
    span_size = total_rows // request_list
    local_kv = key_projection_matrix.shape[1] // HEAD_WIDTH
    local_q = query_weight.shape[1] // HEAD_WIDTH
    query_groups = local_q // local_kv

    past_share = earlier_rotated_keys.shape[1]
    stacked = jnp.stack([earlier_rotated_keys, earlier_values])
    stacked = stacked.reshape(2, request_list, past_share, kv_count, local_kv * HEAD_WIDTH)
    stacked = stacked.transpose(0, 3, 1, 2, 4)
    arrived = lax.all_to_all(stacked, ("kvy", "core"), split_axis=1, concat_axis=1, tiled=True)
    head_kv = arrived.transpose(0, 2, 1, 3, 4).reshape(
        2, request_list, kv_count * past_share, local_kv * HEAD_WIDTH
    )
    past_size = head_kv.shape[2]

    capacity = max(2, (request_list + req_count - 1) // req_count)
    order_ids = jnp.arange(request_list, dtype=jnp.int32)
    earlier = order_ids[None, :] < order_ids[:, None]
    own_dest = decode_slot // request_list
    same_dest = own_dest[:, None] == own_dest[None, :]
    own_rank = jnp.sum((same_dest & earlier).astype(jnp.int32), axis=1)
    buffer_place = own_dest * capacity + own_rank
    buffer_ids = jnp.arange(req_count * capacity, dtype=jnp.int32)
    matches = buffer_place[None, :] == buffer_ids[:, None]
    picked = jnp.sum(jnp.where(matches, order_ids[None, :], 0), axis=1)
    filled = jnp.any(matches, axis=1)
    lanes = local_kv * HEAD_WIDTH
    slot_code = jnp.stack([decode_slot // 16, decode_slot % 16], axis=1).astype(jnp.bfloat16)
    trailer = jnp.pad(slot_code[:, None, :], ((0, 0), (0, 7), (0, lanes - 2)))
    payload = jnp.concatenate([head_kv[0], head_kv[1], trailer], axis=1)
    packed = jnp.take(payload, picked, axis=0)
    packed = jnp.where(filled[:, None, None], packed, -jnp.ones((), packed.dtype))
    packed = packed.reshape((req_count, capacity) + payload.shape[1:])
    landed = lax.all_to_all(packed, "req", split_axis=0, concat_axis=0, tiled=True)
    x_whole = gather_features(activations)
    chip_cols = output_weight.shape[1] // chips
    far_cols = lax.dynamic_slice_in_dim(
        output_weight, (1 - lax.axis_index("kvy")) * chip_cols, chip_cols, 1
    )
    weight_far = swap(far_cols, "kvy")
    x_float = x_whole.astype(jnp.float32)
    square_sum = jnp.sum(x_float * x_float, axis=-1, keepdims=True)
    normalized_input = (
        x_float * lax.rsqrt(square_sum / x_float.shape[-1] + epsilon) * attention_gain
    ).astype(jnp.bfloat16)
    position = (
        offsets[:, None].astype(jnp.float32) + jnp.arange(span_size, dtype=jnp.float32)[None, :]
    )
    query_rows = jnp.dot(
        normalized_input, query_weight, preferred_element_type=jnp.float32
    ).reshape(request_list, span_size, local_q, HEAD_WIDTH)
    query_rows = rotate_pairs(query_rows, position).astype(jnp.bfloat16)
    fresh_keys = jnp.dot(
        normalized_input, key_projection_matrix, preferred_element_type=jnp.float32
    ).reshape(request_list, span_size, local_kv, HEAD_WIDTH)
    fresh_keys = rotate_pairs(fresh_keys, position).astype(jnp.bfloat16)
    fresh_values = (
        jnp.dot(normalized_input, value_projection_matrix, preferred_element_type=jnp.float32)
        .astype(jnp.bfloat16)
        .reshape(request_list, span_size, local_kv, HEAD_WIDTH)
    )
    combined_keys = jnp.concatenate(
        [head_kv[0].reshape(request_list, past_size, local_kv, HEAD_WIDTH), fresh_keys], axis=1
    )
    combined_values = jnp.concatenate(
        [head_kv[1].reshape(request_list, past_size, local_kv, HEAD_WIDTH), fresh_values], axis=1
    )
    grouped_queries = query_rows.reshape(
        request_list, span_size, local_kv, query_groups, HEAD_WIDTH
    )
    scores = jnp.einsum(
        "rckgd,rskd->rkgcs", grouped_queries, combined_keys, preferred_element_type=jnp.float32
    ) / math.sqrt(HEAD_WIDTH)
    allowed = allowed_keys(span_length, span_size, past_size)[:, None, None, :, :]
    scores = jnp.where(allowed, scores, -jnp.inf)
    weights = jax.nn.softmax(scores, axis=-1).astype(jnp.bfloat16)
    mixed_heads = jnp.einsum(
        "rkgcs,rskd->rckgd", weights, combined_values, preferred_element_type=jnp.float32
    )
    mixed_heads = mixed_heads.astype(jnp.bfloat16).reshape(total_rows, local_q * HEAD_WIDTH)
    head_share = project_heads(mixed_heads, output_weight, weight_far)
    residual_share = activations.astype(jnp.float32) + head_share

    gain_share = lax.dynamic_slice_in_dim(feedforward_gain, kv_index * width_share, width_share)
    normed_share = row_scale(residual_share, gain_share).astype(jnp.bfloat16)
    gate_proj, upward = gather_project(normed_share, (gate_weight, up_weight))
    hidden = (jax.nn.silu(gate_proj) * upward).astype(jnp.bfloat16)
    hidden = lax.optimization_barrier(hidden)
    mlp_share = scatter_features(hidden, down_weight, jnp.bfloat16)
    landed, mlp_share = lax.optimization_barrier((landed, mlp_share))
    landed = landed.reshape((req_count * capacity,) + payload.shape[1:])
    code = landed[:, 2 * past_size, :2].astype(jnp.int32)
    landed_slots = code[:, 0] * 16 + code[:, 1]
    wanted = req_index * request_list + order_ids
    slot_hits = landed_slots[None, :] == wanted[:, None]
    entry_ids = jnp.arange(req_count * capacity, dtype=jnp.int32)
    slot_position = jnp.sum(jnp.where(slot_hits, entry_ids[None, :], 0), axis=1)
    decode_rows = jnp.take(landed, slot_position, axis=0)
    decode_kv = (decode_rows[:, :past_size], decode_rows[:, past_size:2 * past_size])

    live_rows = (jnp.arange(span_size, dtype=jnp.int32)[None, :] < span_length[:, None]).reshape(
        total_rows
    )
    layer_out = jnp.where(live_rows[:, None], residual_share + mlp_share, 0.0).astype(jnp.bfloat16)
    return (layer_out, decode_kv[0], decode_kv[1])


def solution(mesh):
    req_size, kv_size = mesh.devices.shape
    split_mesh = Mesh(
        mesh.devices.reshape(req_size, kv_size // CORES, CORES), ("req", "kvy", "core")
    )
    kv = ("kvy", "core")
    return jax.shard_map(
        local,
        mesh=split_mesh,
        in_specs=(
            P("req", kv),
            P("req"),
            P("req"),
            P("req"),
            P(),
            P(None, kv),
            P(None, kv),
            P(None, kv),
            P(kv, None),
            P(),
            P(None, kv),
            P(None, kv),
            P(kv, None),
            P("req", kv, None),
            P("req", kv, None),
        ),
        out_specs=(P("req", kv), P("req", None, kv), P("req", None, kv)),
        check_vma=False,
    )
```

```python
import math

import jax
import jax.numpy as jnp
from jax import lax
from jax.sharding import Mesh
from jax.sharding import PartitionSpec as P

HEAD_WIDTH = 256
CORES = 2


rope_base = 1000042.0
epsilon = 1e-05


def rotate_pairs(tensor, position):
    half_size = tensor.shape[-1] // 2
    steps_float = jnp.arange(half_size, dtype=jnp.float32)
    inverse = jnp.exp(steps_float * (-2.0 * math.log(rope_base) / tensor.shape[-1]))
    angles = position[:, :, None] * inverse[None, None, :]
    cosine = jnp.cos(angles)[:, :, None, :]
    sine_part = jnp.sin(angles)[:, :, None, :]
    first_half = tensor[..., :half_size]
    second = tensor[..., half_size:]
    return jnp.concatenate(
        [first_half * cosine - second * sine_part, second * cosine + first_half * sine_part],
        axis=-1,
    )


def allowed_keys(span_length, span_size, past_size):
    key_pos = jnp.arange(past_size + span_size, dtype=jnp.int32) - past_size
    query_pos = jnp.arange(span_size, dtype=jnp.int32)
    causal = key_pos[None, :] <= query_pos[:, None]
    live_keys = key_pos[None, None, :] < span_length[:, None, None]
    return (key_pos[None, None, :] < 0) | causal[None, :, :] & live_keys


def swap(values, axis_name):
    return lax.ppermute(values, axis_name, [(0, 1), (1, 0)])


def gather_features(share):
    chip = lax.axis_index("kvy")
    core = lax.axis_index("core")
    partner = swap(share, "kvy")
    pair = jnp.where(chip == 0, jnp.stack([share, partner]), jnp.stack([partner, share]))
    other = swap(pair, "core")
    blocks = []
    for chip_block in range(2):
        for core_block in range(2):
            blocks.append(jnp.where(core == core_block, pair[chip_block], other[chip_block]))
    return jnp.concatenate(blocks, axis=1)


def gather_project(share, weights):
    chip = lax.axis_index("kvy")
    core = lax.axis_index("core")
    from_core = swap(share, "core")
    from_chip = swap(share, "kvy")
    local_pair = jnp.where(
        core == 0,
        jnp.concatenate([share, from_core], axis=1),
        jnp.concatenate([from_core, share], axis=1),
    )
    half = local_pair.shape[1]
    local_parts = tuple(
        jnp.dot(
            local_pair,
            lax.dynamic_slice_in_dim(weight, chip * half, half, 0),
            preferred_element_type=jnp.float32,
        )
        for weight in weights
    )
    from_chip, local_parts = lax.optimization_barrier((from_chip, local_parts))
    from_diagonal = swap(from_chip, "core")
    remote_pair = jnp.where(
        core == 0,
        jnp.concatenate([from_chip, from_diagonal], axis=1),
        jnp.concatenate([from_diagonal, from_chip], axis=1),
    )
    return [
        part
        + jnp.dot(
            remote_pair,
            lax.dynamic_slice_in_dim(weight, (1 - chip) * half, half, 0),
            preferred_element_type=jnp.float32,
        )
        for part, weight in zip(local_parts, weights)
    ]


def scatter_features(matrix_in, weight, link_type=None):
    chip = lax.axis_index("kvy")
    core = lax.axis_index("core")
    product = jnp.dot(matrix_in, weight, preferred_element_type=jnp.float32)
    width = product.shape[1] // (2 * CORES)

    def block(chip_block, core_block):
        start = (chip_block * CORES + core_block) * width
        return product[:, start:start + width]

    keep = jnp.stack([jnp.where(core == 0, block(k, 0), block(k, 1)) for k in range(2)])
    give = jnp.stack([jnp.where(core == 0, block(k, 1), block(k, 0)) for k in range(2)])
    chip_sum = keep + swap(give, "core")
    mine = jnp.where(chip == 0, chip_sum[0], chip_sum[1])
    theirs = jnp.where(chip == 0, chip_sum[1], chip_sum[0])
    if link_type is not None:
        theirs = theirs.astype(link_type)
    return mine + swap(theirs, "kvy").astype(jnp.float32)


def project_heads(mixed, weight, weight_far):
    chip = lax.axis_index("kvy")
    core = lax.axis_index("core")
    half = weight_far.shape[1]
    width = half // CORES
    mixed_far = swap(mixed, "kvy")
    weight_near = lax.dynamic_slice_in_dim(weight, chip * half, half, 1)
    chip_sum = jnp.dot(mixed, weight_near, preferred_element_type=jnp.float32) + jnp.dot(
        mixed_far, weight_far, preferred_element_type=jnp.float32
    )
    keep = lax.dynamic_slice_in_dim(chip_sum, core * width, width, 1)
    give = lax.dynamic_slice_in_dim(chip_sum, (1 - core) * width, width, 1)
    return keep + swap(give, "core")


def row_scale(values, gain_share):
    square_sum = jnp.sum(values * values, axis=-1, keepdims=True)
    square_sum = square_sum + swap(square_sum, "core")
    square_sum = square_sum + swap(square_sum, "kvy")
    width = values.shape[-1] * 2 * CORES
    return values * lax.rsqrt(square_sum / width + epsilon) * gain_share


def local(
    activations,
    span_length,
    offsets,
    decode_slot,
    attention_gain,
    query_weight,
    key_projection_matrix,
    value_projection_matrix,
    output_weight,
    feedforward_gain,
    gate_weight,
    up_weight,
    down_weight,
    earlier_rotated_keys,
    earlier_values,
):
    req_count = lax.axis_size("req")
    chips = lax.axis_size("kvy")
    kv_count = chips * CORES
    kv_index = lax.axis_index("kvy") * CORES + lax.axis_index("core")
    req_index = lax.axis_index("req")
    request_list = span_length.shape[0]
    total_rows, width_share = activations.shape
    span_size = total_rows // request_list
    local_kv = key_projection_matrix.shape[1] // HEAD_WIDTH
    local_q = query_weight.shape[1] // HEAD_WIDTH
    query_groups = local_q // local_kv

    past_share = earlier_rotated_keys.shape[1]
    lanes_share = local_kv * HEAD_WIDTH
    stacked = jnp.stack(
        [
            jnp.stack([past[..., j * lanes_share:(j + 1) * lanes_share] for past in (earlier_rotated_keys, earlier_values)])
            for j in range(kv_count)
        ]
    )
    arrived = lax.all_to_all(stacked, ("kvy", "core"), split_axis=0, concat_axis=0, tiled=True)
    head_kv = arrived.transpose(1, 2, 0, 3, 4).reshape(
        2, request_list, kv_count * past_share, lanes_share
    )
    past_size = head_kv.shape[2]

    capacity = max(2, (request_list + req_count - 1) // req_count)
    order_ids = jnp.arange(request_list, dtype=jnp.int32)
    earlier = order_ids[None, :] < order_ids[:, None]
    own_dest = decode_slot // request_list
    same_dest = own_dest[:, None] == own_dest[None, :]
    own_rank = jnp.sum((same_dest & earlier).astype(jnp.int32), axis=1)
    buffer_place = own_dest * capacity + own_rank
    buffer_ids = jnp.arange(req_count * capacity, dtype=jnp.int32)
    matches = buffer_place[None, :] == buffer_ids[:, None]
    picked = jnp.sum(jnp.where(matches, order_ids[None, :], 0), axis=1)
    filled = jnp.any(matches, axis=1)
    lanes = local_kv * HEAD_WIDTH
    slot_code = jnp.stack([decode_slot // 16, decode_slot % 16], axis=1).astype(jnp.bfloat16)
    trailer = jnp.pad(slot_code[:, None, :], ((0, 0), (0, 7), (0, lanes - 2)))
    payload = jnp.concatenate([head_kv[0], head_kv[1], trailer], axis=1)
    packed = jnp.take(payload, picked, axis=0)
    packed = jnp.where(filled[:, None, None], packed, -jnp.ones((), packed.dtype))
    packed = packed.reshape((req_count, capacity) + payload.shape[1:])
    landed = lax.all_to_all(packed, "req", split_axis=0, concat_axis=0, tiled=True)
    x_whole = gather_features(activations)
    chip_cols = output_weight.shape[1] // chips
    far_cols = lax.dynamic_slice_in_dim(
        output_weight, (1 - lax.axis_index("kvy")) * chip_cols, chip_cols, 1
    )
    weight_far = swap(far_cols, "kvy")
    x_float = x_whole.astype(jnp.float32)
    square_sum = jnp.sum(x_float * x_float, axis=-1, keepdims=True)
    normalized_input = (
        x_float * lax.rsqrt(square_sum / x_float.shape[-1] + epsilon) * attention_gain
    ).astype(jnp.bfloat16)
    position = (
        offsets[:, None].astype(jnp.float32) + jnp.arange(span_size, dtype=jnp.float32)[None, :]
    )
    query_rows = jnp.dot(
        normalized_input, query_weight, preferred_element_type=jnp.float32
    ).reshape(request_list, span_size, local_q, HEAD_WIDTH)
    query_rows = rotate_pairs(query_rows, position).astype(jnp.bfloat16)
    fresh_keys = jnp.dot(
        normalized_input, key_projection_matrix, preferred_element_type=jnp.float32
    ).reshape(request_list, span_size, local_kv, HEAD_WIDTH)
    fresh_keys = rotate_pairs(fresh_keys, position).astype(jnp.bfloat16)
    fresh_values = (
        jnp.dot(normalized_input, value_projection_matrix, preferred_element_type=jnp.float32)
        .astype(jnp.bfloat16)
        .reshape(request_list, span_size, local_kv, HEAD_WIDTH)
    )
    combined_keys = jnp.concatenate(
        [head_kv[0].reshape(request_list, past_size, local_kv, HEAD_WIDTH), fresh_keys], axis=1
    )
    combined_values = jnp.concatenate(
        [head_kv[1].reshape(request_list, past_size, local_kv, HEAD_WIDTH), fresh_values], axis=1
    )
    grouped_queries = query_rows.reshape(
        request_list, span_size, local_kv, query_groups, HEAD_WIDTH
    )
    scores = jnp.einsum(
        "rckgd,rskd->rkgcs", grouped_queries, combined_keys, preferred_element_type=jnp.float32
    ) / math.sqrt(HEAD_WIDTH)
    allowed = allowed_keys(span_length, span_size, past_size)[:, None, None, :, :]
    scores = jnp.where(allowed, scores, -jnp.inf)
    weights = jax.nn.softmax(scores, axis=-1).astype(jnp.bfloat16)
    mixed_heads = jnp.einsum(
        "rkgcs,rskd->rckgd", weights, combined_values, preferred_element_type=jnp.float32
    )
    mixed_heads = mixed_heads.astype(jnp.bfloat16).reshape(total_rows, local_q * HEAD_WIDTH)
    head_share = project_heads(mixed_heads, output_weight, weight_far)
    residual_share = activations.astype(jnp.float32) + head_share

    gain_share = lax.dynamic_slice_in_dim(feedforward_gain, kv_index * width_share, width_share)
    normed_share = row_scale(residual_share, gain_share).astype(jnp.bfloat16)
    gate_proj, upward = gather_project(normed_share, (gate_weight, up_weight))
    hidden = (jax.nn.silu(gate_proj) * upward).astype(jnp.bfloat16)
    hidden = lax.optimization_barrier(hidden)
    mlp_share = scatter_features(hidden, down_weight, jnp.bfloat16)
    landed, mlp_share = lax.optimization_barrier((landed, mlp_share))
    landed = landed.reshape((req_count * capacity,) + payload.shape[1:])
    code = landed[:, 2 * past_size, :2].astype(jnp.int32)
    landed_slots = code[:, 0] * 16 + code[:, 1]
    wanted = req_index * request_list + order_ids
    slot_hits = landed_slots[None, :] == wanted[:, None]
    entry_ids = jnp.arange(req_count * capacity, dtype=jnp.int32)
    slot_position = jnp.sum(jnp.where(slot_hits, entry_ids[None, :], 0), axis=1)
    decode_rows = jnp.take(landed, slot_position, axis=0)
    decode_kv = (decode_rows[:, :past_size], decode_rows[:, past_size:2 * past_size])

    live_rows = (jnp.arange(span_size, dtype=jnp.int32)[None, :] < span_length[:, None]).reshape(
        total_rows
    )
    layer_out = jnp.where(live_rows[:, None], residual_share + mlp_share, 0.0).astype(jnp.bfloat16)
    return (layer_out, decode_kv[0], decode_kv[1])


def solution(mesh):
    req_size, kv_size = mesh.devices.shape
    split_mesh = Mesh(
        mesh.devices.reshape(req_size, kv_size // CORES, CORES), ("req", "kvy", "core")
    )
    kv = ("kvy", "core")
    return jax.shard_map(
        local,
        mesh=split_mesh,
        in_specs=(
            P("req", kv),
            P("req"),
            P("req"),
            P("req"),
            P(),
            P(None, kv),
            P(None, kv),
            P(None, kv),
            P(kv, None),
            P(),
            P(None, kv),
            P(None, kv),
            P(kv, None),
            P("req", kv, None),
            P("req", kv, None),
        ),
        out_specs=(P("req", kv), P("req", None, kv), P("req", None, kv)),
        check_vma=False,
    )
```

```python
import math

import jax
import jax.numpy as jnp
from jax import lax
from jax.sharding import Mesh
from jax.sharding import PartitionSpec as P

HEAD_WIDTH = 256
CORES = 2


rope_base = 1000042.0
epsilon = 1e-05


def rotate_pairs(tensor, position):
    half_size = tensor.shape[-1] // 2
    steps_float = jnp.arange(half_size, dtype=jnp.float32)
    inverse = jnp.exp(steps_float * (-2.0 * math.log(rope_base) / tensor.shape[-1]))
    angles = position[:, :, None] * inverse[None, None, :]
    cosine = jnp.cos(angles)[:, :, None, :]
    sine_part = jnp.sin(angles)[:, :, None, :]
    first_half = tensor[..., :half_size]
    second = tensor[..., half_size:]
    return jnp.concatenate(
        [first_half * cosine - second * sine_part, second * cosine + first_half * sine_part],
        axis=-1,
    )


def allowed_keys(span_length, span_size, past_size):
    key_pos = jnp.arange(past_size + span_size, dtype=jnp.int32) - past_size
    query_pos = jnp.arange(span_size, dtype=jnp.int32)
    causal = key_pos[None, :] <= query_pos[:, None]
    live_keys = key_pos[None, None, :] < span_length[:, None, None]
    return (key_pos[None, None, :] < 0) | causal[None, :, :] & live_keys


def swap(values, axis_name):
    return lax.ppermute(values, axis_name, [(0, 1), (1, 0)])


def gather_features(share):
    chip = lax.axis_index("kvy")
    core = lax.axis_index("core")
    partner = swap(share, "kvy")
    pair = jnp.where(chip == 0, jnp.stack([share, partner]), jnp.stack([partner, share]))
    other = swap(pair, "core")
    blocks = []
    for chip_block in range(2):
        for core_block in range(2):
            blocks.append(jnp.where(core == core_block, pair[chip_block], other[chip_block]))
    return jnp.concatenate(blocks, axis=1)


def gather_project(share, weights):
    chip = lax.axis_index("kvy")
    core = lax.axis_index("core")
    from_core = swap(share, "core")
    from_chip = swap(share, "kvy")
    local_pair = jnp.where(
        core == 0,
        jnp.concatenate([share, from_core], axis=1),
        jnp.concatenate([from_core, share], axis=1),
    )
    half = local_pair.shape[1]
    local_parts = tuple(
        jnp.dot(
            local_pair,
            lax.dynamic_slice_in_dim(weight, chip * half, half, 0),
            preferred_element_type=jnp.float32,
        )
        for weight in weights
    )
    from_chip, local_parts = lax.optimization_barrier((from_chip, local_parts))
    from_diagonal = swap(from_chip, "core")
    remote_pair = jnp.where(
        core == 0,
        jnp.concatenate([from_chip, from_diagonal], axis=1),
        jnp.concatenate([from_diagonal, from_chip], axis=1),
    )
    return [
        part
        + jnp.dot(
            remote_pair,
            lax.dynamic_slice_in_dim(weight, (1 - chip) * half, half, 0),
            preferred_element_type=jnp.float32,
        )
        for part, weight in zip(local_parts, weights)
    ]


def scatter_features(matrix_in, weight, link_type=None):
    chip = lax.axis_index("kvy")
    core = lax.axis_index("core")
    product = jnp.dot(matrix_in, weight, preferred_element_type=jnp.float32)
    width = product.shape[1] // (2 * CORES)

    def block(chip_block, core_block):
        start = (chip_block * CORES + core_block) * width
        return product[:, start:start + width]

    keep = jnp.stack([jnp.where(core == 0, block(k, 0), block(k, 1)) for k in range(2)])
    give = jnp.stack([jnp.where(core == 0, block(k, 1), block(k, 0)) for k in range(2)])
    chip_sum = keep + swap(give, "core")
    mine = jnp.where(chip == 0, chip_sum[0], chip_sum[1])
    theirs = jnp.where(chip == 0, chip_sum[1], chip_sum[0])
    if link_type is not None:
        theirs = theirs.astype(link_type)
    return mine + swap(theirs, "kvy").astype(jnp.float32)


def project_heads(mixed, weight, weight_far):
    chip = lax.axis_index("kvy")
    core = lax.axis_index("core")
    half = weight_far.shape[1]
    width = half // CORES
    mixed_far = swap(mixed, "kvy")
    weight_near = lax.dynamic_slice_in_dim(weight, chip * half, half, 1)
    chip_sum = jnp.dot(mixed, weight_near, preferred_element_type=jnp.float32) + jnp.dot(
        mixed_far, weight_far, preferred_element_type=jnp.float32
    )
    keep = lax.dynamic_slice_in_dim(chip_sum, core * width, width, 1)
    give = lax.dynamic_slice_in_dim(chip_sum, (1 - core) * width, width, 1)
    return keep + swap(give, "core")


def row_scale(values, gain_share):
    square_sum = jnp.sum(values * values, axis=-1, keepdims=True)
    diagonal = [(source, 2 * CORES - 1 - source) for source in range(2 * CORES)]
    square_sum = (
        square_sum
        + swap(square_sum, "core")
        + swap(square_sum, "kvy")
        + lax.ppermute(square_sum, ("kvy", "core"), diagonal)
    )
    width = values.shape[-1] * 2 * CORES
    return values * lax.rsqrt(square_sum / width + epsilon) * gain_share


def local(
    activations,
    span_length,
    offsets,
    decode_slot,
    attention_gain,
    query_weight,
    key_projection_matrix,
    value_projection_matrix,
    output_weight,
    feedforward_gain,
    gate_weight,
    up_weight,
    down_weight,
    earlier_rotated_keys,
    earlier_values,
):
    req_count = lax.axis_size("req")
    chips = lax.axis_size("kvy")
    kv_count = chips * CORES
    kv_index = lax.axis_index("kvy") * CORES + lax.axis_index("core")
    req_index = lax.axis_index("req")
    request_list = span_length.shape[0]
    total_rows, width_share = activations.shape
    span_size = total_rows // request_list
    local_kv = key_projection_matrix.shape[1] // HEAD_WIDTH
    local_q = query_weight.shape[1] // HEAD_WIDTH
    query_groups = local_q // local_kv

    past_share = earlier_rotated_keys.shape[1]
    stacked = jnp.stack([earlier_rotated_keys, earlier_values])
    stacked = stacked.reshape(2, request_list, past_share, kv_count, local_kv * HEAD_WIDTH)
    stacked = stacked.transpose(0, 3, 1, 2, 4)
    arrived = lax.all_to_all(stacked, ("kvy", "core"), split_axis=1, concat_axis=1, tiled=True)
    head_kv = arrived.transpose(0, 2, 1, 3, 4).reshape(
        2, request_list, kv_count * past_share, local_kv * HEAD_WIDTH
    )
    past_size = head_kv.shape[2]

    capacity = max(2, (request_list + req_count - 1) // req_count)
    order_ids = jnp.arange(request_list, dtype=jnp.int32)
    earlier = order_ids[None, :] < order_ids[:, None]
    own_dest = decode_slot // request_list
    same_dest = own_dest[:, None] == own_dest[None, :]
    own_rank = jnp.sum((same_dest & earlier).astype(jnp.int32), axis=1)
    buffer_place = own_dest * capacity + own_rank
    buffer_ids = jnp.arange(req_count * capacity, dtype=jnp.int32)
    matches = buffer_place[None, :] == buffer_ids[:, None]
    picked = jnp.sum(jnp.where(matches, order_ids[None, :], 0), axis=1)
    filled = jnp.any(matches, axis=1)
    lanes = local_kv * HEAD_WIDTH
    slot_code = jnp.stack([decode_slot // 16, decode_slot % 16], axis=1).astype(jnp.bfloat16)
    trailer = jnp.pad(slot_code[:, None, :], ((0, 0), (0, 7), (0, lanes - 2)))
    payload = jnp.concatenate([head_kv[0], head_kv[1], trailer], axis=1)
    packed = jnp.take(payload, picked, axis=0)
    packed = jnp.where(filled[:, None, None], packed, -jnp.ones((), packed.dtype))
    packed = packed.reshape((req_count, capacity) + payload.shape[1:])
    landed = lax.all_to_all(packed, "req", split_axis=0, concat_axis=0, tiled=True)
    x_whole = gather_features(activations)
    chip_cols = output_weight.shape[1] // chips
    far_cols = lax.dynamic_slice_in_dim(
        output_weight, (1 - lax.axis_index("kvy")) * chip_cols, chip_cols, 1
    )
    weight_far = swap(far_cols, "kvy")
    x_float = x_whole.astype(jnp.float32)
    square_sum = jnp.sum(x_float * x_float, axis=-1, keepdims=True)
    normalized_input = (
        x_float * lax.rsqrt(square_sum / x_float.shape[-1] + epsilon) * attention_gain
    ).astype(jnp.bfloat16)
    position = (
        offsets[:, None].astype(jnp.float32) + jnp.arange(span_size, dtype=jnp.float32)[None, :]
    )
    query_rows = jnp.dot(
        normalized_input, query_weight, preferred_element_type=jnp.float32
    ).reshape(request_list, span_size, local_q, HEAD_WIDTH)
    query_rows = rotate_pairs(query_rows, position).astype(jnp.bfloat16)
    fresh_keys = jnp.dot(
        normalized_input, key_projection_matrix, preferred_element_type=jnp.float32
    ).reshape(request_list, span_size, local_kv, HEAD_WIDTH)
    fresh_keys = rotate_pairs(fresh_keys, position).astype(jnp.bfloat16)
    fresh_values = (
        jnp.dot(normalized_input, value_projection_matrix, preferred_element_type=jnp.float32)
        .astype(jnp.bfloat16)
        .reshape(request_list, span_size, local_kv, HEAD_WIDTH)
    )
    combined_keys = jnp.concatenate(
        [head_kv[0].reshape(request_list, past_size, local_kv, HEAD_WIDTH), fresh_keys], axis=1
    )
    combined_values = jnp.concatenate(
        [head_kv[1].reshape(request_list, past_size, local_kv, HEAD_WIDTH), fresh_values], axis=1
    )
    grouped_queries = query_rows.reshape(
        request_list, span_size, local_kv, query_groups, HEAD_WIDTH
    )
    scores = jnp.einsum(
        "rckgd,rskd->rkgcs", grouped_queries, combined_keys, preferred_element_type=jnp.float32
    ) / math.sqrt(HEAD_WIDTH)
    allowed = allowed_keys(span_length, span_size, past_size)[:, None, None, :, :]
    scores = jnp.where(allowed, scores, -jnp.inf)
    weights = jax.nn.softmax(scores, axis=-1).astype(jnp.bfloat16)
    mixed_heads = jnp.einsum(
        "rkgcs,rskd->rckgd", weights, combined_values, preferred_element_type=jnp.float32
    )
    mixed_heads = mixed_heads.astype(jnp.bfloat16).reshape(total_rows, local_q * HEAD_WIDTH)
    head_share = project_heads(mixed_heads, output_weight, weight_far)
    residual_share = activations.astype(jnp.float32) + head_share

    gain_share = lax.dynamic_slice_in_dim(feedforward_gain, kv_index * width_share, width_share)
    normed_share = row_scale(residual_share, gain_share).astype(jnp.bfloat16)
    gate_proj, upward = gather_project(normed_share, (gate_weight, up_weight))
    hidden = (jax.nn.silu(gate_proj) * upward).astype(jnp.bfloat16)
    hidden = lax.optimization_barrier(hidden)
    mlp_share = scatter_features(hidden, down_weight, jnp.bfloat16)
    landed, mlp_share = lax.optimization_barrier((landed, mlp_share))
    landed = landed.reshape((req_count * capacity,) + payload.shape[1:])
    code = landed[:, 2 * past_size, :2].astype(jnp.int32)
    landed_slots = code[:, 0] * 16 + code[:, 1]
    wanted = req_index * request_list + order_ids
    slot_hits = landed_slots[None, :] == wanted[:, None]
    entry_ids = jnp.arange(req_count * capacity, dtype=jnp.int32)
    slot_position = jnp.sum(jnp.where(slot_hits, entry_ids[None, :], 0), axis=1)
    decode_rows = jnp.take(landed, slot_position, axis=0)
    decode_kv = (decode_rows[:, :past_size], decode_rows[:, past_size:2 * past_size])

    live_rows = (jnp.arange(span_size, dtype=jnp.int32)[None, :] < span_length[:, None]).reshape(
        total_rows
    )
    layer_out = jnp.where(live_rows[:, None], residual_share + mlp_share, 0.0).astype(jnp.bfloat16)
    return (layer_out, decode_kv[0], decode_kv[1])


def solution(mesh):
    req_size, kv_size = mesh.devices.shape
    split_mesh = Mesh(
        mesh.devices.reshape(req_size, kv_size // CORES, CORES), ("req", "kvy", "core")
    )
    kv = ("kvy", "core")
    return jax.shard_map(
        local,
        mesh=split_mesh,
        in_specs=(
            P("req", kv),
            P("req"),
            P("req"),
            P("req"),
            P(),
            P(None, kv),
            P(None, kv),
            P(None, kv),
            P(kv, None),
            P(),
            P(None, kv),
            P(None, kv),
            P(kv, None),
            P("req", kv, None),
            P("req", kv, None),
        ),
        out_specs=(P("req", kv), P("req", None, kv), P("req", None, kv)),
        check_vma=False,
    )
```

```python
import math

import jax
import jax.numpy as jnp
from jax import lax
from jax.sharding import Mesh
from jax.sharding import PartitionSpec as P

HEAD_WIDTH = 256
CORES = 2


rope_base = 1000042.0
epsilon = 1e-05


def rotate_pairs(tensor, position):
    half_size = tensor.shape[-1] // 2
    steps_float = jnp.arange(half_size, dtype=jnp.float32)
    inverse = jnp.exp(steps_float * (-2.0 * math.log(rope_base) / tensor.shape[-1]))
    angles = position[:, :, None] * inverse[None, None, :]
    cosine = jnp.cos(angles)[:, :, None, :]
    sine_part = jnp.sin(angles)[:, :, None, :]
    first_half = tensor[..., :half_size]
    second = tensor[..., half_size:]
    return jnp.concatenate(
        [first_half * cosine - second * sine_part, second * cosine + first_half * sine_part],
        axis=-1,
    )


def allowed_keys(span_length, span_size, past_size):
    key_pos = jnp.arange(past_size + span_size, dtype=jnp.int32) - past_size
    query_pos = jnp.arange(span_size, dtype=jnp.int32)
    causal = key_pos[None, :] <= query_pos[:, None]
    live_keys = key_pos[None, None, :] < span_length[:, None, None]
    return (key_pos[None, None, :] < 0) | causal[None, :, :] & live_keys


def swap(values, axis_name):
    return lax.ppermute(values, axis_name, [(0, 1), (1, 0)])


def gather_features(share):
    chip = lax.axis_index("kvy")
    core = lax.axis_index("core")
    partner = swap(share, "kvy")
    pair = jnp.where(chip == 0, jnp.stack([share, partner]), jnp.stack([partner, share]))
    other = swap(pair, "core")
    blocks = []
    for chip_block in range(2):
        for core_block in range(2):
            blocks.append(jnp.where(core == core_block, pair[chip_block], other[chip_block]))
    return jnp.concatenate(blocks, axis=1)


def gather_project(share, weights):
    chip = lax.axis_index("kvy")
    core = lax.axis_index("core")
    from_core = swap(share, "core")
    from_chip = swap(share, "kvy")
    local_pair = jnp.where(
        core == 0,
        jnp.concatenate([share, from_core], axis=1),
        jnp.concatenate([from_core, share], axis=1),
    )
    half = local_pair.shape[1]
    local_parts = tuple(
        jnp.dot(
            local_pair,
            lax.dynamic_slice_in_dim(weight, chip * half, half, 0),
            preferred_element_type=jnp.float32,
        )
        for weight in weights
    )
    from_chip, local_parts = lax.optimization_barrier((from_chip, local_parts))
    from_diagonal = swap(from_chip, "core")
    remote_pair = jnp.where(
        core == 0,
        jnp.concatenate([from_chip, from_diagonal], axis=1),
        jnp.concatenate([from_diagonal, from_chip], axis=1),
    )
    return [
        part
        + jnp.dot(
            remote_pair,
            lax.dynamic_slice_in_dim(weight, (1 - chip) * half, half, 0),
            preferred_element_type=jnp.float32,
        )
        for part, weight in zip(local_parts, weights)
    ]


def scatter_features(matrix_in, weight, link_type=None):
    chip = lax.axis_index("kvy")
    core = lax.axis_index("core")
    product = jnp.dot(matrix_in, weight, preferred_element_type=jnp.float32)
    width = product.shape[1] // (2 * CORES)

    def pick(chip_block, core_block):
        start = (chip_block * CORES + core_block) * width
        return lax.dynamic_slice_in_dim(product, start, width, 1)

    keep = jnp.stack([pick(k, core) for k in range(2)])
    give = jnp.stack([pick(k, 1 - core) for k in range(2)])
    chip_sum = keep + swap(give, "core")
    mine = jnp.where(chip == 0, chip_sum[0], chip_sum[1])
    theirs = jnp.where(chip == 0, chip_sum[1], chip_sum[0])
    if link_type is not None:
        theirs = theirs.astype(link_type)
    return mine + swap(theirs, "kvy").astype(jnp.float32)


def project_heads(mixed, weight, weight_far):
    chip = lax.axis_index("kvy")
    core = lax.axis_index("core")
    half = weight_far.shape[1]
    width = half // CORES
    mixed_far = swap(mixed, "kvy")
    weight_near = lax.dynamic_slice_in_dim(weight, chip * half, half, 1)
    chip_sum = jnp.dot(mixed, weight_near, preferred_element_type=jnp.float32) + jnp.dot(
        mixed_far, weight_far, preferred_element_type=jnp.float32
    )
    keep = lax.dynamic_slice_in_dim(chip_sum, core * width, width, 1)
    give = lax.dynamic_slice_in_dim(chip_sum, (1 - core) * width, width, 1)
    return keep + swap(give, "core")


def row_scale(values, gain_share):
    square_sum = jnp.sum(values * values, axis=-1, keepdims=True)
    diagonal = [(source, 2 * CORES - 1 - source) for source in range(2 * CORES)]
    square_sum = (
        square_sum
        + swap(square_sum, "core")
        + swap(square_sum, "kvy")
        + lax.ppermute(square_sum, ("kvy", "core"), diagonal)
    )
    width = values.shape[-1] * 2 * CORES
    return values * lax.rsqrt(square_sum / width + epsilon) * gain_share


def local(
    activations,
    span_length,
    offsets,
    decode_slot,
    attention_gain,
    query_weight,
    key_projection_matrix,
    value_projection_matrix,
    output_weight,
    feedforward_gain,
    gate_weight,
    up_weight,
    down_weight,
    earlier_rotated_keys,
    earlier_values,
):
    req_count = lax.axis_size("req")
    chips = lax.axis_size("kvy")
    kv_count = chips * CORES
    kv_index = lax.axis_index("kvy") * CORES + lax.axis_index("core")
    req_index = lax.axis_index("req")
    request_list = span_length.shape[0]
    total_rows, width_share = activations.shape
    span_size = total_rows // request_list
    local_kv = key_projection_matrix.shape[1] // HEAD_WIDTH
    local_q = query_weight.shape[1] // HEAD_WIDTH
    query_groups = local_q // local_kv

    past_share = earlier_rotated_keys.shape[1]
    stacked = jnp.stack([earlier_rotated_keys, earlier_values])
    stacked = stacked.reshape(2, request_list, past_share, kv_count, local_kv * HEAD_WIDTH)
    stacked = stacked.transpose(0, 3, 1, 2, 4)
    arrived = lax.all_to_all(stacked, ("kvy", "core"), split_axis=1, concat_axis=1, tiled=True)
    head_kv = arrived.transpose(0, 2, 1, 3, 4).reshape(
        2, request_list, kv_count * past_share, local_kv * HEAD_WIDTH
    )
    past_size = head_kv.shape[2]

    capacity = max(2, (request_list + req_count - 1) // req_count)
    order_ids = jnp.arange(request_list, dtype=jnp.int32)
    earlier = order_ids[None, :] < order_ids[:, None]
    own_dest = decode_slot // request_list
    same_dest = own_dest[:, None] == own_dest[None, :]
    own_rank = jnp.sum((same_dest & earlier).astype(jnp.int32), axis=1)
    buffer_place = own_dest * capacity + own_rank
    buffer_ids = jnp.arange(req_count * capacity, dtype=jnp.int32)
    matches = buffer_place[None, :] == buffer_ids[:, None]
    picked = jnp.sum(jnp.where(matches, order_ids[None, :], 0), axis=1)
    filled = jnp.any(matches, axis=1)
    lanes = local_kv * HEAD_WIDTH
    slot_code = jnp.stack([decode_slot // 16, decode_slot % 16], axis=1).astype(jnp.bfloat16)
    trailer = jnp.pad(slot_code[:, None, :], ((0, 0), (0, 7), (0, lanes - 2)))
    payload = jnp.concatenate([head_kv[0], head_kv[1], trailer], axis=1)
    packed = jnp.take(payload, picked, axis=0)
    packed = jnp.where(filled[:, None, None], packed, -jnp.ones((), packed.dtype))
    packed = packed.reshape((req_count, capacity) + payload.shape[1:])
    landed = lax.all_to_all(packed, "req", split_axis=0, concat_axis=0, tiled=True)
    x_whole = gather_features(activations)
    chip_cols = output_weight.shape[1] // chips
    far_cols = lax.dynamic_slice_in_dim(
        output_weight, (1 - lax.axis_index("kvy")) * chip_cols, chip_cols, 1
    )
    weight_far = swap(far_cols, "kvy")
    x_float = x_whole.astype(jnp.float32)
    square_sum = jnp.sum(x_float * x_float, axis=-1, keepdims=True)
    normalized_input = (
        x_float * lax.rsqrt(square_sum / x_float.shape[-1] + epsilon) * attention_gain
    ).astype(jnp.bfloat16)
    position = (
        offsets[:, None].astype(jnp.float32) + jnp.arange(span_size, dtype=jnp.float32)[None, :]
    )
    query_rows = jnp.dot(
        normalized_input, query_weight, preferred_element_type=jnp.float32
    ).reshape(request_list, span_size, local_q, HEAD_WIDTH)
    query_rows = rotate_pairs(query_rows, position).astype(jnp.bfloat16)
    fresh_keys = jnp.dot(
        normalized_input, key_projection_matrix, preferred_element_type=jnp.float32
    ).reshape(request_list, span_size, local_kv, HEAD_WIDTH)
    fresh_keys = rotate_pairs(fresh_keys, position).astype(jnp.bfloat16)
    fresh_values = (
        jnp.dot(normalized_input, value_projection_matrix, preferred_element_type=jnp.float32)
        .astype(jnp.bfloat16)
        .reshape(request_list, span_size, local_kv, HEAD_WIDTH)
    )
    combined_keys = jnp.concatenate(
        [head_kv[0].reshape(request_list, past_size, local_kv, HEAD_WIDTH), fresh_keys], axis=1
    )
    combined_values = jnp.concatenate(
        [head_kv[1].reshape(request_list, past_size, local_kv, HEAD_WIDTH), fresh_values], axis=1
    )
    grouped_queries = query_rows.reshape(
        request_list, span_size, local_kv, query_groups, HEAD_WIDTH
    )
    scores = jnp.einsum(
        "rckgd,rskd->rkgcs", grouped_queries, combined_keys, preferred_element_type=jnp.float32
    ) / math.sqrt(HEAD_WIDTH)
    allowed = allowed_keys(span_length, span_size, past_size)[:, None, None, :, :]
    scores = jnp.where(allowed, scores, -jnp.inf)
    weights = jax.nn.softmax(scores, axis=-1).astype(jnp.bfloat16)
    mixed_heads = jnp.einsum(
        "rkgcs,rskd->rckgd", weights, combined_values, preferred_element_type=jnp.float32
    )
    mixed_heads = mixed_heads.astype(jnp.bfloat16).reshape(total_rows, local_q * HEAD_WIDTH)
    head_share = project_heads(mixed_heads, output_weight, weight_far)
    residual_share = activations.astype(jnp.float32) + head_share

    gain_share = lax.dynamic_slice_in_dim(feedforward_gain, kv_index * width_share, width_share)
    normed_share = row_scale(residual_share, gain_share).astype(jnp.bfloat16)
    gate_proj, upward = gather_project(normed_share, (gate_weight, up_weight))
    hidden = (jax.nn.silu(gate_proj) * upward).astype(jnp.bfloat16)
    hidden = lax.optimization_barrier(hidden)
    mlp_share = scatter_features(hidden, down_weight, jnp.bfloat16)
    landed, mlp_share = lax.optimization_barrier((landed, mlp_share))
    landed = landed.reshape((req_count * capacity,) + payload.shape[1:])
    code = landed[:, 2 * past_size, :2].astype(jnp.int32)
    landed_slots = code[:, 0] * 16 + code[:, 1]
    wanted = req_index * request_list + order_ids
    slot_hits = landed_slots[None, :] == wanted[:, None]
    entry_ids = jnp.arange(req_count * capacity, dtype=jnp.int32)
    slot_position = jnp.sum(jnp.where(slot_hits, entry_ids[None, :], 0), axis=1)
    decode_rows = jnp.take(landed, slot_position, axis=0)
    decode_kv = (decode_rows[:, :past_size], decode_rows[:, past_size:2 * past_size])

    live_rows = (jnp.arange(span_size, dtype=jnp.int32)[None, :] < span_length[:, None]).reshape(
        total_rows
    )
    layer_out = jnp.where(live_rows[:, None], residual_share + mlp_share, 0.0).astype(jnp.bfloat16)
    return (layer_out, decode_kv[0], decode_kv[1])


def solution(mesh):
    req_size, kv_size = mesh.devices.shape
    split_mesh = Mesh(
        mesh.devices.reshape(req_size, kv_size // CORES, CORES), ("req", "kvy", "core")
    )
    kv = ("kvy", "core")
    return jax.shard_map(
        local,
        mesh=split_mesh,
        in_specs=(
            P("req", kv),
            P("req"),
            P("req"),
            P("req"),
            P(),
            P(None, kv),
            P(None, kv),
            P(None, kv),
            P(kv, None),
            P(),
            P(None, kv),
            P(None, kv),
            P(kv, None),
            P("req", kv, None),
            P("req", kv, None),
        ),
        out_specs=(P("req", kv), P("req", None, kv), P("req", None, kv)),
        check_vma=False,
    )
```
